32 devices in a mesh: groups: 2 (over y), ctx: 4 (over z), dp: 2 (over x), sub: 2 (over core).
Axes of the slice: x: 2, y: 2, z: 4, core: 2. Of those that a mesh axis runs over, the one named last changes fastest.
Arguments:
- hidden: bfloat16 [8, 768, 2304], P(('groups', 'dp', 'sub'), 'ctx'), parts along dimension 0, may hold values from -16 to 16
- queries: bfloat16 [8, 768, 2048], P(('groups', 'dp', 'sub'), 'ctx'), parts along dimension 0, may hold values from -16 to 16
- kv_weight: bfloat16 [2, 2304, 1024], P(None, 'ctx', ('dp', 'sub')), may hold values from -0.125 to 0.125
- adapter_down: bfloat16 [2, 16, 2304], P(None, None, ('ctx', 'dp', 'sub')), may hold values from -0.125 to 0.125
- adapter_up: bfloat16 [2, 16, 1024], P(None, None, ('ctx', 'dp', 'sub')), may hold values from -1.5 to 1.5
- out_grad: bfloat16 [8, 768, 2048], P(('groups', 'dp', 'sub'), 'ctx'), parts along dimension 0, may hold values from -6 to 6
Outputs:
- attended: bfloat16 [8, 768, 2048], P(('groups', 'dp', 'sub'), 'ctx'), parts along dimension 0
- query_grad: bfloat16 [8, 768, 2048], P(('groups', 'dp', 'sub'), 'ctx'), parts along dimension 0
- down_grad: float32 [4, 16, 2304], P('groups', None, ('ctx', 'dp', 'sub')), parts along dimension 0
- up_grad: float32 [4, 16, 1024], P('groups', None, ('ctx', 'dp', 'sub')), parts along dimension 0
The draws below stay inside these ranges and needn't reach their ends.
There are 2 independent parts, one for each index of `groups`. The reference program is written for one: setup_inputs(seed, part) draws one part's arguments, and reference() takes and returns one part's arrays. A program takes and returns all parts, laid end to end along the dimension named above; an argument that names none is the same for every part. Nothing has to cross between parts.
All inputs are finite; a program needn't handle non-finite values.
Results may differ from the reference program's by a relative error of at most 0.015.
The reference program's roundings to bfloat16 on the way count: a program that leaves them out, or rounds other values in their place, can miss the bound.
Values may be sent and summed in bfloat16 or wider, within the bound.
No kernel may reach another device: no remote copies, remote signals or barrier semaphores. Data moves between devices by JAX's collectives and lax.ppermute only.
A program may use at most 64 MiB of HBM per device.

```python
import math
import jax
import jax.numpy as jnp
from jax import lax

D = 2304
HEADS = 16
KV_HEADS = 8
HEAD_DIM = 128
RANK = 16
TOK_DEV = 192
SEQ_LEN = 768
SEQS = 4
KV_WIDTH = 1024
Q_WIDTH = 2048


def scaled_rows(key, shape):
    first_key, second_key = jax.random.split(key)
    values = jax.random.truncated_normal(first_key, -4.0, 4.0, shape, jnp.float32)
    low_end = math.log(0.4)
    high_end = math.log(4.0)
    factors = jnp.exp(jax.random.uniform(second_key, shape[:-1] + (1,), jnp.float32, low_end, high_end))
    return values * factors


def draw_hidden(key, part):
    return scaled_rows(jax.random.fold_in(key, 11), (SEQS, SEQ_LEN, D)).astype(jnp.bfloat16)


def draw_queries(key, part):
    return scaled_rows(jax.random.fold_in(key, 23), (SEQS, SEQ_LEN, Q_WIDTH)).astype(jnp.bfloat16)


def level_of(own_key, dims, cuts, least, top_value):
    loudness = 1.0
    for position, parts in cuts:
        draws = jax.random.uniform(jax.random.fold_in(jax.random.fold_in(own_key, 6), position), (parts,), jnp.float32, least / len(cuts), top_value / len(cuts))
        loudness = loudness * jnp.repeat(jnp.exp(draws), dims[position] // parts).reshape((-1,) + (1,) * (len(dims) - 1 - position))
    return loudness


def noise(stream_key, extent, spread, most, cuts=(), held_as=jnp.bfloat16):
    array = jax.random.normal(stream_key, extent, jnp.float32) * spread
    if len(cuts) > 0:
        array = level_of(stream_key, extent, cuts, -0.22, 0.18) * array
    return jnp.clip(array, min=-most, max=most).astype(held_as)


def setup_inputs(seed: int = 0, part: int = 0) -> dict:
    arg_keys = jax.random.split(jax.random.key(seed), 7)
    part_splits = jax.random.split(jax.random.fold_in(arg_keys[6], part), 7)
    hidden = draw_hidden(jax.random.fold_in(jax.random.fold_in(arg_keys[6], part), 71), part)
    queries = draw_queries(jax.random.fold_in(jax.random.fold_in(arg_keys[6], part), 71), part)
    kv_weight = noise(arg_keys[2], (2, D, KV_WIDTH), D ** -0.5, 0.125, ((1, 4), (2, 4)))
    adapter_down = noise(arg_keys[3], (2, RANK, D), D ** -0.5, 0.125, ((2, 16),))
    adapter_up = noise(arg_keys[4], (2, RANK, KV_WIDTH), RANK ** -0.5, 1.5, ((2, 16),))
    out_grad = noise(part_splits[5], (SEQS, SEQ_LEN, Q_WIDTH), 1.0, 6.0, ((0, 4), (1, 4)))
    return dict(hidden=hidden, queries=queries, kv_weight=kv_weight, adapter_down=adapter_down, adapter_up=adapter_up, out_grad=out_grad)


query_scale = 1.0 / 12.0
logit_cap = 50.0
adapter_scale = 0.5


def settle(values):
    return lax.optimization_barrier(values.astype(jnp.bfloat16)).astype(jnp.float32)


def attend_block(query_rows, key_rows, value_rows, grad_rows, is_first):
    length = query_rows.shape[0]
    group_size = HEADS // KV_HEADS
    head_query = query_rows.reshape(length, KV_HEADS, group_size, HEAD_DIM).transpose(1, 2, 0, 3).astype(jnp.float32)
    head_grad = grad_rows.reshape(length, KV_HEADS, group_size, HEAD_DIM).transpose(1, 2, 0, 3).astype(jnp.float32)
    head_key = key_rows.reshape(2 * length, KV_HEADS, HEAD_DIM).transpose(1, 0, 2).astype(jnp.float32)
    head_value = value_rows.reshape(2 * length, KV_HEADS, HEAD_DIM).transpose(1, 0, 2).astype(jnp.float32)
    query_pos = lax.broadcasted_iota(jnp.int32, (length, 2 * length), 0)
    key_pos = lax.broadcasted_iota(jnp.int32, (length, 2 * length), 1)
    visible = (key_pos > query_pos) & (key_pos <= query_pos + length) & (jnp.logical_not(is_first) | (key_pos >= length))

    def one_head(operands):
        queries_g, grads_g, keys_g, values_g = operands
        raw_score = jnp.einsum("grd,kd->grk", queries_g, keys_g) * query_scale
        bent_score = jnp.tanh(raw_score / logit_cap)
        expo_terms = jnp.where(visible, jnp.exp(logit_cap * bent_score), 0.0)
        denominator = jnp.sum(expo_terms, axis=-1, keepdims=True)
        attn_prob = settle(expo_terms / denominator)
        head_out = jnp.einsum("grk,kd->grd", attn_prob, values_g)
        prob_grad = jnp.einsum("grd,kd->grk", grads_g, values_g)
        row_delta = jnp.sum(attn_prob * prob_grad, axis=-1, keepdims=True)
        score_grad = settle(attn_prob * (prob_grad - row_delta) * (1.0 - bent_score * bent_score) * query_scale)
        head_qgrad = jnp.einsum("grk,kd->grd", score_grad, keys_g)
        key_part = jnp.einsum("grk,grd->kd", score_grad, queries_g)
        value_part = jnp.einsum("grk,grd->kd", attn_prob, grads_g)
        return head_out, head_qgrad, key_part, value_part

    head_out, head_qgrad, key_part, value_part = lax.map(one_head, (head_query, head_grad, head_key, head_value))
    attended = head_out.transpose(2, 0, 1, 3).reshape(length, HEADS * HEAD_DIM).astype(jnp.bfloat16)
    query_grad = head_qgrad.transpose(2, 0, 1, 3).reshape(length, HEADS * HEAD_DIM).astype(jnp.bfloat16)
    key_grad = key_part.transpose(1, 0, 2).reshape(2 * length, KV_HEADS * HEAD_DIM)
    value_grad = value_part.transpose(1, 0, 2).reshape(2 * length, KV_HEADS * HEAD_DIM)
    return attended, query_grad, jnp.stack([key_grad, value_grad])


def to_rows(blocked):
    seq_count, blocks = blocked.shape[0], blocked.shape[1]
    return blocked.transpose(2, 0, 1, 3, 4).reshape(2, seq_count * blocks * TOK_DEV, KV_WIDTH)


def reference(hidden, queries, kv_weight, adapter_down, adapter_up, out_grad):
    seq_count, length, model_width = hidden.shape
    blocks = length // TOK_DEV
    flat_rows = hidden.reshape(seq_count * length, model_width)
    low_rank = jnp.stack([jnp.dot(flat_rows, adapter_down[member].T, preferred_element_type=jnp.float32) for member in range(2)]).astype(jnp.bfloat16)
    key_value = jnp.stack([
        jnp.dot(flat_rows, kv_weight[member], preferred_element_type=jnp.float32)
        + adapter_scale * jnp.dot(low_rank[member], adapter_up[member], preferred_element_type=jnp.float32)
        for member in range(2)]).astype(jnp.bfloat16)
    per_block = key_value.reshape(2, seq_count, blocks, TOK_DEV, KV_WIDTH)
    earlier = jnp.concatenate([jnp.zeros_like(per_block[:, :, :1]), per_block[:, :, :-1]], axis=2)
    joined = jnp.concatenate([earlier, per_block], axis=3).reshape(2, seq_count * blocks, 2 * TOK_DEV, KV_WIDTH)
    query_blocks = queries.reshape(seq_count * blocks, TOK_DEV, HEADS * HEAD_DIM)
    grad_blocks = out_grad.reshape(seq_count * blocks, TOK_DEV, HEADS * HEAD_DIM)
    first_flags = (jnp.arange(seq_count * blocks) % blocks) == 0

    def run_block(operands):
        query_rows, key_rows, value_rows, grad_rows, is_first = operands
        attended, query_grad, kv_grads = attend_block(query_rows, key_rows, value_rows, grad_rows, is_first)
        return attended, query_grad, kv_grads.astype(jnp.bfloat16)

    attended, query_grad, kv_grads = lax.map(run_block, (query_blocks, joined[0], joined[1], grad_blocks, first_flags))
    far_part = kv_grads[:, :, :TOK_DEV].reshape(seq_count, blocks, 2, TOK_DEV, KV_WIDTH)
    near_part = kv_grads[:, :, TOK_DEV:].reshape(seq_count, blocks, 2, TOK_DEV, KV_WIDTH)
    returned = jnp.concatenate([far_part[:, 1:], jnp.zeros_like(far_part[:, :1])], axis=1)
    pieces = (to_rows(near_part), to_rows(returned))
    factor = adapter_scale / seq_count
    down_list = []
    up_list = []
    for member in range(2):
        down_terms = jnp.zeros((RANK, model_width), jnp.float32)
        up_terms = jnp.zeros((RANK, KV_WIDTH), jnp.float32)
        for piece_rows in pieces:
            projected = jnp.dot(piece_rows[member], adapter_up[member].T, preferred_element_type=jnp.float32).astype(jnp.bfloat16)
            down_terms = down_terms + jnp.dot(projected.T, flat_rows, preferred_element_type=jnp.float32)
            up_terms = up_terms + jnp.dot(low_rank[member].T, piece_rows[member], preferred_element_type=jnp.float32)
        down_list.append(down_terms * factor)
        up_list.append(up_terms * factor)
    return (attended.reshape(seq_count, length, HEADS * HEAD_DIM),
            query_grad.reshape(seq_count, length, HEADS * HEAD_DIM),
            jnp.stack(down_list), jnp.stack(up_list))
```

```python
import jax
import jax.numpy as jnp
from jax import lax
from jax.sharding import PartitionSpec as P

HEADS = 16
KV_HEADS = 8
HEAD_DIM = 128


query_scale = 1.0 / 12.0
logit_cap = 50.0
adapter_scale = 0.5


def shifted(value, axis, by):
    length = lax.axis_size(axis)
    pairs = [(i, i + by) for i in range(length) if 0 <= i + by < length]
    return lax.ppermute(value, axis, pairs)


def attend(query_rows, key_rows, value_rows, grad_rows, is_first):
    length = query_rows.shape[0]
    group_size = HEADS // KV_HEADS
    queries_g = query_rows.reshape(length, KV_HEADS, group_size, HEAD_DIM)
    grads_g = grad_rows.reshape(length, KV_HEADS, group_size, HEAD_DIM)
    keys_g = key_rows.reshape(2 * length, KV_HEADS, HEAD_DIM)
    values_g = value_rows.reshape(2 * length, KV_HEADS, HEAD_DIM)
    query_pos = lax.broadcasted_iota(jnp.int32, (length, 2 * length), 0)
    key_pos = lax.broadcasted_iota(jnp.int32, (length, 2 * length), 1)
    visible = (
        (key_pos > query_pos)
        & (key_pos <= query_pos + length)
        & (jnp.logical_not(is_first) | (key_pos >= length))
    )
    raw_score = (
        jnp.einsum("rgjd,kgd->gjrk", queries_g, keys_g, preferred_element_type=jnp.float32)
        * query_scale
    )
    bent_score = jnp.tanh(raw_score / logit_cap)
    expo_terms = jnp.where(visible, jnp.exp(logit_cap * bent_score), 0.0)
    denominator = jnp.sum(expo_terms, axis=-1, keepdims=True)
    attn_prob = (expo_terms / denominator).astype(jnp.bfloat16)
    head_out = jnp.einsum(
        "gjrk,kgd->rgjd", attn_prob, values_g, preferred_element_type=jnp.float32
    )
    prob_grad = jnp.einsum(
        "rgjd,kgd->gjrk", grads_g, values_g, preferred_element_type=jnp.float32
    )
    prob_wide = attn_prob.astype(jnp.float32)
    row_delta = jnp.sum(prob_wide * prob_grad, axis=-1, keepdims=True)
    score_grad = (
        prob_wide * (prob_grad - row_delta) * (1.0 - bent_score * bent_score) * query_scale
    ).astype(jnp.bfloat16)
    head_qgrad = jnp.einsum(
        "gjrk,kgd->rgjd", score_grad, keys_g, preferred_element_type=jnp.float32
    )
    key_part = jnp.einsum(
        "gjrk,rgjd->kgd", score_grad, queries_g, preferred_element_type=jnp.float32
    )
    value_part = jnp.einsum(
        "gjrk,rgjd->kgd", attn_prob, grads_g, preferred_element_type=jnp.float32
    )
    attended = head_out.reshape(length, HEADS * HEAD_DIM).astype(jnp.bfloat16)
    query_grad = head_qgrad.reshape(length, HEADS * HEAD_DIM).astype(jnp.bfloat16)
    key_grad = key_part.reshape(2 * length, KV_HEADS * HEAD_DIM)
    value_grad = value_part.reshape(2 * length, KV_HEADS * HEAD_DIM)
    return (attended, query_grad, jnp.stack([key_grad, value_grad]))


def project_rows(row_block, kv_weight, down_full, up_full):
    low_rank = jnp.einsum(
        "rd,mkd->mrk", row_block, down_full, preferred_element_type=jnp.float32
    ).astype(jnp.bfloat16)
    partial_weight = lax.all_gather(kv_weight, "ctx", axis=1, tiled=True)
    base_part = jnp.einsum(
        "rd,mdc->mrc",
        row_block,
        lax.all_gather(partial_weight, ("dp", "sub"), axis=2, tiled=True),
        preferred_element_type=jnp.float32,
    )
    extra_part = jnp.einsum("mrk,mkc->mrc", low_rank, up_full, preferred_element_type=jnp.float32)
    key_value = (base_part + adapter_scale * extra_part).astype(jnp.bfloat16)
    return (low_rank, key_value)


def gather_adapters(adapter_down, adapter_up):
    axes = ("ctx", "dp", "sub")
    down_cols = adapter_down.shape[2]
    joined = jnp.concatenate([adapter_down, adapter_up], axis=2)
    gathered = lax.all_gather(joined, axes, axis=0, tiled=False)
    shards = gathered.shape[0]

    def unshard(piece):
        return piece.transpose(1, 2, 0, 3).reshape(2, piece.shape[2], shards * piece.shape[3])

    return unshard(gathered[..., :down_cols]), unshard(gathered[..., down_cols:])


def scatter_adapter_grads(down_terms, up_terms):
    axes = ("ctx", "dp", "sub")
    shards = lax.axis_size(axes)
    members, rank = down_terms.shape[0], down_terms.shape[1]

    def shard_major(terms):
        cols = terms.shape[2]
        return terms.transpose(2, 0, 1).reshape(shards, cols // shards, members * rank)

    down_cols = down_terms.shape[2] // shards
    joined = jnp.concatenate([shard_major(down_terms), shard_major(up_terms)], axis=1)
    mine = lax.psum_scatter(
        joined.reshape(-1, members * rank), axes, scatter_dimension=0, tiled=True
    )

    def unshard(piece):
        return piece.reshape(-1, members, rank).transpose(1, 2, 0)

    return unshard(mine[:down_cols]), unshard(mine[down_cols:])


def on_device(hidden, queries, kv_weight, adapter_down, adapter_up, out_grad):
    rows_own = hidden[0]
    query_rows = queries[0]
    grad_rows = out_grad[0]
    length = rows_own.shape[0]
    down_full, up_full = gather_adapters(adapter_down, adapter_up)
    is_first = lax.axis_index("ctx") == 0
    low_rank, key_value = project_rows(rows_own, kv_weight, down_full, up_full)
    previous = shifted(key_value, "ctx", 1)
    key_rows = jnp.concatenate([previous[0], key_value[0]], axis=0)
    value_rows = jnp.concatenate([previous[1], key_value[1]], axis=0)
    attended, query_grad, kv_grads = attend(query_rows, key_rows, value_rows, grad_rows, is_first)
    kv_rounded = kv_grads.astype(jnp.bfloat16)
    far_part = kv_rounded[:, :length]
    near_part = kv_rounded[:, length:]
    returned = shifted(far_part, "ctx", -1)
    sources = (rows_own, rows_own)
    low_parts = (low_rank, low_rank)
    pieces = (near_part, returned)
    down_terms = jnp.zeros(down_full.shape, jnp.float32)
    up_terms = jnp.zeros(up_full.shape, jnp.float32)
    for source, low_piece, piece_rows in zip(sources, low_parts, pieces):
        projected = jnp.einsum(
            "mrc,mkc->mrk", piece_rows, up_full, preferred_element_type=jnp.float32
        ).astype(jnp.bfloat16)
        down_terms = down_terms + jnp.einsum(
            "mrk,rd->mkd", projected, source, preferred_element_type=jnp.float32
        )
        up_terms = up_terms + jnp.einsum(
            "mrk,mrc->mkc", low_piece, piece_rows, preferred_element_type=jnp.float32
        )
    factor = adapter_scale / (lax.axis_size("dp") * lax.axis_size("sub"))
    down_part, up_part = scatter_adapter_grads(down_terms * factor, up_terms * factor)
    return (attended[None], query_grad[None], down_part, up_part)


def solution(mesh):
    placed = (
        P(("groups", "dp", "sub"), "ctx", None),
        P(("groups", "dp", "sub"), "ctx", None),
        P(None, "ctx", ("dp", "sub")),
        P(None, None, ("ctx", "dp", "sub")),
        P(None, None, ("ctx", "dp", "sub")),
        P(("groups", "dp", "sub"), "ctx", None),
    )
    return jax.shard_map(
        on_device,
        mesh=mesh,
        in_specs=placed,
        out_specs=(
            P(("groups", "dp", "sub"), "ctx", None),
            P(("groups", "dp", "sub"), "ctx", None),
            P("groups", None, ("ctx", "dp", "sub")),
            P("groups", None, ("ctx", "dp", "sub")),
        ),
        check_vma=False,
    )
```

```python
import jax
import jax.numpy as jnp
from jax import lax
from jax.sharding import PartitionSpec as P

HEADS = 16
KV_HEADS = 8
HEAD_DIM = 128


query_scale = 1.0 / 12.0
logit_cap = 50.0
adapter_scale = 0.5


def shifted(value, axis, by):
    length = lax.axis_size(axis)
    pairs = [(i, i + by) for i in range(length) if 0 <= i + by < length]
    return lax.ppermute(value, axis, pairs)


def attend(query_rows, key_rows, value_rows, grad_rows, is_first):
    length = query_rows.shape[0]
    group_size = HEADS // KV_HEADS
    queries_g = query_rows.reshape(length, KV_HEADS, group_size, HEAD_DIM)
    grads_g = grad_rows.reshape(length, KV_HEADS, group_size, HEAD_DIM)
    keys_g = key_rows.reshape(2 * length, KV_HEADS, HEAD_DIM)
    values_g = value_rows.reshape(2 * length, KV_HEADS, HEAD_DIM)
    query_pos = lax.broadcasted_iota(jnp.int32, (length, 2 * length), 0)
    key_pos = lax.broadcasted_iota(jnp.int32, (length, 2 * length), 1)
    visible = (
        (key_pos > query_pos)
        & (key_pos <= query_pos + length)
        & (jnp.logical_not(is_first) | (key_pos >= length))
    )
    raw_score = (
        jnp.einsum("rgjd,kgd->gjrk", queries_g, keys_g, preferred_element_type=jnp.float32)
        * query_scale
    )
    bent_score = jnp.tanh(raw_score / logit_cap)
    expo_terms = jnp.where(visible, jnp.exp(logit_cap * bent_score), 0.0)
    denominator = jnp.sum(expo_terms, axis=-1, keepdims=True)
    attn_prob = (expo_terms / denominator).astype(jnp.bfloat16)
    head_out = jnp.einsum(
        "gjrk,kgd->rgjd", attn_prob, values_g, preferred_element_type=jnp.float32
    )
    prob_grad = jnp.einsum(
        "rgjd,kgd->gjrk", grads_g, values_g, preferred_element_type=jnp.float32
    )
    prob_wide = attn_prob.astype(jnp.float32)
    row_delta = jnp.sum(prob_wide * prob_grad, axis=-1, keepdims=True)
    score_grad = (
        prob_wide * (prob_grad - row_delta) * (1.0 - bent_score * bent_score) * query_scale
    ).astype(jnp.bfloat16)
    head_qgrad = jnp.einsum(
        "gjrk,kgd->rgjd", score_grad, keys_g, preferred_element_type=jnp.float32
    )
    key_part = jnp.einsum(
        "gjrk,rgjd->kgd", score_grad, queries_g, preferred_element_type=jnp.float32
    )
    value_part = jnp.einsum(
        "gjrk,rgjd->kgd", attn_prob, grads_g, preferred_element_type=jnp.float32
    )
    attended = head_out.reshape(length, HEADS * HEAD_DIM).astype(jnp.bfloat16)
    query_grad = head_qgrad.reshape(length, HEADS * HEAD_DIM).astype(jnp.bfloat16)
    key_grad = key_part.reshape(2 * length, KV_HEADS * HEAD_DIM)
    value_grad = value_part.reshape(2 * length, KV_HEADS * HEAD_DIM)
    return (attended, query_grad, jnp.stack([key_grad, value_grad]))


def project_rows(row_block, kv_weight, down_full, up_full):
    low_rank = jnp.einsum(
        "rd,mkd->mrk", row_block, down_full, preferred_element_type=jnp.float32
    ).astype(jnp.bfloat16)
    row_shards, col_shards = lax.axis_size("ctx"), lax.axis_size(("dp", "sub"))
    gathered = lax.all_gather(kv_weight, ("ctx", "dp", "sub"), axis=0, tiled=False)
    gathered = gathered.reshape((row_shards, col_shards) + kv_weight.shape)
    base_part = jnp.einsum(
        "rcd,cimdn->mrin",
        row_block.reshape(row_block.shape[0], row_shards, kv_weight.shape[1]),
        gathered,
        preferred_element_type=jnp.float32,
    ).reshape(2, row_block.shape[0], col_shards * kv_weight.shape[2])
    extra_part = jnp.einsum("mrk,mkc->mrc", low_rank, up_full, preferred_element_type=jnp.float32)
    key_value = (base_part + adapter_scale * extra_part).astype(jnp.bfloat16)
    return (low_rank, key_value)


def gather_adapters(adapter_down, adapter_up):
    axes = ("ctx", "dp", "sub")
    down_cols = adapter_down.shape[2]
    joined = jnp.concatenate([adapter_down, adapter_up], axis=2)
    gathered = lax.all_gather(joined, axes, axis=0, tiled=False)
    shards = gathered.shape[0]

    def unshard(piece):
        return piece.transpose(1, 2, 0, 3).reshape(2, piece.shape[2], shards * piece.shape[3])

    return unshard(gathered[..., :down_cols]), unshard(gathered[..., down_cols:])


def scatter_adapter_grads(down_terms, up_terms):
    axes = ("ctx", "dp", "sub")
    shards = lax.axis_size(axes)
    row_shards, col_shards = lax.axis_size("ctx"), lax.axis_size(("dp", "sub"))
    members, rank = down_terms.shape[0], down_terms.shape[1]

    def shard_major(terms):
        cols = terms.shape[2]
        return terms.transpose(2, 0, 1).reshape(shards, cols // shards, members * rank)

    down_cols = down_terms.shape[2] // shards
    joined = jnp.concatenate([shard_major(down_terms), shard_major(up_terms)], axis=1)
    joined = joined.reshape((row_shards, col_shards) + joined.shape[1:]).swapaxes(0, 1)
    partial = lax.psum_scatter(
        joined.reshape(-1, members * rank), ("dp", "sub"), scatter_dimension=0, tiled=True
    )
    mine = lax.psum_scatter(partial, "ctx", scatter_dimension=0, tiled=True)

    def unshard(piece):
        return piece.reshape(-1, members, rank).transpose(1, 2, 0)

    return unshard(mine[:down_cols]), unshard(mine[down_cols:])


def on_device(hidden, queries, kv_weight, adapter_down, adapter_up, out_grad):
    rows_own = hidden[0]
    query_rows = queries[0]
    grad_rows = out_grad[0]
    length = rows_own.shape[0]
    down_full, up_full = gather_adapters(adapter_down, adapter_up)
    is_first = lax.axis_index("ctx") == 0
    low_rank, key_value = project_rows(rows_own, kv_weight, down_full, up_full)
    width = key_value.shape[2]
    previous = shifted(jnp.concatenate([key_value, low_rank], axis=2), "ctx", 1)
    low_previous = previous[:, :, width:]
    key_rows = jnp.concatenate([previous[0, :, :width], key_value[0]], axis=0)
    value_rows = jnp.concatenate([previous[1, :, :width], key_value[1]], axis=0)
    attended, query_grad, kv_grads = attend(query_rows, key_rows, value_rows, grad_rows, is_first)
    kv_rounded = kv_grads.astype(jnp.bfloat16)
    far_part = kv_rounded[:, :length]
    near_part = kv_rounded[:, length:]
    projected_far = jnp.einsum(
        "mrc,mkc->mrk", far_part, up_full, preferred_element_type=jnp.float32
    ).astype(jnp.bfloat16)
    projected_returned = shifted(projected_far, "ctx", -1)
    projected_near = jnp.einsum(
        "mrc,mkc->mrk", near_part, up_full, preferred_element_type=jnp.float32
    ).astype(jnp.bfloat16)
    up_terms = jnp.einsum(
        "mrk,mrc->mkc", low_rank, near_part, preferred_element_type=jnp.float32
    ) + jnp.einsum(
        "mrk,mrc->mkc", low_previous, far_part, preferred_element_type=jnp.float32
    )
    down_terms = jnp.einsum(
        "mrk,rd->mkd", projected_near, rows_own, preferred_element_type=jnp.float32
    ) + jnp.einsum(
        "mrk,rd->mkd", projected_returned, rows_own, preferred_element_type=jnp.float32
    )
    factor = adapter_scale / (lax.axis_size("dp") * lax.axis_size("sub"))
    down_part, up_part = scatter_adapter_grads(down_terms * factor, up_terms * factor)
    return (attended[None], query_grad[None], down_part, up_part)


def solution(mesh):
    placed = (
        P(("groups", "dp", "sub"), "ctx", None),
        P(("groups", "dp", "sub"), "ctx", None),
        P(None, "ctx", ("dp", "sub")),
        P(None, None, ("ctx", "dp", "sub")),
        P(None, None, ("ctx", "dp", "sub")),
        P(("groups", "dp", "sub"), "ctx", None),
    )
    return jax.shard_map(
        on_device,
        mesh=mesh,
        in_specs=placed,
        out_specs=(
            P(("groups", "dp", "sub"), "ctx", None),
            P(("groups", "dp", "sub"), "ctx", None),
            P("groups", None, ("ctx", "dp", "sub")),
            P("groups", None, ("ctx", "dp", "sub")),
        ),
        check_vma=False,
    )
```

```python
import jax
import jax.numpy as jnp
from jax import lax
from jax.sharding import PartitionSpec as P

HEADS = 16
KV_HEADS = 8
HEAD_DIM = 128


query_scale = 1.0 / 12.0
logit_cap = 50.0
adapter_scale = 0.5


def shifted(value, axis, by):
    length = lax.axis_size(axis)
    pairs = [(i, i + by) for i in range(length) if 0 <= i + by < length]
    return lax.ppermute(value, axis, pairs)


def attend(query_rows, key_rows, value_rows, grad_rows, is_first):
    length = query_rows.shape[0]
    group_size = HEADS // KV_HEADS

    def by_head(rows):
        return (
            rows.reshape(length, KV_HEADS, group_size, HEAD_DIM)
            .transpose(1, 2, 0, 3)
            .reshape(KV_HEADS, group_size * length, HEAD_DIM)
        )

    def from_head(parts):
        return (
            parts.reshape(KV_HEADS, group_size, length, HEAD_DIM)
            .transpose(2, 0, 1, 3)
            .reshape(length, HEADS * HEAD_DIM)
            .astype(jnp.bfloat16)
        )

    queries_g = by_head(query_rows)
    grads_g = by_head(grad_rows)
    keys_g = key_rows.reshape(2 * length, KV_HEADS, HEAD_DIM).transpose(1, 0, 2)
    values_g = value_rows.reshape(2 * length, KV_HEADS, HEAD_DIM).transpose(1, 0, 2)
    query_pos = lax.broadcasted_iota(jnp.int32, (group_size * length, 2 * length), 0) % length
    key_pos = lax.broadcasted_iota(jnp.int32, (group_size * length, 2 * length), 1)
    visible = (
        (key_pos > query_pos)
        & (key_pos <= query_pos + length)
        & (jnp.logical_not(is_first) | (key_pos >= length))
    )
    raw_score = (
        jnp.einsum("gqd,gkd->gqk", queries_g, keys_g, preferred_element_type=jnp.float32)
        * query_scale
    )
    bent_score = jnp.tanh(raw_score / logit_cap)
    expo_terms = jnp.where(visible, jnp.exp(logit_cap * bent_score), 0.0)
    denominator = jnp.sum(expo_terms, axis=-1, keepdims=True)
    attn_prob = (expo_terms / denominator).astype(jnp.bfloat16)
    head_out = jnp.einsum("gqk,gkd->gqd", attn_prob, values_g, preferred_element_type=jnp.float32)
    prob_grad = jnp.einsum("gqd,gkd->gqk", grads_g, values_g, preferred_element_type=jnp.float32)
    prob_wide = attn_prob.astype(jnp.float32)
    row_delta = jnp.sum(prob_wide * prob_grad, axis=-1, keepdims=True)
    score_grad = (
        prob_wide * (prob_grad - row_delta) * (1.0 - bent_score * bent_score) * query_scale
    ).astype(jnp.bfloat16)
    head_qgrad = jnp.einsum("gqk,gkd->gqd", score_grad, keys_g, preferred_element_type=jnp.float32)
    key_part = jnp.einsum("gqk,gqd->kgd", score_grad, queries_g, preferred_element_type=jnp.float32)
    value_part = jnp.einsum("gqk,gqd->kgd", attn_prob, grads_g, preferred_element_type=jnp.float32)
    key_grad = key_part.reshape(2 * length, KV_HEADS * HEAD_DIM)
    value_grad = value_part.reshape(2 * length, KV_HEADS * HEAD_DIM)
    return (from_head(head_out), from_head(head_qgrad), jnp.stack([key_grad, value_grad]))


def project_rows(row_block, kv_weight, down_full, up_full):
    low_rank = jnp.einsum(
        "rd,mkd->mrk", row_block, down_full, preferred_element_type=jnp.float32
    ).astype(jnp.bfloat16)
    row_shards, col_shards = lax.axis_size("ctx"), lax.axis_size(("dp", "sub"))
    gathered = lax.all_gather(kv_weight, ("ctx", "dp", "sub"), axis=0, tiled=False)
    gathered = gathered.reshape((row_shards, col_shards) + kv_weight.shape)
    base_part = jnp.einsum(
        "rcd,cimdn->mrin",
        row_block.reshape(row_block.shape[0], row_shards, kv_weight.shape[1]),
        gathered,
        preferred_element_type=jnp.float32,
    ).reshape(2, row_block.shape[0], col_shards * kv_weight.shape[2])
    extra_part = jnp.einsum("mrk,mkc->mrc", low_rank, up_full, preferred_element_type=jnp.float32)
    key_value = (base_part + adapter_scale * extra_part).astype(jnp.bfloat16)
    return (low_rank, key_value)


def gather_adapters(adapter_down, adapter_up):
    axes = ("ctx", "dp", "sub")
    down_cols = adapter_down.shape[2]
    joined = jnp.concatenate([adapter_down, adapter_up], axis=2)
    gathered = lax.all_gather(joined, axes, axis=0, tiled=False)
    shards = gathered.shape[0]

    def unshard(piece):
        return piece.transpose(1, 2, 0, 3).reshape(2, piece.shape[2], shards * piece.shape[3])

    return unshard(gathered[..., :down_cols]), unshard(gathered[..., down_cols:])


def scatter_adapter_grads(down_terms, up_terms):
    axes = ("ctx", "dp", "sub")
    shards = lax.axis_size(axes)
    row_shards, col_shards = lax.axis_size("ctx"), lax.axis_size(("dp", "sub"))
    members, rank = down_terms.shape[0], down_terms.shape[1]

    def shard_major(terms):
        cols = terms.shape[2]
        return terms.transpose(2, 0, 1).reshape(shards, cols // shards, members * rank)

    down_cols = down_terms.shape[2] // shards
    joined = jnp.concatenate([shard_major(down_terms), shard_major(up_terms)], axis=1)
    joined = joined.reshape((row_shards, col_shards) + joined.shape[1:]).swapaxes(0, 1)
    partial = lax.psum_scatter(
        joined.reshape(-1, members * rank), ("dp", "sub"), scatter_dimension=0, tiled=True
    )
    mine = lax.psum_scatter(partial, "ctx", scatter_dimension=0, tiled=True)

    def unshard(piece):
        return piece.reshape(-1, members, rank).transpose(1, 2, 0)

    return unshard(mine[:down_cols]), unshard(mine[down_cols:])


def on_device(hidden, queries, kv_weight, adapter_down, adapter_up, out_grad):
    rows_own = hidden[0]
    query_rows = queries[0]
    grad_rows = out_grad[0]
    length = rows_own.shape[0]
    rows_previous = shifted(rows_own, "ctx", 1)
    down_full, up_full = gather_adapters(adapter_down, adapter_up)
    is_first = lax.axis_index("ctx") == 0
    low_both, kv_both = project_rows(
        jnp.concatenate([rows_previous, rows_own], axis=0), kv_weight, down_full, up_full
    )
    low_previous = low_both[:, :length]
    low_rank = low_both[:, length:]
    key_rows = kv_both[0]
    value_rows = kv_both[1]
    attended, query_grad, kv_grads = attend(query_rows, key_rows, value_rows, grad_rows, is_first)
    kv_rounded = kv_grads.astype(jnp.bfloat16)
    far_part = kv_rounded[:, :length]
    near_part = kv_rounded[:, length:]
    projected_far = jnp.einsum(
        "mrc,mkc->mrk", far_part, up_full, preferred_element_type=jnp.float32
    ).astype(jnp.bfloat16)
    projected_returned = shifted(projected_far, "ctx", -1)
    projected_near = jnp.einsum(
        "mrc,mkc->mrk", near_part, up_full, preferred_element_type=jnp.float32
    ).astype(jnp.bfloat16)
    up_terms = jnp.einsum(
        "mrk,mrc->mkc", low_rank, near_part, preferred_element_type=jnp.float32
    ) + jnp.einsum(
        "mrk,mrc->mkc", low_previous, far_part, preferred_element_type=jnp.float32
    )
    down_terms = jnp.einsum(
        "mrk,rd->mkd", projected_near, rows_own, preferred_element_type=jnp.float32
    ) + jnp.einsum(
        "mrk,rd->mkd", projected_returned, rows_own, preferred_element_type=jnp.float32
    )
    factor = adapter_scale / (lax.axis_size("dp") * lax.axis_size("sub"))
    down_part, up_part = scatter_adapter_grads(down_terms * factor, up_terms * factor)
    return (attended[None], query_grad[None], down_part, up_part)


def solution(mesh):
    placed = (
        P(("groups", "dp", "sub"), "ctx", None),
        P(("groups", "dp", "sub"), "ctx", None),
        P(None, "ctx", ("dp", "sub")),
        P(None, None, ("ctx", "dp", "sub")),
        P(None, None, ("ctx", "dp", "sub")),
        P(("groups", "dp", "sub"), "ctx", None),
    )
    return jax.shard_map(
        on_device,
        mesh=mesh,
        in_specs=placed,
        out_specs=(
            P(("groups", "dp", "sub"), "ctx", None),
            P(("groups", "dp", "sub"), "ctx", None),
            P("groups", None, ("ctx", "dp", "sub")),
            P("groups", None, ("ctx", "dp", "sub")),
        ),
        check_vma=False,
    )
```

```python
import jax
import jax.numpy as jnp
from jax import lax
from jax.experimental import pallas as pl
from jax.experimental.pallas import tpu as pltpu
from jax.sharding import PartitionSpec as P

HEADS = 16
KV_HEADS = 8
HEAD_DIM = 128


query_scale = 1.0 / 12.0
logit_cap = 50.0
adapter_scale = 0.5


def shifted(value, axis, by):
    length = lax.axis_size(axis)
    pairs = [(i, i + by) for i in range(length) if 0 <= i + by < length]
    return lax.ppermute(value, axis, pairs)


def attention_kernel(mask_ref, q_ref, do_ref, k_ref, v_ref, out_ref, dq_ref, dk_ref, dv_ref):
    q = q_ref[0]
    do = do_ref[0]
    k = k_ref[0]
    v = v_ref[0]
    visible = mask_ref[...] != 0
    contract_last = (((1,), (1,)), ((), ()))
    raw_score = lax.dot_general(q, k, contract_last, preferred_element_type=jnp.float32) * query_scale
    bent_score = jnp.tanh(raw_score / logit_cap)
    expo_terms = jnp.where(visible, jnp.exp(logit_cap * bent_score), 0.0)
    denominator = jnp.sum(expo_terms, axis=-1, keepdims=True)
    prob_wide = (expo_terms / denominator).astype(jnp.bfloat16).astype(jnp.float32)
    attn_prob = prob_wide.astype(jnp.bfloat16)
    out_ref[0] = jnp.dot(attn_prob, v, preferred_element_type=jnp.float32).astype(out_ref.dtype)
    prob_grad = lax.dot_general(do, v, contract_last, preferred_element_type=jnp.float32)
    row_delta = jnp.sum(prob_wide * prob_grad, axis=-1, keepdims=True)
    score_wide = prob_wide * (prob_grad - row_delta) * (1.0 - bent_score * bent_score) * query_scale
    score_grad = score_wide.astype(jnp.bfloat16)
    dq_ref[0] = jnp.dot(score_grad, k, preferred_element_type=jnp.float32).astype(dq_ref.dtype)
    score_t = score_grad.astype(jnp.float32).T.astype(jnp.bfloat16)
    prob_t = prob_wide.T.astype(jnp.bfloat16)
    dk_ref[0] = jnp.dot(score_t, q, preferred_element_type=jnp.float32).astype(dk_ref.dtype)
    dv_ref[0] = jnp.dot(prob_t, do, preferred_element_type=jnp.float32).astype(dv_ref.dtype)


def attention_heads(mask, q, do, k, v):
    heads, rows, dim = q.shape
    keys = k.shape[1]
    head_block = lambda n: pl.BlockSpec((1, n, dim), lambda g: (g, 0, 0))
    return pl.pallas_call(
        attention_kernel,
        grid=(heads,),
        in_specs=[
            pl.BlockSpec((rows, keys), lambda g: (0, 0)),
            head_block(rows),
            head_block(rows),
            head_block(keys),
            head_block(keys),
        ],
        out_specs=[head_block(rows), head_block(rows), head_block(keys), head_block(keys)],
        out_shape=[
            jax.ShapeDtypeStruct((heads, rows, dim), jnp.bfloat16),
            jax.ShapeDtypeStruct((heads, rows, dim), jnp.bfloat16),
            jax.ShapeDtypeStruct((heads, keys, dim), jnp.bfloat16),
            jax.ShapeDtypeStruct((heads, keys, dim), jnp.bfloat16),
        ],
    )(mask, q, do, k, v)


def attend(query_rows, key_rows, value_rows, grad_rows, is_first):
    length = query_rows.shape[0]
    group_size = HEADS // KV_HEADS

    def by_head(rows):
        return (
            rows.reshape(length, KV_HEADS, group_size, HEAD_DIM)
            .transpose(1, 2, 0, 3)
            .reshape(KV_HEADS, group_size * length, HEAD_DIM)
        )

    def from_head(parts):
        return (
            parts.reshape(KV_HEADS, group_size, length, HEAD_DIM)
            .transpose(2, 0, 1, 3)
            .reshape(length, HEADS * HEAD_DIM)
        )

    def kv_by_head(rows):
        return rows.reshape(2 * length, KV_HEADS, HEAD_DIM).transpose(1, 0, 2)

    def kv_from_head(parts):
        return parts.transpose(1, 0, 2).reshape(2 * length, KV_HEADS * HEAD_DIM)

    query_pos = lax.broadcasted_iota(jnp.int32, (group_size * length, 2 * length), 0) % length
    key_pos = lax.broadcasted_iota(jnp.int32, (group_size * length, 2 * length), 1)
    visible = (
        (key_pos > query_pos)
        & (key_pos <= query_pos + length)
        & (jnp.logical_not(is_first) | (key_pos >= length))
    )
    head_out, head_qgrad, key_part, value_part = attention_heads(
        visible.astype(jnp.int32),
        by_head(query_rows),
        by_head(grad_rows),
        kv_by_head(key_rows),
        kv_by_head(value_rows),
    )
    kv_grads = jnp.stack([kv_from_head(key_part), kv_from_head(value_part)])
    return (from_head(head_out), from_head(head_qgrad), kv_grads)


def project_rows(row_block, kv_weight, down_full, up_full):
    low_rank = jnp.einsum(
        "rd,mkd->mrk", row_block, down_full, preferred_element_type=jnp.float32
    ).astype(jnp.bfloat16)
    row_shards, col_shards = lax.axis_size("ctx"), lax.axis_size(("dp", "sub"))
    gathered = lax.all_gather(kv_weight, ("ctx", "dp", "sub"), axis=0, tiled=False)
    gathered = gathered.reshape((row_shards, col_shards) + kv_weight.shape)
    base_part = jnp.einsum(
        "rcd,cimdn->mrin",
        row_block.reshape(row_block.shape[0], row_shards, kv_weight.shape[1]),
        gathered,
        preferred_element_type=jnp.float32,
    ).reshape(2, row_block.shape[0], col_shards * kv_weight.shape[2])
    extra_part = jnp.einsum("mrk,mkc->mrc", low_rank, up_full, preferred_element_type=jnp.float32)
    key_value = (base_part + adapter_scale * extra_part).astype(jnp.bfloat16)
    return (low_rank, key_value)


def gather_adapters(adapter_down, adapter_up):
    axes = ("ctx", "dp", "sub")
    down_cols = adapter_down.shape[2]
    joined = jnp.concatenate([adapter_down, adapter_up], axis=2)
    gathered = lax.all_gather(joined, axes, axis=0, tiled=False)
    shards = gathered.shape[0]

    def unshard(piece):
        return piece.transpose(1, 2, 0, 3).reshape(2, piece.shape[2], shards * piece.shape[3])

    return unshard(gathered[..., :down_cols]), unshard(gathered[..., down_cols:])


def scatter_adapter_grads(down_terms, up_terms):
    axes = ("ctx", "dp", "sub")
    shards = lax.axis_size(axes)
    row_shards, col_shards = lax.axis_size("ctx"), lax.axis_size(("dp", "sub"))
    members, rank = down_terms.shape[0], down_terms.shape[1]

    def shard_major(terms):
        cols = terms.shape[2]
        return terms.transpose(2, 0, 1).reshape(shards, cols // shards, members * rank)

    down_cols = down_terms.shape[2] // shards
    joined = jnp.concatenate([shard_major(down_terms), shard_major(up_terms)], axis=1)
    joined = joined.reshape((row_shards, col_shards) + joined.shape[1:]).swapaxes(0, 1)
    partial = lax.psum_scatter(
        joined.reshape(-1, members * rank), ("dp", "sub"), scatter_dimension=0, tiled=True
    )
    mine = lax.psum_scatter(partial, "ctx", scatter_dimension=0, tiled=True)

    def unshard(piece):
        return piece.reshape(-1, members, rank).transpose(1, 2, 0)

    return unshard(mine[:down_cols]), unshard(mine[down_cols:])


def on_device(hidden, queries, kv_weight, adapter_down, adapter_up, out_grad):
    rows_own = hidden[0]
    query_rows = queries[0]
    grad_rows = out_grad[0]
    length = rows_own.shape[0]
    rows_previous = shifted(rows_own, "ctx", 1)
    down_full, up_full = gather_adapters(adapter_down, adapter_up)
    is_first = lax.axis_index("ctx") == 0
    low_both, kv_both = project_rows(
        jnp.concatenate([rows_previous, rows_own], axis=0), kv_weight, down_full, up_full
    )
    low_previous = low_both[:, :length]
    low_rank = low_both[:, length:]
    key_rows = kv_both[0]
    value_rows = kv_both[1]
    attended, query_grad, kv_grads = attend(query_rows, key_rows, value_rows, grad_rows, is_first)
    kv_rounded = kv_grads
    far_part = kv_rounded[:, :length]
    near_part = kv_rounded[:, length:]
    projected_far = jnp.einsum(
        "mrc,mkc->mrk", far_part, up_full, preferred_element_type=jnp.float32
    ).astype(jnp.bfloat16)
    projected_returned = shifted(projected_far, "ctx", -1)
    projected_near = jnp.einsum(
        "mrc,mkc->mrk", near_part, up_full, preferred_element_type=jnp.float32
    ).astype(jnp.bfloat16)
    up_terms = jnp.einsum(
        "mrk,mrc->mkc", low_rank, near_part, preferred_element_type=jnp.float32
    ) + jnp.einsum(
        "mrk,mrc->mkc", low_previous, far_part, preferred_element_type=jnp.float32
    )
    down_terms = jnp.einsum(
        "mrk,rd->mkd", projected_near, rows_own, preferred_element_type=jnp.float32
    ) + jnp.einsum(
        "mrk,rd->mkd", projected_returned, rows_own, preferred_element_type=jnp.float32
    )
    factor = adapter_scale / (lax.axis_size("dp") * lax.axis_size("sub"))
    down_part, up_part = scatter_adapter_grads(down_terms * factor, up_terms * factor)
    return (attended[None], query_grad[None], down_part, up_part)


def solution(mesh):
    placed = (
        P(("groups", "dp", "sub"), "ctx", None),
        P(("groups", "dp", "sub"), "ctx", None),
        P(None, "ctx", ("dp", "sub")),
        P(None, None, ("ctx", "dp", "sub")),
        P(None, None, ("ctx", "dp", "sub")),
        P(("groups", "dp", "sub"), "ctx", None),
    )
    return jax.shard_map(
        on_device,
        mesh=mesh,
        in_specs=placed,
        out_specs=(
            P(("groups", "dp", "sub"), "ctx", None),
            P(("groups", "dp", "sub"), "ctx", None),
            P("groups", None, ("ctx", "dp", "sub")),
            P("groups", None, ("ctx", "dp", "sub")),
        ),
        check_vma=False,
    )
```

```python
import jax
import jax.numpy as jnp
from jax import lax
from jax.experimental import pallas as pl
from jax.experimental.pallas import tpu as pltpu
from jax.sharding import PartitionSpec as P

HEADS = 16
KV_HEADS = 8
HEAD_DIM = 128


query_scale = 1.0 / 12.0
logit_cap = 50.0
adapter_scale = 0.5


def shifted(value, axis, by):
    length = lax.axis_size(axis)
    pairs = [(i, i + by) for i in range(length) if 0 <= i + by < length]
    return lax.ppermute(value, axis, pairs)


def attention_kernel(mask_ref, q_ref, do_ref, kv_ref, out_ref, dq_ref, dkv_ref):
    half = HEAD_DIM
    q = jnp.concatenate([q_ref[:, :half], q_ref[:, half:]], axis=0)
    do = jnp.concatenate([do_ref[:, :half], do_ref[:, half:]], axis=0)
    k = kv_ref[0]
    v = kv_ref[1]
    rows = q_ref.shape[0]
    visible = mask_ref[...] != 0
    contract_last = (((1,), (1,)), ((), ()))
    raw_score = lax.dot_general(q, k, contract_last, preferred_element_type=jnp.float32) * query_scale
    bent_score = jnp.tanh(raw_score / logit_cap)
    expo_terms = jnp.where(visible, jnp.exp(logit_cap * bent_score), 0.0)
    denominator = jnp.sum(expo_terms, axis=-1, keepdims=True)
    prob_wide = (expo_terms / denominator).astype(jnp.bfloat16).astype(jnp.float32)
    attn_prob = prob_wide.astype(jnp.bfloat16)
    head_out = jnp.dot(attn_prob, v, preferred_element_type=jnp.float32).astype(out_ref.dtype)
    out_ref[:, :half] = head_out[:rows]
    out_ref[:, half:] = head_out[rows:]
    prob_grad = lax.dot_general(do, v, contract_last, preferred_element_type=jnp.float32)
    row_delta = jnp.sum(prob_wide * prob_grad, axis=-1, keepdims=True)
    score_wide = prob_wide * (prob_grad - row_delta) * (1.0 - bent_score * bent_score) * query_scale
    score_grad = score_wide.astype(jnp.bfloat16)
    head_qgrad = jnp.dot(score_grad, k, preferred_element_type=jnp.float32).astype(dq_ref.dtype)
    dq_ref[:, :half] = head_qgrad[:rows]
    dq_ref[:, half:] = head_qgrad[rows:]
    score_t = score_grad.astype(jnp.float32).T.astype(jnp.bfloat16)
    prob_t = prob_wide.T.astype(jnp.bfloat16)
    dkv_ref[0] = jnp.dot(score_t, q, preferred_element_type=jnp.float32).astype(dkv_ref.dtype)
    dkv_ref[1] = jnp.dot(prob_t, do, preferred_element_type=jnp.float32).astype(dkv_ref.dtype)


def attention_heads(mask, queries, grads, key_value):
    rows, width = queries.shape
    keys, kv_width = key_value.shape[1], key_value.shape[2]
    heads = kv_width // HEAD_DIM
    group_cols = width // heads
    row_block = pl.BlockSpec((rows, group_cols), lambda g: (0, g))
    kv_block = pl.BlockSpec((2, keys, HEAD_DIM), lambda g: (0, 0, g))
    return pl.pallas_call(
        attention_kernel,
        grid=(heads,),
        in_specs=[pl.BlockSpec(mask.shape, lambda g: (0, 0)), row_block, row_block, kv_block],
        out_specs=[row_block, row_block, kv_block],
        out_shape=[
            jax.ShapeDtypeStruct((rows, width), jnp.bfloat16),
            jax.ShapeDtypeStruct((rows, width), jnp.bfloat16),
            jax.ShapeDtypeStruct(key_value.shape, jnp.bfloat16),
        ],
    )(mask, queries, grads, key_value)


def attend(query_rows, key_value, grad_rows, is_first):
    length = query_rows.shape[0]
    group_size = HEADS // KV_HEADS
    query_pos = lax.broadcasted_iota(jnp.int32, (group_size * length, 2 * length), 0) % length
    key_pos = lax.broadcasted_iota(jnp.int32, (group_size * length, 2 * length), 1)
    visible = (
        (key_pos > query_pos)
        & (key_pos <= query_pos + length)
        & (jnp.logical_not(is_first) | (key_pos >= length))
    )
    return attention_heads(visible.astype(jnp.int32), query_rows, grad_rows, key_value)


def project_rows(row_block, kv_weight, down_full, up_full):
    low_rank = jnp.einsum(
        "rd,mkd->mrk", row_block, down_full, preferred_element_type=jnp.float32
    ).astype(jnp.bfloat16)
    row_shards, col_shards = lax.axis_size("ctx"), lax.axis_size(("dp", "sub"))
    gathered = lax.all_gather(kv_weight, ("ctx", "dp", "sub"), axis=0, tiled=False)
    gathered = gathered.reshape((row_shards, col_shards) + kv_weight.shape)
    base_part = jnp.einsum(
        "rcd,cimdn->mrin",
        row_block.reshape(row_block.shape[0], row_shards, kv_weight.shape[1]),
        gathered,
        preferred_element_type=jnp.float32,
    ).reshape(2, row_block.shape[0], col_shards * kv_weight.shape[2])
    extra_part = jnp.einsum("mrk,mkc->mrc", low_rank, up_full, preferred_element_type=jnp.float32)
    key_value = (base_part + adapter_scale * extra_part).astype(jnp.bfloat16)
    return (low_rank, key_value)


def gather_adapters(adapter_down, adapter_up):
    axes = ("ctx", "dp", "sub")
    down_cols = adapter_down.shape[2]
    joined = jnp.concatenate([adapter_down, adapter_up], axis=2)
    gathered = lax.all_gather(joined, axes, axis=0, tiled=False)
    shards = gathered.shape[0]

    def unshard(piece):
        return piece.transpose(1, 2, 0, 3).reshape(2, piece.shape[2], shards * piece.shape[3])

    return unshard(gathered[..., :down_cols]), unshard(gathered[..., down_cols:])


def scatter_adapter_grads(joined_down, joined_up):
    members_rank = joined_down.shape[-1]
    down_cols = joined_down.shape[2]
    joined = jnp.concatenate([joined_down, joined_up], axis=2)
    partial = lax.psum_scatter(
        joined.reshape(-1, members_rank), ("dp", "sub"), scatter_dimension=0, tiled=True
    )
    mine = lax.psum_scatter(partial, "ctx", scatter_dimension=0, tiled=True)

    def unshard(piece):
        return piece.reshape(piece.shape[0], 2, -1).transpose(1, 2, 0)

    return unshard(mine[:down_cols]), unshard(mine[down_cols:])


def on_device(hidden, queries, kv_weight, adapter_down, adapter_up, out_grad):
    rows_own = hidden[0]
    query_rows = queries[0]
    grad_rows = out_grad[0]
    length = rows_own.shape[0]
    row_shards, col_shards = lax.axis_size("ctx"), lax.axis_size(("dp", "sub"))
    rows_previous = shifted(rows_own, "ctx", 1)
    down_full, up_full = gather_adapters(adapter_down, adapter_up)
    is_first = lax.axis_index("ctx") == 0
    low_both, kv_both = project_rows(
        jnp.concatenate([rows_previous, rows_own], axis=0), kv_weight, down_full, up_full
    )
    low_previous = low_both[:, :length]
    low_rank = low_both[:, length:]
    attended, query_grad, kv_grads = attend(query_rows, kv_both, grad_rows, is_first)
    far_part = kv_grads[:, :length]
    near_part = kv_grads[:, length:]
    projected_far = jnp.einsum(
        "mrc,mkc->mrk", far_part, up_full, preferred_element_type=jnp.float32
    ).astype(jnp.bfloat16)
    projected_returned = shifted(projected_far, "ctx", -1)
    projected_near = jnp.einsum(
        "mrc,mkc->mrk", near_part, up_full, preferred_element_type=jnp.float32
    ).astype(jnp.bfloat16)
    shards = row_shards * col_shards
    rows_split = rows_own.reshape(length, row_shards, col_shards, -1)

    def split_cols(part):
        return part.reshape(part.shape[:2] + (row_shards, col_shards, -1))

    up_terms = jnp.einsum(
        "mrk,mrcij->icjmk", low_rank, split_cols(near_part), preferred_element_type=jnp.float32
    ) + jnp.einsum(
        "mrk,mrcij->icjmk", low_previous, split_cols(far_part), preferred_element_type=jnp.float32
    )
    down_terms = jnp.einsum(
        "mrk,rcij->icjmk", projected_near, rows_split, preferred_element_type=jnp.float32
    ) + jnp.einsum(
        "mrk,rcij->icjmk", projected_returned, rows_split, preferred_element_type=jnp.float32
    )
    factor = adapter_scale / (lax.axis_size("dp") * lax.axis_size("sub"))
    flat = lambda terms: (terms * factor).reshape(terms.shape[:3] + (-1,))
    down_part, up_part = scatter_adapter_grads(flat(down_terms), flat(up_terms))
    return (attended[None], query_grad[None], down_part, up_part)


def solution(mesh):
    placed = (
        P(("groups", "dp", "sub"), "ctx", None),
        P(("groups", "dp", "sub"), "ctx", None),
        P(None, "ctx", ("dp", "sub")),
        P(None, None, ("ctx", "dp", "sub")),
        P(None, None, ("ctx", "dp", "sub")),
        P(("groups", "dp", "sub"), "ctx", None),
    )
    return jax.shard_map(
        on_device,
        mesh=mesh,
        in_specs=placed,
        out_specs=(
            P(("groups", "dp", "sub"), "ctx", None),
            P(("groups", "dp", "sub"), "ctx", None),
            P("groups", None, ("ctx", "dp", "sub")),
            P("groups", None, ("ctx", "dp", "sub")),
        ),
        check_vma=False,
    )
```

```python
import jax
import jax.numpy as jnp
from jax import lax
from jax.experimental import pallas as pl
from jax.experimental.pallas import tpu as pltpu
from jax.sharding import PartitionSpec as P

HEADS = 16
KV_HEADS = 8
HEAD_DIM = 128


query_scale = 1.0 / 12.0
logit_cap = 50.0
adapter_scale = 0.5


def shifted(value, axis, by):
    length = lax.axis_size(axis)
    pairs = [(i, i + by) for i in range(length) if 0 <= i + by < length]
    return lax.ppermute(value, axis, pairs)


def attention_kernel(mask_ref, q_ref, do_ref, kv_ref, out_ref, dq_ref, dkv_ref):
    half = HEAD_DIM
    q = jnp.concatenate([q_ref[:, :half], q_ref[:, half:]], axis=0)
    do = jnp.concatenate([do_ref[:, :half], do_ref[:, half:]], axis=0)
    k = kv_ref[0]
    v = kv_ref[1]
    rows = q_ref.shape[0]
    visible = mask_ref[...] != 0
    contract_last = (((1,), (1,)), ((), ()))
    raw_score = lax.dot_general(q, k, contract_last, preferred_element_type=jnp.float32) * query_scale
    bent_score = jnp.tanh(raw_score / logit_cap)
    expo_terms = jnp.where(visible, jnp.exp(logit_cap * bent_score), 0.0)
    denominator = jnp.sum(expo_terms, axis=-1, keepdims=True)
    prob_wide = (expo_terms / denominator).astype(jnp.bfloat16).astype(jnp.float32)
    attn_prob = prob_wide.astype(jnp.bfloat16)
    head_out = jnp.dot(attn_prob, v, preferred_element_type=jnp.float32).astype(out_ref.dtype)
    out_ref[:, :half] = head_out[:rows]
    out_ref[:, half:] = head_out[rows:]
    prob_grad = lax.dot_general(do, v, contract_last, preferred_element_type=jnp.float32)
    row_delta = jnp.sum(prob_wide * prob_grad, axis=-1, keepdims=True)
    score_wide = prob_wide * (prob_grad - row_delta) * (1.0 - bent_score * bent_score) * query_scale
    score_grad = score_wide.astype(jnp.bfloat16)
    head_qgrad = jnp.dot(score_grad, k, preferred_element_type=jnp.float32).astype(dq_ref.dtype)
    dq_ref[:, :half] = head_qgrad[:rows]
    dq_ref[:, half:] = head_qgrad[rows:]
    score_t = score_grad.astype(jnp.float32).T.astype(jnp.bfloat16)
    prob_t = prob_wide.T.astype(jnp.bfloat16)
    dkv_ref[0] = jnp.dot(score_t, q, preferred_element_type=jnp.float32).astype(dkv_ref.dtype)
    dkv_ref[1] = jnp.dot(prob_t, do, preferred_element_type=jnp.float32).astype(dkv_ref.dtype)


def attention_heads(mask, queries, grads, key_value):
    rows, width = queries.shape
    keys, kv_width = key_value.shape[1], key_value.shape[2]
    heads = kv_width // HEAD_DIM
    group_cols = width // heads
    row_block = pl.BlockSpec((rows, group_cols), lambda g: (0, g))
    kv_block = pl.BlockSpec((2, keys, HEAD_DIM), lambda g: (0, 0, g))
    return pl.pallas_call(
        attention_kernel,
        grid=(heads,),
        in_specs=[pl.BlockSpec(mask.shape, lambda g: (0, 0)), row_block, row_block, kv_block],
        out_specs=[row_block, row_block, kv_block],
        out_shape=[
            jax.ShapeDtypeStruct((rows, width), jnp.bfloat16),
            jax.ShapeDtypeStruct((rows, width), jnp.bfloat16),
            jax.ShapeDtypeStruct(key_value.shape, jnp.bfloat16),
        ],
    )(mask, queries, grads, key_value)


def attend(query_rows, key_value, grad_rows, is_first):
    length = query_rows.shape[0]
    group_size = HEADS // KV_HEADS
    query_pos = lax.broadcasted_iota(jnp.int32, (group_size * length, 2 * length), 0) % length
    key_pos = lax.broadcasted_iota(jnp.int32, (group_size * length, 2 * length), 1)
    visible = (
        (key_pos > query_pos)
        & (key_pos <= query_pos + length)
        & (jnp.logical_not(is_first) | (key_pos >= length))
    )
    return attention_heads(visible.astype(jnp.int32), query_rows, grad_rows, key_value)


def projection_kernel(prev_ref, own_ref, weight_ref, low_prev_ref, low_own_ref, up_ref, out_ref):
    row_shards = weight_ref.shape[0]
    depth = weight_ref.shape[3]
    rows = own_ref.shape[0]
    up = up_ref[0]
    for half, (rows_ref, low_ref) in enumerate(((prev_ref, low_prev_ref), (own_ref, low_own_ref))):
        total = jnp.dot(low_ref[0], up, preferred_element_type=jnp.float32) * adapter_scale
        base = jnp.dot(
            rows_ref[:, :depth], weight_ref[0, 0, 0], preferred_element_type=jnp.float32
        )
        for c in range(1, row_shards):
            base = base + jnp.dot(
                rows_ref[:, c * depth:(c + 1) * depth],
                weight_ref[c, 0, 0],
                preferred_element_type=jnp.float32,
            )
        out_ref[0, half * rows:(half + 1) * rows, :] = (base + total).astype(out_ref.dtype)


def project_pair(rows_prev, rows_own, gathered, low_prev, low_own, up_full):
    row_shards, col_shards, members, depth, cols = gathered.shape
    rows, width = rows_own.shape
    rank = up_full.shape[1]
    return pl.pallas_call(
        projection_kernel,
        grid=(members, col_shards),
        in_specs=[
            pl.BlockSpec((rows, width), lambda m, i: (0, 0)),
            pl.BlockSpec((rows, width), lambda m, i: (0, 0)),
            pl.BlockSpec((row_shards, 1, 1, depth, cols), lambda m, i: (0, i, m, 0, 0)),
            pl.BlockSpec((1, rows, rank), lambda m, i: (m, 0, 0)),
            pl.BlockSpec((1, rows, rank), lambda m, i: (m, 0, 0)),
            pl.BlockSpec((1, rank, cols), lambda m, i: (m, 0, i)),
        ],
        out_specs=pl.BlockSpec((1, 2 * rows, cols), lambda m, i: (m, 0, i)),
        out_shape=jax.ShapeDtypeStruct((members, 2 * rows, col_shards * cols), jnp.bfloat16),
    )(rows_prev, rows_own, gathered, low_prev, low_own, up_full)


def project_rows(rows_previous, rows_own, kv_weight, down_full, up_full):
    def low_of(rows):
        return jnp.einsum(
            "rd,mkd->mrk", rows, down_full, preferred_element_type=jnp.float32
        ).astype(jnp.bfloat16)

    low_previous, low_rank = low_of(rows_previous), low_of(rows_own)
    row_shards, col_shards = lax.axis_size("ctx"), lax.axis_size(("dp", "sub"))
    gathered = lax.all_gather(kv_weight, ("ctx", "dp", "sub"), axis=0, tiled=False)
    gathered = gathered.reshape((row_shards, col_shards) + kv_weight.shape)
    key_value = project_pair(rows_previous, rows_own, gathered, low_previous, low_rank, up_full)
    return low_previous, low_rank, key_value


def gather_adapters(adapter_down, adapter_up):
    axes = ("ctx", "dp", "sub")
    down_cols = adapter_down.shape[2]
    joined = jnp.concatenate([adapter_down, adapter_up], axis=2)
    gathered = lax.all_gather(joined, axes, axis=0, tiled=False)
    shards = gathered.shape[0]

    def unshard(piece):
        return piece.transpose(1, 2, 0, 3).reshape(2, piece.shape[2], shards * piece.shape[3])

    return unshard(gathered[..., :down_cols]), unshard(gathered[..., down_cols:])


def scatter_adapter_grads(joined_down, joined_up):
    members_rank = joined_down.shape[-1]
    down_cols = joined_down.shape[2]
    joined = jnp.concatenate([joined_down, joined_up], axis=2)
    partial = lax.psum_scatter(
        joined.reshape(-1, members_rank), ("dp", "sub"), scatter_dimension=0, tiled=True
    )
    mine = lax.psum_scatter(partial, "ctx", scatter_dimension=0, tiled=True)

    def unshard(piece):
        return piece.reshape(piece.shape[0], 2, -1).transpose(1, 2, 0)

    return unshard(mine[:down_cols]), unshard(mine[down_cols:])


def on_device(hidden, queries, kv_weight, adapter_down, adapter_up, out_grad):
    rows_own = hidden[0]
    query_rows = queries[0]
    grad_rows = out_grad[0]
    length = rows_own.shape[0]
    row_shards, col_shards = lax.axis_size("ctx"), lax.axis_size(("dp", "sub"))
    rows_previous = shifted(rows_own, "ctx", 1)
    down_full, up_full = gather_adapters(adapter_down, adapter_up)
    is_first = lax.axis_index("ctx") == 0
    low_previous, low_rank, kv_both = project_rows(
        rows_previous, rows_own, kv_weight, down_full, up_full
    )
    attended, query_grad, kv_grads = attend(query_rows, kv_both, grad_rows, is_first)
    far_part = kv_grads[:, :length]
    near_part = kv_grads[:, length:]
    projected_far = jnp.einsum(
        "mrc,mkc->mrk", far_part, up_full, preferred_element_type=jnp.float32
    ).astype(jnp.bfloat16)
    projected_returned = shifted(projected_far, "ctx", -1)
    projected_near = jnp.einsum(
        "mrc,mkc->mrk", near_part, up_full, preferred_element_type=jnp.float32
    ).astype(jnp.bfloat16)
    shards = row_shards * col_shards
    rows_split = rows_own.reshape(length, row_shards, col_shards, -1)

    def split_cols(part):
        return part.reshape(part.shape[:2] + (row_shards, col_shards, -1))

    up_terms = jnp.einsum(
        "mrk,mrcij->icjmk", low_rank, split_cols(near_part), preferred_element_type=jnp.float32
    ) + jnp.einsum(
        "mrk,mrcij->icjmk", low_previous, split_cols(far_part), preferred_element_type=jnp.float32
    )
    down_terms = jnp.einsum(
        "mrk,rcij->icjmk", projected_near, rows_split, preferred_element_type=jnp.float32
    ) + jnp.einsum(
        "mrk,rcij->icjmk", projected_returned, rows_split, preferred_element_type=jnp.float32
    )
    factor = adapter_scale / (lax.axis_size("dp") * lax.axis_size("sub"))
    flat = lambda terms: (terms * factor).reshape(terms.shape[:3] + (-1,))
    down_part, up_part = scatter_adapter_grads(flat(down_terms), flat(up_terms))
    return (attended[None], query_grad[None], down_part, up_part)


def solution(mesh):
    placed = (
        P(("groups", "dp", "sub"), "ctx", None),
        P(("groups", "dp", "sub"), "ctx", None),
        P(None, "ctx", ("dp", "sub")),
        P(None, None, ("ctx", "dp", "sub")),
        P(None, None, ("ctx", "dp", "sub")),
        P(("groups", "dp", "sub"), "ctx", None),
    )
    return jax.shard_map(
        on_device,
        mesh=mesh,
        in_specs=placed,
        out_specs=(
            P(("groups", "dp", "sub"), "ctx", None),
            P(("groups", "dp", "sub"), "ctx", None),
            P("groups", None, ("ctx", "dp", "sub")),
            P("groups", None, ("ctx", "dp", "sub")),
        ),
        check_vma=False,
    )
```

```python
import jax
import jax.numpy as jnp
from jax import lax
from jax.experimental import pallas as pl
from jax.experimental.pallas import tpu as pltpu
from jax.sharding import PartitionSpec as P

HEADS = 16
KV_HEADS = 8
HEAD_DIM = 128


query_scale = 1.0 / 12.0
logit_cap = 50.0
adapter_scale = 0.5


def shifted(value, axis, by):
    length = lax.axis_size(axis)
    pairs = [(i, i + by) for i in range(length) if 0 <= i + by < length]
    return lax.ppermute(value, axis, pairs)


def attention_kernel(mask_ref, q_ref, do_ref, kv_ref, out_ref, dq_ref, dkv_ref):
    half = HEAD_DIM
    q = jnp.concatenate([q_ref[:, :half], q_ref[:, half:]], axis=0)
    do = jnp.concatenate([do_ref[:, :half], do_ref[:, half:]], axis=0)
    k = kv_ref[0]
    v = kv_ref[1]
    rows = q_ref.shape[0]
    visible = mask_ref[...] != 0
    contract_last = (((1,), (1,)), ((), ()))
    raw_score = lax.dot_general(q, k, contract_last, preferred_element_type=jnp.float32) * query_scale
    bent_score = jnp.tanh(raw_score / logit_cap)
    expo_terms = jnp.where(visible, jnp.exp(logit_cap * bent_score), 0.0)
    denominator = jnp.sum(expo_terms, axis=-1, keepdims=True)
    prob_wide = (expo_terms / denominator).astype(jnp.bfloat16).astype(jnp.float32)
    attn_prob = prob_wide.astype(jnp.bfloat16)
    head_out = jnp.dot(attn_prob, v, preferred_element_type=jnp.float32).astype(out_ref.dtype)
    out_ref[:, :half] = head_out[:rows]
    out_ref[:, half:] = head_out[rows:]
    prob_grad = lax.dot_general(do, v, contract_last, preferred_element_type=jnp.float32)
    row_delta = jnp.sum(prob_wide * prob_grad, axis=-1, keepdims=True)
    score_wide = prob_wide * (prob_grad - row_delta) * (1.0 - bent_score * bent_score) * query_scale
    score_grad = score_wide.astype(jnp.bfloat16)
    head_qgrad = jnp.dot(score_grad, k, preferred_element_type=jnp.float32).astype(dq_ref.dtype)
    dq_ref[:, :half] = head_qgrad[:rows]
    dq_ref[:, half:] = head_qgrad[rows:]
    score_t = score_grad.astype(jnp.float32).T.astype(jnp.bfloat16)
    prob_t = prob_wide.T.astype(jnp.bfloat16)
    dkv_ref[0] = jnp.dot(score_t, q, preferred_element_type=jnp.float32).astype(dkv_ref.dtype)
    dkv_ref[1] = jnp.dot(prob_t, do, preferred_element_type=jnp.float32).astype(dkv_ref.dtype)


def attention_heads(mask, queries, grads, key_value):
    rows, width = queries.shape
    keys, kv_width = key_value.shape[1], key_value.shape[2]
    heads = kv_width // HEAD_DIM
    group_cols = width // heads
    row_block = pl.BlockSpec((rows, group_cols), lambda g: (0, g))
    kv_block = pl.BlockSpec((2, keys, HEAD_DIM), lambda g: (0, 0, g))
    return pl.pallas_call(
        attention_kernel,
        grid=(heads,),
        in_specs=[pl.BlockSpec(mask.shape, lambda g: (0, 0)), row_block, row_block, kv_block],
        out_specs=[row_block, row_block, kv_block],
        out_shape=[
            jax.ShapeDtypeStruct((rows, width), jnp.bfloat16),
            jax.ShapeDtypeStruct((rows, width), jnp.bfloat16),
            jax.ShapeDtypeStruct(key_value.shape, jnp.bfloat16),
        ],
    )(mask, queries, grads, key_value)


def attend(query_rows, key_value, grad_rows, is_first):
    length = query_rows.shape[0]
    group_size = HEADS // KV_HEADS
    query_pos = lax.broadcasted_iota(jnp.int32, (group_size * length, 2 * length), 0) % length
    key_pos = lax.broadcasted_iota(jnp.int32, (group_size * length, 2 * length), 1)
    visible = (
        (key_pos > query_pos)
        & (key_pos <= query_pos + length)
        & (jnp.logical_not(is_first) | (key_pos >= length))
    )
    return attention_heads(visible.astype(jnp.int32), query_rows, grad_rows, key_value)


def projection_kernel(prev_ref, own_ref, weight_ref, low_prev_ref, low_own_ref, up_ref, out_ref):
    row_shards = weight_ref.shape[0]
    depth = weight_ref.shape[3]
    rows = own_ref.shape[0]
    up = up_ref[0]
    for half, (rows_ref, low_ref) in enumerate(((prev_ref, low_prev_ref), (own_ref, low_own_ref))):
        total = jnp.dot(low_ref[0], up, preferred_element_type=jnp.float32) * adapter_scale
        if depth % 16 == 0:
            weight = jnp.concatenate([weight_ref[c, 0, 0] for c in range(row_shards)], axis=0)
            base = jnp.dot(rows_ref[...], weight, preferred_element_type=jnp.float32)
        else:
            base = jnp.dot(
                rows_ref[:, :depth], weight_ref[0, 0, 0], preferred_element_type=jnp.float32
            )
            for c in range(1, row_shards):
                base = base + jnp.dot(
                    rows_ref[:, c * depth:(c + 1) * depth],
                    weight_ref[c, 0, 0],
                    preferred_element_type=jnp.float32,
                )
        out_ref[0, half * rows:(half + 1) * rows, :] = (base + total).astype(out_ref.dtype)


def project_pair(rows_prev, rows_own, gathered, low_prev, low_own, up_full):
    row_shards, col_shards, members, depth, cols = gathered.shape
    rows, width = rows_own.shape
    rank = up_full.shape[1]
    return pl.pallas_call(
        projection_kernel,
        grid=(members, col_shards),
        in_specs=[
            pl.BlockSpec((rows, width), lambda m, i: (0, 0)),
            pl.BlockSpec((rows, width), lambda m, i: (0, 0)),
            pl.BlockSpec((row_shards, 1, 1, depth, cols), lambda m, i: (0, i, m, 0, 0)),
            pl.BlockSpec((1, rows, rank), lambda m, i: (m, 0, 0)),
            pl.BlockSpec((1, rows, rank), lambda m, i: (m, 0, 0)),
            pl.BlockSpec((1, rank, cols), lambda m, i: (m, 0, i)),
        ],
        out_specs=pl.BlockSpec((1, 2 * rows, cols), lambda m, i: (m, 0, i)),
        out_shape=jax.ShapeDtypeStruct((members, 2 * rows, col_shards * cols), jnp.bfloat16),
    )(rows_prev, rows_own, gathered, low_prev, low_own, up_full)


def project_rows(rows_previous, rows_own, kv_weight, down_full, up_full):
    def low_of(rows):
        return jnp.einsum(
            "rd,mkd->mrk", rows, down_full, preferred_element_type=jnp.float32
        ).astype(jnp.bfloat16)

    low_previous, low_rank = low_of(rows_previous), low_of(rows_own)
    row_shards, col_shards = lax.axis_size("ctx"), lax.axis_size(("dp", "sub"))
    gathered = lax.all_gather(kv_weight, ("ctx", "dp", "sub"), axis=0, tiled=False)
    gathered = gathered.reshape((row_shards, col_shards) + kv_weight.shape)
    key_value = project_pair(rows_previous, rows_own, gathered, low_previous, low_rank, up_full)
    return low_previous, low_rank, key_value


def gather_adapters(adapter_down, adapter_up):
    axes = ("ctx", "dp", "sub")
    down_cols = adapter_down.shape[2]
    joined = jnp.concatenate([adapter_down, adapter_up], axis=2)
    gathered = lax.all_gather(joined, axes, axis=0, tiled=False)
    shards = gathered.shape[0]

    def unshard(piece):
        return piece.transpose(1, 2, 0, 3).reshape(2, piece.shape[2], shards * piece.shape[3])

    return unshard(gathered[..., :down_cols]), unshard(gathered[..., down_cols:])


def halving_scatter(blocks, axis):
    size = lax.axis_size(axis)
    if size & (size - 1):
        return lax.psum_scatter(blocks, axis, scatter_dimension=0, tiled=True)[0]
    me = lax.axis_index(axis)
    stride = size // 2
    while stride >= 1:
        halves = blocks.reshape((2, blocks.shape[0] // 2) + blocks.shape[1:])
        bit = (me // stride) % 2
        keep = lax.dynamic_index_in_dim(halves, bit, axis=0, keepdims=False)
        send = lax.dynamic_index_in_dim(halves, 1 - bit, axis=0, keepdims=False)
        pairs = [(i, i ^ stride) for i in range(size)]
        blocks = keep + lax.ppermute(send, axis, pairs)
        stride //= 2
    return blocks[0]


def scatter_adapter_grads(joined_down, joined_up):
    members_rank = joined_down.shape[-1]
    down_cols = joined_down.shape[2]
    joined = jnp.concatenate([joined_down, joined_up], axis=2)
    dp_size, sub_size = lax.axis_size("dp"), lax.axis_size("sub")
    joined = joined.reshape((dp_size, sub_size) + joined.shape[1:])
    mine = halving_scatter(joined.swapaxes(0, 1), "sub")
    mine = halving_scatter(mine, "dp")
    mine = halving_scatter(mine, "ctx")

    def unshard(piece):
        return piece.reshape(piece.shape[0], 2, -1).transpose(1, 2, 0)

    return unshard(mine[:down_cols]), unshard(mine[down_cols:])


def on_device(hidden, queries, kv_weight, adapter_down, adapter_up, out_grad):
    rows_own = hidden[0]
    query_rows = queries[0]
    grad_rows = out_grad[0]
    length = rows_own.shape[0]
    row_shards, col_shards = lax.axis_size("ctx"), lax.axis_size(("dp", "sub"))
    rows_previous = shifted(rows_own, "ctx", 1)
    down_full, up_full = gather_adapters(adapter_down, adapter_up)
    is_first = lax.axis_index("ctx") == 0
    low_previous, low_rank, kv_both = project_rows(
        rows_previous, rows_own, kv_weight, down_full, up_full
    )
    attended, query_grad, kv_grads = attend(query_rows, kv_both, grad_rows, is_first)
    far_part = kv_grads[:, :length]
    near_part = kv_grads[:, length:]
    projected_far = jnp.einsum(
        "mrc,mkc->mrk", far_part, up_full, preferred_element_type=jnp.float32
    ).astype(jnp.bfloat16)
    projected_returned = shifted(projected_far, "ctx", -1)
    projected_near = jnp.einsum(
        "mrc,mkc->mrk", near_part, up_full, preferred_element_type=jnp.float32
    ).astype(jnp.bfloat16)
    shards = row_shards * col_shards
    rows_split = rows_own.reshape(length, row_shards, col_shards, -1)

    def split_cols(part):
        return part.reshape(part.shape[:2] + (row_shards, col_shards, -1))

    up_terms = jnp.einsum(
        "mrk,mrcij->icjmk", low_rank, split_cols(near_part), preferred_element_type=jnp.float32
    ) + jnp.einsum(
        "mrk,mrcij->icjmk", low_previous, split_cols(far_part), preferred_element_type=jnp.float32
    )
    down_terms = jnp.einsum(
        "mrk,rcij->icjmk", projected_near, rows_split, preferred_element_type=jnp.float32
    ) + jnp.einsum(
        "mrk,rcij->icjmk", projected_returned, rows_split, preferred_element_type=jnp.float32
    )
    factor = adapter_scale / (lax.axis_size("dp") * lax.axis_size("sub"))
    flat = lambda terms: (terms * factor).reshape(terms.shape[:3] + (-1,))
    down_part, up_part = scatter_adapter_grads(flat(down_terms), flat(up_terms))
    return (attended[None], query_grad[None], down_part, up_part)


def solution(mesh):
    placed = (
        P(("groups", "dp", "sub"), "ctx", None),
        P(("groups", "dp", "sub"), "ctx", None),
        P(None, "ctx", ("dp", "sub")),
        P(None, None, ("ctx", "dp", "sub")),
        P(None, None, ("ctx", "dp", "sub")),
        P(("groups", "dp", "sub"), "ctx", None),
    )
    return jax.shard_map(
        on_device,
        mesh=mesh,
        in_specs=placed,
        out_specs=(
            P(("groups", "dp", "sub"), "ctx", None),
            P(("groups", "dp", "sub"), "ctx", None),
            P("groups", None, ("ctx", "dp", "sub")),
            P("groups", None, ("ctx", "dp", "sub")),
        ),
        check_vma=False,
    )
```

```python
import jax
import jax.numpy as jnp
from jax import lax
from jax.experimental import pallas as pl
from jax.experimental.pallas import tpu as pltpu
from jax.sharding import PartitionSpec as P

HEADS = 16
KV_HEADS = 8
HEAD_DIM = 128


query_scale = 1.0 / 12.0
logit_cap = 50.0
adapter_scale = 0.5


def shifted(value, axis, by):
    length = lax.axis_size(axis)
    pairs = [(i, i + by) for i in range(length) if 0 <= i + by < length]
    return lax.ppermute(value, axis, pairs)


def attention_kernel(mask_ref, q_ref, do_ref, kv_ref, out_ref, dq_ref, dkv_ref):
    half = HEAD_DIM
    q = jnp.concatenate([q_ref[:, :half], q_ref[:, half:]], axis=0)
    do = jnp.concatenate([do_ref[:, :half], do_ref[:, half:]], axis=0)
    k = kv_ref[0]
    v = kv_ref[1]
    rows = q_ref.shape[0]
    visible = mask_ref[...] != 0
    contract_last = (((1,), (1,)), ((), ()))
    raw_score = lax.dot_general(q, k, contract_last, preferred_element_type=jnp.float32) * query_scale
    bent_score = jnp.tanh(raw_score / logit_cap)
    expo_terms = jnp.where(visible, jnp.exp(logit_cap * bent_score), 0.0)
    denominator = jnp.sum(expo_terms, axis=-1, keepdims=True)
    prob_wide = (expo_terms / denominator).astype(jnp.bfloat16).astype(jnp.float32)
    attn_prob = prob_wide.astype(jnp.bfloat16)
    head_out = jnp.dot(attn_prob, v, preferred_element_type=jnp.float32).astype(out_ref.dtype)
    out_ref[:, :half] = head_out[:rows]
    out_ref[:, half:] = head_out[rows:]
    prob_grad = lax.dot_general(do, v, contract_last, preferred_element_type=jnp.float32)
    row_delta = jnp.sum(prob_wide * prob_grad, axis=-1, keepdims=True)
    score_wide = prob_wide * (prob_grad - row_delta) * (1.0 - bent_score * bent_score) * query_scale
    score_grad = score_wide.astype(jnp.bfloat16)
    head_qgrad = jnp.dot(score_grad, k, preferred_element_type=jnp.float32).astype(dq_ref.dtype)
    dq_ref[:, :half] = head_qgrad[:rows]
    dq_ref[:, half:] = head_qgrad[rows:]
    score_t = score_grad.astype(jnp.float32).T.astype(jnp.bfloat16)
    prob_t = prob_wide.T.astype(jnp.bfloat16)
    dkv_ref[0] = jnp.dot(score_t, q, preferred_element_type=jnp.float32).astype(dkv_ref.dtype)
    dkv_ref[1] = jnp.dot(prob_t, do, preferred_element_type=jnp.float32).astype(dkv_ref.dtype)


def attention_heads(mask, queries, grads, key_value):
    rows, width = queries.shape
    keys, kv_width = key_value.shape[1], key_value.shape[2]
    heads = kv_width // HEAD_DIM
    group_cols = width // heads
    row_block = pl.BlockSpec((rows, group_cols), lambda g: (0, g))
    kv_block = pl.BlockSpec((2, keys, HEAD_DIM), lambda g: (0, 0, g))
    return pl.pallas_call(
        attention_kernel,
        grid=(heads,),
        in_specs=[pl.BlockSpec(mask.shape, lambda g: (0, 0)), row_block, row_block, kv_block],
        out_specs=[row_block, row_block, kv_block],
        out_shape=[
            jax.ShapeDtypeStruct((rows, width), jnp.bfloat16),
            jax.ShapeDtypeStruct((rows, width), jnp.bfloat16),
            jax.ShapeDtypeStruct(key_value.shape, jnp.bfloat16),
        ],
    )(mask, queries, grads, key_value)


def attend(query_rows, key_value, grad_rows, is_first):
    length = query_rows.shape[0]
    group_size = HEADS // KV_HEADS
    query_pos = lax.broadcasted_iota(jnp.int32, (group_size * length, 2 * length), 0) % length
    key_pos = lax.broadcasted_iota(jnp.int32, (group_size * length, 2 * length), 1)
    visible = (
        (key_pos > query_pos)
        & (key_pos <= query_pos + length)
        & (jnp.logical_not(is_first) | (key_pos >= length))
    )
    return attention_heads(visible.astype(jnp.int32), query_rows, grad_rows, key_value)


def projection_kernel(rows_ref, weight_ref, low_ref, up_ref, out_ref):
    row_shards = weight_ref.shape[0]
    base = jnp.dot(low_ref[0], up_ref[0], preferred_element_type=jnp.float32) * adapter_scale
    for c in range(row_shards):
        base = base + jnp.dot(rows_ref[c], weight_ref[c, 0, 0], preferred_element_type=jnp.float32)
    out_ref[0] = base.astype(out_ref.dtype)


def project_pair(rows_split, gathered, low_rows, up_full):
    row_shards, col_shards, members, depth, cols = gathered.shape
    rows = rows_split.shape[1]
    rank = up_full.shape[1]
    return pl.pallas_call(
        projection_kernel,
        grid=(members, col_shards),
        in_specs=[
            pl.BlockSpec((row_shards, rows, depth), lambda m, i: (0, 0, 0)),
            pl.BlockSpec((row_shards, 1, 1, depth, cols), lambda m, i: (0, i, m, 0, 0)),
            pl.BlockSpec((1, rows, rank), lambda m, i: (m, 0, 0)),
            pl.BlockSpec((1, rank, cols), lambda m, i: (m, 0, i)),
        ],
        out_specs=pl.BlockSpec((1, rows, cols), lambda m, i: (m, 0, i)),
        out_shape=jax.ShapeDtypeStruct((members, rows, col_shards * cols), jnp.bfloat16),
    )(rows_split, gathered, low_rows, up_full)


def project_rows(rows_previous, rows_own, kv_weight, down_full, up_full):
    def low_of(rows):
        return jnp.einsum(
            "rd,mkd->mrk", rows, down_full, preferred_element_type=jnp.float32
        ).astype(jnp.bfloat16)

    low_previous, low_rank = low_of(rows_previous), low_of(rows_own)
    row_shards, col_shards = lax.axis_size("ctx"), lax.axis_size(("dp", "sub"))
    rows_both = jnp.concatenate([rows_previous, rows_own], axis=0)
    rows_split = rows_both.reshape(rows_both.shape[0], row_shards, -1).swapaxes(0, 1)
    gathered = lax.all_gather(kv_weight, ("ctx", "dp", "sub"), axis=0, tiled=False)
    gathered = gathered.reshape((row_shards, col_shards) + kv_weight.shape)
    low_rows = jnp.concatenate([low_previous, low_rank], axis=1)
    key_value = project_pair(rows_split, gathered, low_rows, up_full)
    return low_previous, low_rank, key_value


def gather_adapters(adapter_down, adapter_up):
    axes = ("ctx", "dp", "sub")
    down_cols = adapter_down.shape[2]
    joined = jnp.concatenate([adapter_down, adapter_up], axis=2)
    gathered = lax.all_gather(joined, axes, axis=0, tiled=False)
    shards = gathered.shape[0]

    def unshard(piece):
        return piece.transpose(1, 2, 0, 3).reshape(2, piece.shape[2], shards * piece.shape[3])

    return unshard(gathered[..., :down_cols]), unshard(gathered[..., down_cols:])


def halving_scatter(blocks, axis):
    size = lax.axis_size(axis)
    if size & (size - 1):
        return lax.psum_scatter(blocks, axis, scatter_dimension=0, tiled=True)[0]
    me = lax.axis_index(axis)
    stride = size // 2
    while stride >= 1:
        halves = blocks.reshape((2, blocks.shape[0] // 2) + blocks.shape[1:])
        bit = (me // stride) % 2
        keep = lax.dynamic_index_in_dim(halves, bit, axis=0, keepdims=False)
        send = lax.dynamic_index_in_dim(halves, 1 - bit, axis=0, keepdims=False)
        pairs = [(i, i ^ stride) for i in range(size)]
        blocks = keep + lax.ppermute(send, axis, pairs)
        stride //= 2
    return blocks[0]


def scatter_adapter_grads(joined_down, joined_up):
    members_rank = joined_down.shape[-1]
    down_cols = joined_down.shape[2]
    joined = jnp.concatenate([joined_down, joined_up], axis=2)
    dp_size, sub_size = lax.axis_size("dp"), lax.axis_size("sub")
    joined = joined.reshape((dp_size, sub_size) + joined.shape[1:])
    mine = halving_scatter(joined.swapaxes(0, 1), "sub")
    mine = halving_scatter(mine, "dp")
    mine = halving_scatter(mine, "ctx")

    def unshard(piece):
        return piece.reshape(piece.shape[0], 2, -1).transpose(1, 2, 0)

    return unshard(mine[:down_cols]), unshard(mine[down_cols:])


def on_device(hidden, queries, kv_weight, adapter_down, adapter_up, out_grad):
    rows_own = hidden[0]
    query_rows = queries[0]
    grad_rows = out_grad[0]
    length = rows_own.shape[0]
    row_shards, col_shards = lax.axis_size("ctx"), lax.axis_size(("dp", "sub"))
    rows_previous = shifted(rows_own, "ctx", 1)
    down_full, up_full = gather_adapters(adapter_down, adapter_up)
    is_first = lax.axis_index("ctx") == 0
    low_previous, low_rank, kv_both = project_rows(
        rows_previous, rows_own, kv_weight, down_full, up_full
    )
    attended, query_grad, kv_grads = attend(query_rows, kv_both, grad_rows, is_first)
    far_part = kv_grads[:, :length]
    near_part = kv_grads[:, length:]
    projected_far = jnp.einsum(
        "mrc,mkc->mrk", far_part, up_full, preferred_element_type=jnp.float32
    ).astype(jnp.bfloat16)
    projected_returned = shifted(projected_far, "ctx", -1)
    projected_near = jnp.einsum(
        "mrc,mkc->mrk", near_part, up_full, preferred_element_type=jnp.float32
    ).astype(jnp.bfloat16)
    shards = row_shards * col_shards
    rows_split = rows_own.reshape(length, row_shards, col_shards, -1)

    def split_cols(part):
        return part.reshape(part.shape[:2] + (row_shards, col_shards, -1))

    up_terms = jnp.einsum(
        "mrk,mrcij->icjmk", low_rank, split_cols(near_part), preferred_element_type=jnp.float32
    ) + jnp.einsum(
        "mrk,mrcij->icjmk", low_previous, split_cols(far_part), preferred_element_type=jnp.float32
    )
    down_terms = jnp.einsum(
        "mrk,rcij->icjmk", projected_near, rows_split, preferred_element_type=jnp.float32
    ) + jnp.einsum(
        "mrk,rcij->icjmk", projected_returned, rows_split, preferred_element_type=jnp.float32
    )
    factor = adapter_scale / (lax.axis_size("dp") * lax.axis_size("sub"))
    flat = lambda terms: (terms * factor).reshape(terms.shape[:3] + (-1,))
    down_part, up_part = scatter_adapter_grads(flat(down_terms), flat(up_terms))
    return (attended[None], query_grad[None], down_part, up_part)


def solution(mesh):
    placed = (
        P(("groups", "dp", "sub"), "ctx", None),
        P(("groups", "dp", "sub"), "ctx", None),
        P(None, "ctx", ("dp", "sub")),
        P(None, None, ("ctx", "dp", "sub")),
        P(None, None, ("ctx", "dp", "sub")),
        P(("groups", "dp", "sub"), "ctx", None),
    )
    return jax.shard_map(
        on_device,
        mesh=mesh,
        in_specs=placed,
        out_specs=(
            P(("groups", "dp", "sub"), "ctx", None),
            P(("groups", "dp", "sub"), "ctx", None),
            P("groups", None, ("ctx", "dp", "sub")),
            P("groups", None, ("ctx", "dp", "sub")),
        ),
        check_vma=False,
    )
```

```python
import jax
import jax.numpy as jnp
from jax import lax
from jax.experimental import pallas as pl
from jax.experimental.pallas import tpu as pltpu
from jax.sharding import PartitionSpec as P

HEADS = 16
KV_HEADS = 8
HEAD_DIM = 128


query_scale = 1.0 / 12.0
logit_cap = 50.0
adapter_scale = 0.5


def shifted(value, axis, by):
    length = lax.axis_size(axis)
    pairs = [(i, i + by) for i in range(length) if 0 <= i + by < length]
    return lax.ppermute(value, axis, pairs)


def attention_kernel(
    mask_ref, q_ref, do_ref, kv_ref, low_ref, up_ref,
    out_ref, dq_ref, projected_ref, up_terms_ref, projected_acc,
):
    head = pl.program_id(0)
    half = HEAD_DIM
    q = jnp.concatenate([q_ref[:, :half], q_ref[:, half:]], axis=0)
    do = jnp.concatenate([do_ref[:, :half], do_ref[:, half:]], axis=0)
    k = kv_ref[0]
    v = kv_ref[1]
    rows = q_ref.shape[0]
    visible = mask_ref[...] != 0
    contract_last = (((1,), (1,)), ((), ()))
    contract_first = (((0,), (0,)), ((), ()))
    raw_score = lax.dot_general(q, k, contract_last, preferred_element_type=jnp.float32) * query_scale
    bent_score = jnp.tanh(raw_score / logit_cap)
    expo_terms = jnp.where(visible, jnp.exp(logit_cap * bent_score), 0.0)
    denominator = jnp.sum(expo_terms, axis=-1, keepdims=True)
    prob_wide = (expo_terms / denominator).astype(jnp.bfloat16).astype(jnp.float32)
    attn_prob = prob_wide.astype(jnp.bfloat16)
    head_out = jnp.dot(attn_prob, v, preferred_element_type=jnp.float32).astype(out_ref.dtype)
    out_ref[:, :half] = head_out[:rows]
    out_ref[:, half:] = head_out[rows:]
    prob_grad = lax.dot_general(do, v, contract_last, preferred_element_type=jnp.float32)
    row_delta = jnp.sum(prob_wide * prob_grad, axis=-1, keepdims=True)
    score_wide = prob_wide * (prob_grad - row_delta) * (1.0 - bent_score * bent_score) * query_scale
    score_grad = score_wide.astype(jnp.bfloat16)
    head_qgrad = jnp.dot(score_grad, k, preferred_element_type=jnp.float32).astype(dq_ref.dtype)
    dq_ref[:, :half] = head_qgrad[:rows]
    dq_ref[:, half:] = head_qgrad[rows:]
    score_t = score_grad.astype(jnp.float32).T.astype(jnp.bfloat16)
    prob_t = prob_wide.T.astype(jnp.bfloat16)
    key_grad = jnp.dot(score_t, q, preferred_element_type=jnp.float32).astype(jnp.bfloat16)
    value_grad = jnp.dot(prob_t, do, preferred_element_type=jnp.float32).astype(jnp.bfloat16)

    @pl.when(head == 0)
    def _():
        projected_acc[...] = jnp.zeros_like(projected_acc)

    for member, grad in enumerate((key_grad, value_grad)):
        projected_acc[member] += lax.dot_general(
            grad, up_ref[member], contract_last, preferred_element_type=jnp.float32
        )
        up_terms_ref[member] = lax.dot_general(
            low_ref[member], grad, contract_first, preferred_element_type=jnp.float32
        )

    @pl.when(head == pl.num_programs(0) - 1)
    def _():
        projected_ref[...] = projected_acc[...].astype(projected_ref.dtype)


def attention_heads(mask, queries, grads, key_value, low_rows, up_full):
    rows, width = queries.shape
    members, keys, kv_width = key_value.shape
    rank = up_full.shape[1]
    heads = kv_width // HEAD_DIM
    group_cols = width // heads
    row_block = pl.BlockSpec((rows, group_cols), lambda g: (0, g))
    kv_block = pl.BlockSpec((members, keys, HEAD_DIM), lambda g: (0, 0, g))
    whole = lambda shape: pl.BlockSpec(shape, lambda g: (0,) * len(shape))
    return pl.pallas_call(
        attention_kernel,
        grid=(heads,),
        in_specs=[
            whole(mask.shape),
            row_block,
            row_block,
            kv_block,
            whole(low_rows.shape),
            pl.BlockSpec((members, rank, HEAD_DIM), lambda g: (0, 0, g)),
        ],
        out_specs=[
            row_block,
            row_block,
            whole((members, keys, rank)),
            pl.BlockSpec((members, rank, HEAD_DIM), lambda g: (0, 0, g)),
        ],
        out_shape=[
            jax.ShapeDtypeStruct((rows, width), jnp.bfloat16),
            jax.ShapeDtypeStruct((rows, width), jnp.bfloat16),
            jax.ShapeDtypeStruct((members, keys, rank), jnp.bfloat16),
            jax.ShapeDtypeStruct((members, rank, kv_width), jnp.float32),
        ],
        scratch_shapes=[pltpu.VMEM((members, keys, rank), jnp.float32)],
    )(mask, queries, grads, key_value, low_rows, up_full)


def attend(query_rows, key_value, grad_rows, is_first, low_rows, up_full):
    length = query_rows.shape[0]
    group_size = HEADS // KV_HEADS
    query_pos = lax.broadcasted_iota(jnp.int32, (group_size * length, 2 * length), 0) % length
    key_pos = lax.broadcasted_iota(jnp.int32, (group_size * length, 2 * length), 1)
    visible = (
        (key_pos > query_pos)
        & (key_pos <= query_pos + length)
        & (jnp.logical_not(is_first) | (key_pos >= length))
    )
    return attention_heads(visible.astype(jnp.int32), query_rows, grad_rows, key_value, low_rows, up_full)


def projection_kernel(rows_ref, weight_ref, low_ref, up_ref, out_ref):
    row_shards = weight_ref.shape[0]
    base = jnp.dot(low_ref[0], up_ref[0], preferred_element_type=jnp.float32) * adapter_scale
    for c in range(row_shards):
        base = base + jnp.dot(rows_ref[c], weight_ref[c, 0, 0], preferred_element_type=jnp.float32)
    out_ref[0] = base.astype(out_ref.dtype)


def project_pair(rows_split, gathered, low_rows, up_full):
    row_shards, col_shards, members, depth, cols = gathered.shape
    rows = rows_split.shape[1]
    rank = up_full.shape[1]
    return pl.pallas_call(
        projection_kernel,
        grid=(members, col_shards),
        in_specs=[
            pl.BlockSpec((row_shards, rows, depth), lambda m, i: (0, 0, 0)),
            pl.BlockSpec((row_shards, 1, 1, depth, cols), lambda m, i: (0, i, m, 0, 0)),
            pl.BlockSpec((1, rows, rank), lambda m, i: (m, 0, 0)),
            pl.BlockSpec((1, rank, cols), lambda m, i: (m, 0, i)),
        ],
        out_specs=pl.BlockSpec((1, rows, cols), lambda m, i: (m, 0, i)),
        out_shape=jax.ShapeDtypeStruct((members, rows, col_shards * cols), jnp.bfloat16),
    )(rows_split, gathered, low_rows, up_full)


def project_rows(rows_previous, rows_own, kv_weight, down_full, up_full):
    def low_of(rows):
        return jnp.einsum(
            "rd,mkd->mrk", rows, down_full, preferred_element_type=jnp.float32
        ).astype(jnp.bfloat16)

    low_previous, low_rank = low_of(rows_previous), low_of(rows_own)
    row_shards, col_shards = lax.axis_size("ctx"), lax.axis_size(("dp", "sub"))
    rows_both = jnp.concatenate([rows_previous, rows_own], axis=0)
    rows_split = rows_both.reshape(rows_both.shape[0], row_shards, -1).swapaxes(0, 1)
    gathered = lax.all_gather(kv_weight, ("ctx", "dp", "sub"), axis=0, tiled=False)
    gathered = gathered.reshape((row_shards, col_shards) + kv_weight.shape)
    low_rows = jnp.concatenate([low_previous, low_rank], axis=1)
    key_value = project_pair(rows_split, gathered, low_rows, up_full)
    return low_rows, key_value


def gather_adapters(adapter_down, adapter_up):
    axes = ("ctx", "dp", "sub")
    down_cols = adapter_down.shape[2]
    joined = jnp.concatenate([adapter_down, adapter_up], axis=2)
    gathered = lax.all_gather(joined, axes, axis=0, tiled=False)
    shards = gathered.shape[0]

    def unshard(piece):
        return piece.transpose(1, 2, 0, 3).reshape(2, piece.shape[2], shards * piece.shape[3])

    return unshard(gathered[..., :down_cols]), unshard(gathered[..., down_cols:])


def halving_scatter(blocks, axis):
    size = lax.axis_size(axis)
    if size & (size - 1):
        return lax.psum_scatter(blocks, axis, scatter_dimension=0, tiled=True)[0]
    me = lax.axis_index(axis)
    stride = size // 2
    while stride >= 1:
        halves = blocks.reshape((2, blocks.shape[0] // 2) + blocks.shape[1:])
        bit = (me // stride) % 2
        keep = lax.dynamic_index_in_dim(halves, bit, axis=0, keepdims=False)
        send = lax.dynamic_index_in_dim(halves, 1 - bit, axis=0, keepdims=False)
        pairs = [(i, i ^ stride) for i in range(size)]
        blocks = keep + lax.ppermute(send, axis, pairs)
        stride //= 2
    return blocks[0]


def scatter_adapter_grads(joined_down, joined_up):
    members_rank = joined_down.shape[-1]
    down_cols = joined_down.shape[2]
    joined = jnp.concatenate([joined_down, joined_up], axis=2)
    dp_size, sub_size = lax.axis_size("dp"), lax.axis_size("sub")
    joined = joined.reshape((dp_size, sub_size) + joined.shape[1:])
    mine = halving_scatter(joined.swapaxes(0, 1), "sub")
    mine = halving_scatter(mine, "dp")
    mine = halving_scatter(mine, "ctx")

    def unshard(piece):
        return piece.reshape(piece.shape[0], 2, -1).transpose(1, 2, 0)

    return unshard(mine[:down_cols]), unshard(mine[down_cols:])


def on_device(hidden, queries, kv_weight, adapter_down, adapter_up, out_grad):
    rows_own = hidden[0]
    query_rows = queries[0]
    grad_rows = out_grad[0]
    length = rows_own.shape[0]
    row_shards, col_shards = lax.axis_size("ctx"), lax.axis_size(("dp", "sub"))
    rows_previous = shifted(rows_own, "ctx", 1)
    down_full, up_full = gather_adapters(adapter_down, adapter_up)
    is_first = lax.axis_index("ctx") == 0
    low_rows, kv_both = project_rows(rows_previous, rows_own, kv_weight, down_full, up_full)
    attended, query_grad, projected, up_terms = attend(
        query_rows, kv_both, grad_rows, is_first, low_rows, up_full
    )
    projected_returned = shifted(projected[:, :length], "ctx", -1)
    projected_near = projected[:, length:]
    rows_split = rows_own.reshape(length, row_shards, col_shards, -1)
    up_terms = up_terms.reshape(up_terms.shape[:2] + (row_shards, col_shards, -1)).transpose(3, 2, 4, 0, 1)
    down_terms = jnp.einsum(
        "mrk,rcij->icjmk", projected_near, rows_split, preferred_element_type=jnp.float32
    ) + jnp.einsum(
        "mrk,rcij->icjmk", projected_returned, rows_split, preferred_element_type=jnp.float32
    )
    factor = adapter_scale / (lax.axis_size("dp") * lax.axis_size("sub"))
    flat = lambda terms: (terms * factor).reshape(terms.shape[:3] + (-1,))
    down_part, up_part = scatter_adapter_grads(flat(down_terms), flat(up_terms))
    return (attended[None], query_grad[None], down_part, up_part)


def solution(mesh):
    placed = (
        P(("groups", "dp", "sub"), "ctx", None),
        P(("groups", "dp", "sub"), "ctx", None),
        P(None, "ctx", ("dp", "sub")),
        P(None, None, ("ctx", "dp", "sub")),
        P(None, None, ("ctx", "dp", "sub")),
        P(("groups", "dp", "sub"), "ctx", None),
    )
    return jax.shard_map(
        on_device,
        mesh=mesh,
        in_specs=placed,
        out_specs=(
            P(("groups", "dp", "sub"), "ctx", None),
            P(("groups", "dp", "sub"), "ctx", None),
            P("groups", None, ("ctx", "dp", "sub")),
            P("groups", None, ("ctx", "dp", "sub")),
        ),
        check_vma=False,
    )
```

```python
import jax
import jax.numpy as jnp
from jax import lax
from jax.experimental import pallas as pl
from jax.experimental.pallas import tpu as pltpu
from jax.sharding import PartitionSpec as P

HEADS = 16
KV_HEADS = 8
HEAD_DIM = 128


query_scale = 1.0 / 12.0
logit_cap = 50.0
adapter_scale = 0.5


def shifted(value, axis, by):
    length = lax.axis_size(axis)
    pairs = [(i, i + by) for i in range(length) if 0 <= i + by < length]
    return lax.ppermute(value, axis, pairs)


def attention_kernel(
    mask_ref, q_ref, do_ref, kv_ref, low_ref, up_ref,
    out_ref, dq_ref, projected_ref, up_terms_ref, projected_acc,
):
    head = pl.program_id(0)
    half = HEAD_DIM
    q = jnp.concatenate([q_ref[:, :half], q_ref[:, half:]], axis=0)
    do = jnp.concatenate([do_ref[:, :half], do_ref[:, half:]], axis=0)
    k = kv_ref[0]
    v = kv_ref[1]
    rows = q_ref.shape[0]
    visible = mask_ref[...] != 0
    contract_last = (((1,), (1,)), ((), ()))
    contract_first = (((0,), (0,)), ((), ()))
    raw_score = lax.dot_general(q, k, contract_last, preferred_element_type=jnp.float32) * query_scale
    bent_score = jnp.tanh(raw_score / logit_cap)
    expo_terms = jnp.where(visible, jnp.exp(logit_cap * bent_score), 0.0)
    denominator = jnp.sum(expo_terms, axis=-1, keepdims=True)
    prob_wide = (expo_terms / denominator).astype(jnp.bfloat16).astype(jnp.float32)
    attn_prob = prob_wide.astype(jnp.bfloat16)
    head_out = jnp.dot(attn_prob, v, preferred_element_type=jnp.float32).astype(out_ref.dtype)
    out_ref[:, :half] = head_out[:rows]
    out_ref[:, half:] = head_out[rows:]
    prob_grad = lax.dot_general(do, v, contract_last, preferred_element_type=jnp.float32)
    row_delta = jnp.sum(prob_wide * prob_grad, axis=-1, keepdims=True)
    score_wide = prob_wide * (prob_grad - row_delta) * (1.0 - bent_score * bent_score) * query_scale
    score_grad = score_wide.astype(jnp.bfloat16)
    head_qgrad = jnp.dot(score_grad, k, preferred_element_type=jnp.float32).astype(dq_ref.dtype)
    dq_ref[:, :half] = head_qgrad[:rows]
    dq_ref[:, half:] = head_qgrad[rows:]
    score_t = score_grad.astype(jnp.float32).T.astype(jnp.bfloat16)
    prob_t = prob_wide.T.astype(jnp.bfloat16)
    key_grad = jnp.dot(score_t, q, preferred_element_type=jnp.float32).astype(jnp.bfloat16)
    value_grad = jnp.dot(prob_t, do, preferred_element_type=jnp.float32).astype(jnp.bfloat16)

    @pl.when(head == 0)
    def _():
        projected_acc[...] = jnp.zeros_like(projected_acc)

    for member, grad in enumerate((key_grad, value_grad)):
        projected_acc[member] += lax.dot_general(
            grad, up_ref[member], contract_last, preferred_element_type=jnp.float32
        )
        up_terms_ref[member] = lax.dot_general(
            low_ref[member], grad, contract_first, preferred_element_type=jnp.float32
        )

    @pl.when(head == pl.num_programs(0) - 1)
    def _():
        projected_ref[...] = projected_acc[...].astype(projected_ref.dtype)


def attention_heads(mask, queries, grads, key_value, low_rows, up_full):
    rows, width = queries.shape
    members, keys, kv_width = key_value.shape
    rank = up_full.shape[1]
    heads = kv_width // HEAD_DIM
    group_cols = width // heads
    row_block = pl.BlockSpec((rows, group_cols), lambda g: (0, g))
    kv_block = pl.BlockSpec((members, keys, HEAD_DIM), lambda g: (0, 0, g))
    whole = lambda shape: pl.BlockSpec(shape, lambda g: (0,) * len(shape))
    return pl.pallas_call(
        attention_kernel,
        grid=(heads,),
        in_specs=[
            whole(mask.shape),
            row_block,
            row_block,
            kv_block,
            whole(low_rows.shape),
            pl.BlockSpec((members, rank, HEAD_DIM), lambda g: (0, 0, g)),
        ],
        out_specs=[
            row_block,
            row_block,
            whole((members, keys, rank)),
            pl.BlockSpec((members, rank, HEAD_DIM), lambda g: (0, 0, g)),
        ],
        out_shape=[
            jax.ShapeDtypeStruct((rows, width), jnp.bfloat16),
            jax.ShapeDtypeStruct((rows, width), jnp.bfloat16),
            jax.ShapeDtypeStruct((members, keys, rank), jnp.bfloat16),
            jax.ShapeDtypeStruct((members, rank, kv_width), jnp.float32),
        ],
        scratch_shapes=[pltpu.VMEM((members, keys, rank), jnp.float32)],
    )(mask, queries, grads, key_value, low_rows, up_full)


def attend(query_rows, key_value, grad_rows, is_first, low_rows, up_full):
    length = query_rows.shape[0]
    group_size = HEADS // KV_HEADS
    query_pos = lax.broadcasted_iota(jnp.int32, (group_size * length, 2 * length), 0) % length
    key_pos = lax.broadcasted_iota(jnp.int32, (group_size * length, 2 * length), 1)
    visible = (
        (key_pos > query_pos)
        & (key_pos <= query_pos + length)
        & (jnp.logical_not(is_first) | (key_pos >= length))
    )
    return attention_heads(visible.astype(jnp.int32), query_rows, grad_rows, key_value, low_rows, up_full)


def projection_kernel(rows_ref, weight_ref, low_ref, up_ref, out_ref):
    row_shards = weight_ref.shape[0]
    base = jnp.dot(low_ref[0], up_ref[0], preferred_element_type=jnp.float32) * adapter_scale
    for c in range(row_shards):
        base = base + jnp.dot(rows_ref[c], weight_ref[c, 0, 0], preferred_element_type=jnp.float32)
    out_ref[0] = base.astype(out_ref.dtype)


def project_pair(rows_split, gathered, low_rows, up_full):
    row_shards, col_shards, members, depth, cols = gathered.shape
    rows = rows_split.shape[1]
    rank = up_full.shape[1]
    return pl.pallas_call(
        projection_kernel,
        grid=(members, col_shards),
        in_specs=[
            pl.BlockSpec((row_shards, rows, depth), lambda m, i: (0, 0, 0)),
            pl.BlockSpec((row_shards, 1, 1, depth, cols), lambda m, i: (0, i, m, 0, 0)),
            pl.BlockSpec((1, rows, rank), lambda m, i: (m, 0, 0)),
            pl.BlockSpec((1, rank, cols), lambda m, i: (m, 0, i)),
        ],
        out_specs=pl.BlockSpec((1, rows, cols), lambda m, i: (m, 0, i)),
        out_shape=jax.ShapeDtypeStruct((members, rows, col_shards * cols), jnp.bfloat16),
    )(rows_split, gathered, low_rows, up_full)


def project_rows(rows_previous, rows_own, kv_weight, down_full, up_full):
    def low_of(rows):
        return jnp.einsum(
            "rd,mkd->mrk", rows, down_full, preferred_element_type=jnp.float32
        ).astype(jnp.bfloat16)

    low_previous, low_rank = low_of(rows_previous), low_of(rows_own)
    row_shards, col_shards = lax.axis_size("ctx"), lax.axis_size(("dp", "sub"))
    rows_both = jnp.concatenate([rows_previous, rows_own], axis=0)
    rows_split = rows_both.reshape(rows_both.shape[0], row_shards, -1).swapaxes(0, 1)
    gathered = lax.all_gather(kv_weight, ("ctx", "dp", "sub"), axis=0, tiled=False)
    gathered = gathered.reshape((row_shards, col_shards) + kv_weight.shape)
    low_rows = jnp.concatenate([low_previous, low_rank], axis=1)
    key_value = project_pair(rows_split, gathered, low_rows, up_full)
    return rows_both, low_rows, key_value


def gather_adapters(adapter_down, adapter_up):
    axes = ("ctx", "dp", "sub")
    down_cols = adapter_down.shape[2]
    joined = jnp.concatenate([adapter_down, adapter_up], axis=2)
    gathered = lax.all_gather(joined, axes, axis=0, tiled=False)
    shards = gathered.shape[0]

    def unshard(piece):
        return piece.transpose(1, 2, 0, 3).reshape(2, piece.shape[2], shards * piece.shape[3])

    return unshard(gathered[..., :down_cols]), unshard(gathered[..., down_cols:])


def exchange_scatter(blocks, axis):
    size = lax.axis_size(axis)
    me = lax.axis_index(axis)
    total = lax.dynamic_index_in_dim(blocks, me, axis=0, keepdims=False)
    for shift in range(1, size):
        send = lax.dynamic_index_in_dim(blocks, (me + shift) % size, axis=0, keepdims=False)
        total = total + lax.ppermute(send, axis, [(i, (i + shift) % size) for i in range(size)])
    return total


def halving_scatter(blocks, axis):
    size = lax.axis_size(axis)
    if size <= 4:
        return exchange_scatter(blocks, axis)
    if size & (size - 1):
        return lax.psum_scatter(blocks, axis, scatter_dimension=0, tiled=True)[0]
    me = lax.axis_index(axis)
    stride = size // 2
    while stride >= 1:
        halves = blocks.reshape((2, blocks.shape[0] // 2) + blocks.shape[1:])
        bit = (me // stride) % 2
        keep = lax.dynamic_index_in_dim(halves, bit, axis=0, keepdims=False)
        send = lax.dynamic_index_in_dim(halves, 1 - bit, axis=0, keepdims=False)
        pairs = [(i, i ^ stride) for i in range(size)]
        blocks = keep + lax.ppermute(send, axis, pairs)
        stride //= 2
    return blocks[0]


def scatter_adapter_grads(joined_down, joined_up):
    members_rank = joined_down.shape[-1]
    down_cols = joined_down.shape[2]
    joined = jnp.concatenate([joined_down, joined_up], axis=2)
    mine = halving_scatter(joined, ("dp", "sub"))
    mine = halving_scatter(mine, "ctx")

    def unshard(piece):
        return piece.reshape(piece.shape[0], 2, -1).transpose(1, 2, 0)

    return unshard(mine[:down_cols]), unshard(mine[down_cols:])


def on_device(hidden, queries, kv_weight, adapter_down, adapter_up, out_grad):
    rows_own = hidden[0]
    query_rows = queries[0]
    grad_rows = out_grad[0]
    length = rows_own.shape[0]
    row_shards, col_shards = lax.axis_size("ctx"), lax.axis_size(("dp", "sub"))
    rows_previous = shifted(rows_own, "ctx", 1)
    down_full, up_full = gather_adapters(adapter_down, adapter_up)
    is_first = lax.axis_index("ctx") == 0
    rows_both, low_rows, kv_both = project_rows(
        rows_previous, rows_own, kv_weight, down_full, up_full
    )
    attended, query_grad, projected, up_terms = attend(
        query_rows, kv_both, grad_rows, is_first, low_rows, up_full
    )
    up_terms = up_terms.reshape(up_terms.shape[:2] + (row_shards, col_shards, -1)).transpose(3, 2, 4, 0, 1)
    down_terms = jnp.einsum(
        "mrk,rcij->icjmk",
        projected,
        rows_both.reshape(rows_both.shape[0], row_shards, col_shards, -1),
        preferred_element_type=jnp.float32,
    )
    factor = adapter_scale / (lax.axis_size("dp") * lax.axis_size("sub"))
    flat = lambda terms: (terms * factor).reshape(terms.shape[:3] + (-1,))
    down_part, up_part = scatter_adapter_grads(flat(down_terms), flat(up_terms))
    return (attended[None], query_grad[None], down_part, up_part)


def solution(mesh):
    placed = (
        P(("groups", "dp", "sub"), "ctx", None),
        P(("groups", "dp", "sub"), "ctx", None),
        P(None, "ctx", ("dp", "sub")),
        P(None, None, ("ctx", "dp", "sub")),
        P(None, None, ("ctx", "dp", "sub")),
        P(("groups", "dp", "sub"), "ctx", None),
    )
    return jax.shard_map(
        on_device,
        mesh=mesh,
        in_specs=placed,
        out_specs=(
            P(("groups", "dp", "sub"), "ctx", None),
            P(("groups", "dp", "sub"), "ctx", None),
            P("groups", None, ("ctx", "dp", "sub")),
            P("groups", None, ("ctx", "dp", "sub")),
        ),
        check_vma=False,
    )
```

```python
import jax
import jax.numpy as jnp
from jax import lax
from jax.experimental import pallas as pl
from jax.experimental.pallas import tpu as pltpu
from jax.sharding import PartitionSpec as P

HEADS = 16
KV_HEADS = 8
HEAD_DIM = 128


query_scale = 1.0 / 12.0
logit_cap = 50.0
adapter_scale = 0.5


def shifted(value, axis, by):
    length = lax.axis_size(axis)
    pairs = [(i, i + by) for i in range(length) if 0 <= i + by < length]
    return lax.ppermute(value, axis, pairs)


def attention_kernel(
    mask_ref, q_ref, do_ref, kv_ref, low_ref, up_ref,
    out_ref, dq_ref, projected_ref, up_terms_ref, projected_acc,
):
    head = pl.program_id(0)
    half = HEAD_DIM
    q = jnp.concatenate([q_ref[:, :half], q_ref[:, half:]], axis=0)
    do = jnp.concatenate([do_ref[:, :half], do_ref[:, half:]], axis=0)
    k = kv_ref[0]
    v = kv_ref[1]
    rows = q_ref.shape[0]
    visible = mask_ref[...] != 0
    contract_last = (((1,), (1,)), ((), ()))
    contract_first = (((0,), (0,)), ((), ()))
    raw_score = lax.dot_general(q, k, contract_last, preferred_element_type=jnp.float32) * query_scale
    bent_score = jnp.tanh(raw_score / logit_cap)
    expo_terms = jnp.where(visible, jnp.exp(logit_cap * bent_score), 0.0)
    denominator = jnp.sum(expo_terms, axis=-1, keepdims=True)
    prob_wide = (expo_terms * (1.0 / denominator)).astype(jnp.bfloat16).astype(jnp.float32)
    attn_prob = prob_wide.astype(jnp.bfloat16)
    head_out = jnp.dot(attn_prob, v, preferred_element_type=jnp.float32).astype(out_ref.dtype)
    out_ref[:, :half] = head_out[:rows]
    out_ref[:, half:] = head_out[rows:]
    prob_grad = lax.dot_general(do, v, contract_last, preferred_element_type=jnp.float32)
    row_delta = jnp.sum(prob_wide * prob_grad, axis=-1, keepdims=True)
    score_wide = prob_wide * (prob_grad - row_delta) * (1.0 - bent_score * bent_score) * query_scale
    score_grad = score_wide.astype(jnp.bfloat16)
    head_qgrad = jnp.dot(score_grad, k, preferred_element_type=jnp.float32).astype(dq_ref.dtype)
    dq_ref[:, :half] = head_qgrad[:rows]
    dq_ref[:, half:] = head_qgrad[rows:]
    key_grad = lax.dot_general(
        score_grad, q, contract_first, preferred_element_type=jnp.float32
    ).astype(jnp.bfloat16)
    value_grad = lax.dot_general(
        attn_prob, do, contract_first, preferred_element_type=jnp.float32
    ).astype(jnp.bfloat16)

    @pl.when(head == 0)
    def _():
        projected_acc[...] = jnp.zeros_like(projected_acc)

    for member, grad in enumerate((key_grad, value_grad)):
        projected_acc[member] += lax.dot_general(
            grad, up_ref[member], contract_last, preferred_element_type=jnp.float32
        )
        up_terms_ref[member] = lax.dot_general(
            low_ref[member], grad, contract_first, preferred_element_type=jnp.float32
        )

    @pl.when(head == pl.num_programs(0) - 1)
    def _():
        projected_ref[...] = projected_acc[...].astype(projected_ref.dtype)


def attention_heads(mask, queries, grads, key_value, low_rows, up_full):
    rows, width = queries.shape
    members, keys, kv_width = key_value.shape
    rank = up_full.shape[1]
    heads = kv_width // HEAD_DIM
    group_cols = width // heads
    row_block = pl.BlockSpec((rows, group_cols), lambda g: (0, g))
    kv_block = pl.BlockSpec((members, keys, HEAD_DIM), lambda g: (0, 0, g))
    whole = lambda shape: pl.BlockSpec(shape, lambda g: (0,) * len(shape))
    return pl.pallas_call(
        attention_kernel,
        grid=(heads,),
        in_specs=[
            whole(mask.shape),
            row_block,
            row_block,
            kv_block,
            whole(low_rows.shape),
            pl.BlockSpec((members, rank, HEAD_DIM), lambda g: (0, 0, g)),
        ],
        out_specs=[
            row_block,
            row_block,
            whole((members, keys, rank)),
            pl.BlockSpec((members, rank, HEAD_DIM), lambda g: (0, 0, g)),
        ],
        out_shape=[
            jax.ShapeDtypeStruct((rows, width), jnp.bfloat16),
            jax.ShapeDtypeStruct((rows, width), jnp.bfloat16),
            jax.ShapeDtypeStruct((members, keys, rank), jnp.bfloat16),
            jax.ShapeDtypeStruct((members, rank, kv_width), jnp.float32),
        ],
        scratch_shapes=[pltpu.VMEM((members, keys, rank), jnp.float32)],
    )(mask, queries, grads, key_value, low_rows, up_full)


def attend(query_rows, key_value, grad_rows, is_first, low_rows, up_full):
    length = query_rows.shape[0]
    group_size = HEADS // KV_HEADS
    query_pos = lax.broadcasted_iota(jnp.int32, (group_size * length, 2 * length), 0) % length
    key_pos = lax.broadcasted_iota(jnp.int32, (group_size * length, 2 * length), 1)
    visible = (
        (key_pos > query_pos)
        & (key_pos <= query_pos + length)
        & (jnp.logical_not(is_first) | (key_pos >= length))
    )
    return attention_heads(visible.astype(jnp.int32), query_rows, grad_rows, key_value, low_rows, up_full)


def projection_kernel(rows_ref, weight_ref, low_ref, up_ref, out_ref):
    row_shards = weight_ref.shape[0]
    base = jnp.dot(low_ref[0], up_ref[0], preferred_element_type=jnp.float32) * adapter_scale
    for c in range(row_shards):
        base = base + jnp.dot(rows_ref[c], weight_ref[c, 0, 0], preferred_element_type=jnp.float32)
    out_ref[0] = base.astype(out_ref.dtype)


def project_pair(rows_split, gathered, low_rows, up_full):
    row_shards, col_shards, members, depth, cols = gathered.shape
    rows = rows_split.shape[1]
    rank = up_full.shape[1]
    return pl.pallas_call(
        projection_kernel,
        grid=(members, col_shards),
        in_specs=[
            pl.BlockSpec((row_shards, rows, depth), lambda m, i: (0, 0, 0)),
            pl.BlockSpec((row_shards, 1, 1, depth, cols), lambda m, i: (0, i, m, 0, 0)),
            pl.BlockSpec((1, rows, rank), lambda m, i: (m, 0, 0)),
            pl.BlockSpec((1, rank, cols), lambda m, i: (m, 0, i)),
        ],
        out_specs=pl.BlockSpec((1, rows, cols), lambda m, i: (m, 0, i)),
        out_shape=jax.ShapeDtypeStruct((members, rows, col_shards * cols), jnp.bfloat16),
    )(rows_split, gathered, low_rows, up_full)


def project_rows(rows_previous, rows_own, kv_weight, down_full, up_full):
    def low_of(rows):
        return jnp.einsum(
            "rd,mkd->mrk", rows, down_full, preferred_element_type=jnp.float32
        ).astype(jnp.bfloat16)

    low_previous, low_rank = low_of(rows_previous), low_of(rows_own)
    row_shards, col_shards = lax.axis_size("ctx"), lax.axis_size(("dp", "sub"))
    rows_both = jnp.concatenate([rows_previous, rows_own], axis=0)
    rows_split = rows_both.reshape(rows_both.shape[0], row_shards, -1).swapaxes(0, 1)
    gathered = lax.all_gather(kv_weight, ("ctx", "dp", "sub"), axis=0, tiled=False)
    gathered = gathered.reshape((row_shards, col_shards) + kv_weight.shape)
    low_rows = jnp.concatenate([low_previous, low_rank], axis=1)
    key_value = project_pair(rows_split, gathered, low_rows, up_full)
    return rows_both, low_rows, key_value


def gather_adapters(adapter_down, adapter_up):
    axes = ("ctx", "dp", "sub")
    down_cols = adapter_down.shape[2]
    joined = jnp.concatenate([adapter_down, adapter_up], axis=2)
    gathered = lax.all_gather(joined, axes, axis=0, tiled=False)
    shards = gathered.shape[0]

    def unshard(piece):
        return piece.transpose(1, 2, 0, 3).reshape(2, piece.shape[2], shards * piece.shape[3])

    return unshard(gathered[..., :down_cols]), unshard(gathered[..., down_cols:])


def exchange_scatter(blocks, axis):
    size = lax.axis_size(axis)
    me = lax.axis_index(axis)
    total = lax.dynamic_index_in_dim(blocks, me, axis=0, keepdims=False)
    for shift in range(1, size):
        send = lax.dynamic_index_in_dim(blocks, (me + shift) % size, axis=0, keepdims=False)
        total = total + lax.ppermute(send, axis, [(i, (i + shift) % size) for i in range(size)])
    return total


def halving_scatter(blocks, axis):
    size = lax.axis_size(axis)
    if size <= 4:
        return exchange_scatter(blocks, axis)
    if size & (size - 1):
        return lax.psum_scatter(blocks, axis, scatter_dimension=0, tiled=True)[0]
    me = lax.axis_index(axis)
    stride = size // 2
    while stride >= 1:
        halves = blocks.reshape((2, blocks.shape[0] // 2) + blocks.shape[1:])
        bit = (me // stride) % 2
        keep = lax.dynamic_index_in_dim(halves, bit, axis=0, keepdims=False)
        send = lax.dynamic_index_in_dim(halves, 1 - bit, axis=0, keepdims=False)
        pairs = [(i, i ^ stride) for i in range(size)]
        blocks = keep + lax.ppermute(send, axis, pairs)
        stride //= 2
    return blocks[0]


def scatter_adapter_grads(joined_down, joined_up):
    members_rank = joined_down.shape[-1]
    down_cols = joined_down.shape[2]
    joined = jnp.concatenate([joined_down, joined_up], axis=2)
    mine = halving_scatter(joined, ("dp", "sub"))
    mine = halving_scatter(mine, "ctx")

    def unshard(piece):
        return piece.reshape(piece.shape[0], 2, -1).transpose(1, 2, 0)

    return unshard(mine[:down_cols]), unshard(mine[down_cols:])


def on_device(hidden, queries, kv_weight, adapter_down, adapter_up, out_grad):
    rows_own = hidden[0]
    query_rows = queries[0]
    grad_rows = out_grad[0]
    length = rows_own.shape[0]
    row_shards, col_shards = lax.axis_size("ctx"), lax.axis_size(("dp", "sub"))
    rows_previous = shifted(rows_own, "ctx", 1)
    down_full, up_full = gather_adapters(adapter_down, adapter_up)
    is_first = lax.axis_index("ctx") == 0
    rows_both, low_rows, kv_both = project_rows(
        rows_previous, rows_own, kv_weight, down_full, up_full
    )
    attended, query_grad, projected, up_terms = attend(
        query_rows, kv_both, grad_rows, is_first, low_rows, up_full
    )
    up_terms = up_terms.reshape(up_terms.shape[:2] + (row_shards, col_shards, -1)).transpose(3, 2, 4, 0, 1)
    down_terms = jnp.einsum(
        "mrk,rcij->icjmk",
        projected,
        rows_both.reshape(rows_both.shape[0], row_shards, col_shards, -1),
        preferred_element_type=jnp.float32,
    )
    factor = adapter_scale / (lax.axis_size("dp") * lax.axis_size("sub"))
    flat = lambda terms: (terms * factor).reshape(terms.shape[:3] + (-1,))
    down_part, up_part = scatter_adapter_grads(flat(down_terms), flat(up_terms))
    return (attended[None], query_grad[None], down_part, up_part)


def solution(mesh):
    placed = (
        P(("groups", "dp", "sub"), "ctx", None),
        P(("groups", "dp", "sub"), "ctx", None),
        P(None, "ctx", ("dp", "sub")),
        P(None, None, ("ctx", "dp", "sub")),
        P(None, None, ("ctx", "dp", "sub")),
        P(("groups", "dp", "sub"), "ctx", None),
    )
    return jax.shard_map(
        on_device,
        mesh=mesh,
        in_specs=placed,
        out_specs=(
            P(("groups", "dp", "sub"), "ctx", None),
            P(("groups", "dp", "sub"), "ctx", None),
            P("groups", None, ("ctx", "dp", "sub")),
            P("groups", None, ("ctx", "dp", "sub")),
        ),
        check_vma=False,
    )
```

```python
import jax
import jax.numpy as jnp
from jax import lax
from jax.experimental import pallas as pl
from jax.experimental.pallas import tpu as pltpu
from jax.sharding import PartitionSpec as P

HEADS = 16
KV_HEADS = 8
HEAD_DIM = 128


query_scale = 1.0 / 12.0
logit_cap = 50.0
adapter_scale = 0.5


def shifted(value, axis, by):
    length = lax.axis_size(axis)
    pairs = [(i, i + by) for i in range(length) if 0 <= i + by < length]
    return lax.ppermute(value, axis, pairs)


def attention_kernel(
    mask_ref, q_ref, do_ref, kv_ref, low_ref, up_ref,
    out_ref, dq_ref, projected_ref, up_terms_ref, projected_acc,
):
    head = pl.program_id(0)
    half = HEAD_DIM
    q = jnp.concatenate([q_ref[:, :half], q_ref[:, half:]], axis=0)
    do = jnp.concatenate([do_ref[:, :half], do_ref[:, half:]], axis=0)
    k = kv_ref[0]
    v = kv_ref[1]
    rows = q_ref.shape[0]
    visible = mask_ref[...] != 0
    contract_last = (((1,), (1,)), ((), ()))
    contract_first = (((0,), (0,)), ((), ()))
    raw_score = lax.dot_general(q, k, contract_last, preferred_element_type=jnp.float32) * query_scale
    bent_score = jnp.tanh(raw_score / logit_cap)
    expo_terms = jnp.where(visible, jnp.exp(logit_cap * bent_score), 0.0)
    denominator = jnp.sum(expo_terms, axis=-1, keepdims=True)
    prob_wide = (expo_terms * (1.0 / denominator)).astype(jnp.bfloat16).astype(jnp.float32)
    attn_prob = prob_wide.astype(jnp.bfloat16)
    head_out = jnp.dot(attn_prob, v, preferred_element_type=jnp.float32).astype(out_ref.dtype)
    out_ref[:, :half] = head_out[:rows]
    out_ref[:, half:] = head_out[rows:]
    prob_grad = lax.dot_general(do, v, contract_last, preferred_element_type=jnp.float32)
    row_delta = jnp.sum(prob_wide * prob_grad, axis=-1, keepdims=True)
    score_wide = prob_wide * (prob_grad - row_delta) * (1.0 - bent_score * bent_score) * query_scale
    score_grad = score_wide.astype(jnp.bfloat16)
    head_qgrad = jnp.dot(score_grad, k, preferred_element_type=jnp.float32).astype(dq_ref.dtype)
    dq_ref[:, :half] = head_qgrad[:rows]
    dq_ref[:, half:] = head_qgrad[rows:]
    key_grad = lax.dot_general(
        score_grad, q, contract_first, preferred_element_type=jnp.float32
    ).astype(jnp.bfloat16)
    value_grad = lax.dot_general(
        attn_prob, do, contract_first, preferred_element_type=jnp.float32
    ).astype(jnp.bfloat16)

    @pl.when(head == 0)
    def _():
        projected_acc[...] = jnp.zeros_like(projected_acc)

    for member, grad in enumerate((key_grad, value_grad)):
        projected_acc[member] += lax.dot_general(
            grad, up_ref[member], contract_last, preferred_element_type=jnp.float32
        )
        up_terms_ref[member] = lax.dot_general(
            low_ref[member], grad, contract_first, preferred_element_type=jnp.float32
        )

    @pl.when(head == pl.num_programs(0) - 1)
    def _():
        projected_ref[...] = projected_acc[...].astype(projected_ref.dtype)


def attention_heads(mask, queries, grads, key_value, low_rows, up_full):
    rows, width = queries.shape
    members, keys, kv_width = key_value.shape
    rank = up_full.shape[1]
    heads = kv_width // HEAD_DIM
    group_cols = width // heads
    row_block = pl.BlockSpec((rows, group_cols), lambda g: (0, g))
    kv_block = pl.BlockSpec((members, keys, HEAD_DIM), lambda g: (0, 0, g))
    whole = lambda shape: pl.BlockSpec(shape, lambda g: (0,) * len(shape))
    return pl.pallas_call(
        attention_kernel,
        grid=(heads,),
        in_specs=[
            whole(mask.shape),
            row_block,
            row_block,
            kv_block,
            whole(low_rows.shape),
            pl.BlockSpec((members, rank, HEAD_DIM), lambda g: (0, 0, g)),
        ],
        out_specs=[
            row_block,
            row_block,
            whole((members, keys, rank)),
            pl.BlockSpec((members, rank, HEAD_DIM), lambda g: (0, 0, g)),
        ],
        out_shape=[
            jax.ShapeDtypeStruct((rows, width), jnp.bfloat16),
            jax.ShapeDtypeStruct((rows, width), jnp.bfloat16),
            jax.ShapeDtypeStruct((members, keys, rank), jnp.bfloat16),
            jax.ShapeDtypeStruct((members, rank, kv_width), jnp.float32),
        ],
        scratch_shapes=[pltpu.VMEM((members, keys, rank), jnp.float32)],
    )(mask, queries, grads, key_value, low_rows, up_full)


def attend(query_rows, key_value, grad_rows, is_first, low_rows, up_full):
    length = query_rows.shape[0]
    group_size = HEADS // KV_HEADS
    query_pos = lax.broadcasted_iota(jnp.int32, (group_size * length, 2 * length), 0) % length
    key_pos = lax.broadcasted_iota(jnp.int32, (group_size * length, 2 * length), 1)
    visible = (
        (key_pos > query_pos)
        & (key_pos <= query_pos + length)
        & (jnp.logical_not(is_first) | (key_pos >= length))
    )
    return attention_heads(visible.astype(jnp.int32), query_rows, grad_rows, key_value, low_rows, up_full)


def projection_kernel(rows_ref, weight_ref, low_ref, up_ref, out_ref):
    row_shards = weight_ref.shape[0]
    base = jnp.dot(low_ref[0], up_ref[0], preferred_element_type=jnp.float32) * adapter_scale
    for c in range(row_shards):
        base = base + jnp.dot(rows_ref[c], weight_ref[c, 0, 0], preferred_element_type=jnp.float32)
    out_ref[0] = base.astype(out_ref.dtype)


def project_pair(rows_split, gathered, low_rows, up_full):
    row_shards, col_shards, members, depth, cols = gathered.shape
    rows = rows_split.shape[1]
    rank = up_full.shape[1]
    return pl.pallas_call(
        projection_kernel,
        grid=(members, col_shards),
        in_specs=[
            pl.BlockSpec((row_shards, rows, depth), lambda m, i: (0, 0, 0)),
            pl.BlockSpec((row_shards, 1, 1, depth, cols), lambda m, i: (0, i, m, 0, 0)),
            pl.BlockSpec((1, rows, rank), lambda m, i: (m, 0, 0)),
            pl.BlockSpec((1, rank, cols), lambda m, i: (m, 0, i)),
        ],
        out_specs=pl.BlockSpec((1, rows, cols), lambda m, i: (m, 0, i)),
        out_shape=jax.ShapeDtypeStruct((members, rows, col_shards * cols), jnp.bfloat16),
    )(rows_split, gathered, low_rows, up_full)


def project_rows(rows_previous, rows_own, kv_weight, down_full, up_full):
    def low_of(rows):
        return jnp.einsum(
            "rd,mkd->mrk", rows, down_full, preferred_element_type=jnp.float32
        ).astype(jnp.bfloat16)

    low_previous, low_rank = low_of(rows_previous), low_of(rows_own)
    row_shards, col_shards = lax.axis_size("ctx"), lax.axis_size(("dp", "sub"))
    rows_both = jnp.concatenate([rows_previous, rows_own], axis=0)
    rows_split = rows_both.reshape(rows_both.shape[0], row_shards, -1).swapaxes(0, 1)
    gathered = lax.all_gather(kv_weight, ("ctx", "dp", "sub"), axis=0, tiled=False)
    gathered = gathered.reshape((row_shards, col_shards) + kv_weight.shape)
    low_rows = jnp.concatenate([low_previous, low_rank], axis=1)
    key_value = project_pair(rows_split, gathered, low_rows, up_full)
    return rows_both, low_rows, key_value


def exchange_gather(block, axis):
    size = lax.axis_size(axis)
    me = lax.axis_index(axis)
    received = [block] + [
        lax.ppermute(block, axis, [(i, (i + shift) % size) for i in range(size)])
        for shift in range(1, size)
    ]
    order = (me - jnp.arange(size)) % size
    return jnp.take(jnp.stack(received), order, axis=0)


def gather_adapters(adapter_down, adapter_up):
    down_cols = adapter_down.shape[2]
    joined = jnp.concatenate([adapter_down, adapter_up], axis=2)
    if lax.axis_size(("dp", "sub")) <= 4 and lax.axis_size("ctx") <= 4:
        gathered = exchange_gather(exchange_gather(joined, ("dp", "sub")), "ctx")
        gathered = gathered.reshape((-1,) + joined.shape)
    else:
        gathered = lax.all_gather(joined, ("ctx", "dp", "sub"), axis=0, tiled=False)
    shards = gathered.shape[0]

    def unshard(piece):
        return piece.transpose(1, 2, 0, 3).reshape(2, piece.shape[2], shards * piece.shape[3])

    return unshard(gathered[..., :down_cols]), unshard(gathered[..., down_cols:])


def exchange_scatter(blocks, axis):
    size = lax.axis_size(axis)
    me = lax.axis_index(axis)
    total = lax.dynamic_index_in_dim(blocks, me, axis=0, keepdims=False)
    for shift in range(1, size):
        send = lax.dynamic_index_in_dim(blocks, (me + shift) % size, axis=0, keepdims=False)
        total = total + lax.ppermute(send, axis, [(i, (i + shift) % size) for i in range(size)])
    return total


def halving_scatter(blocks, axis):
    size = lax.axis_size(axis)
    if size <= 4:
        return exchange_scatter(blocks, axis)
    if size & (size - 1):
        return lax.psum_scatter(blocks, axis, scatter_dimension=0, tiled=True)[0]
    me = lax.axis_index(axis)
    stride = size // 2
    while stride >= 1:
        halves = blocks.reshape((2, blocks.shape[0] // 2) + blocks.shape[1:])
        bit = (me // stride) % 2
        keep = lax.dynamic_index_in_dim(halves, bit, axis=0, keepdims=False)
        send = lax.dynamic_index_in_dim(halves, 1 - bit, axis=0, keepdims=False)
        pairs = [(i, i ^ stride) for i in range(size)]
        blocks = keep + lax.ppermute(send, axis, pairs)
        stride //= 2
    return blocks[0]


def scatter_adapter_grads(joined_down, joined_up):
    members_rank = joined_down.shape[-1]
    down_cols = joined_down.shape[2]
    joined = jnp.concatenate([joined_down, joined_up], axis=2)
    mine = halving_scatter(joined, ("dp", "sub"))
    mine = halving_scatter(mine, "ctx")

    def unshard(piece):
        return piece.reshape(piece.shape[0], 2, -1).transpose(1, 2, 0)

    return unshard(mine[:down_cols]), unshard(mine[down_cols:])


def on_device(hidden, queries, kv_weight, adapter_down, adapter_up, out_grad):
    rows_own = hidden[0]
    query_rows = queries[0]
    grad_rows = out_grad[0]
    length = rows_own.shape[0]
    row_shards, col_shards = lax.axis_size("ctx"), lax.axis_size(("dp", "sub"))
    rows_previous = shifted(rows_own, "ctx", 1)
    down_full, up_full = gather_adapters(adapter_down, adapter_up)
    is_first = lax.axis_index("ctx") == 0
    rows_both, low_rows, kv_both = project_rows(
        rows_previous, rows_own, kv_weight, down_full, up_full
    )
    attended, query_grad, projected, up_terms = attend(
        query_rows, kv_both, grad_rows, is_first, low_rows, up_full
    )
    up_terms = up_terms.reshape(up_terms.shape[:2] + (row_shards, col_shards, -1)).transpose(3, 2, 4, 0, 1)
    down_terms = jnp.einsum(
        "mrk,rcij->icjmk",
        projected,
        rows_both.reshape(rows_both.shape[0], row_shards, col_shards, -1),
        preferred_element_type=jnp.float32,
    )
    factor = adapter_scale / (lax.axis_size("dp") * lax.axis_size("sub"))
    flat = lambda terms: (terms * factor).reshape(terms.shape[:3] + (-1,))
    down_part, up_part = scatter_adapter_grads(flat(down_terms), flat(up_terms))
    return (attended[None], query_grad[None], down_part, up_part)


def solution(mesh):
    placed = (
        P(("groups", "dp", "sub"), "ctx", None),
        P(("groups", "dp", "sub"), "ctx", None),
        P(None, "ctx", ("dp", "sub")),
        P(None, None, ("ctx", "dp", "sub")),
        P(None, None, ("ctx", "dp", "sub")),
        P(("groups", "dp", "sub"), "ctx", None),
    )
    return jax.shard_map(
        on_device,
        mesh=mesh,
        in_specs=placed,
        out_specs=(
            P(("groups", "dp", "sub"), "ctx", None),
            P(("groups", "dp", "sub"), "ctx", None),
            P("groups", None, ("ctx", "dp", "sub")),
            P("groups", None, ("ctx", "dp", "sub")),
        ),
        check_vma=False,
    )
```

```python
import jax
import jax.numpy as jnp
from jax import lax
from jax.experimental import pallas as pl
from jax.experimental.pallas import tpu as pltpu
from jax.sharding import PartitionSpec as P

HEADS = 16
KV_HEADS = 8
HEAD_DIM = 128


query_scale = 1.0 / 12.0
logit_cap = 50.0
adapter_scale = 0.5


def shifted(value, axis, by):
    length = lax.axis_size(axis)
    pairs = [(i, i + by) for i in range(length) if 0 <= i + by < length]
    return lax.ppermute(value, axis, pairs)


def attention_kernel(
    mask_ref, q_ref, do_ref, rows_ref, weight_ref, low_ref, up_ref,
    out_ref, dq_ref, projected_ref, up_terms_ref, projected_acc,
):
    head = pl.program_id(0)
    half = HEAD_DIM
    q = jnp.concatenate([q_ref[:, :half], q_ref[:, half:]], axis=0)
    do = jnp.concatenate([do_ref[:, :half], do_ref[:, half:]], axis=0)
    row_shards = weight_ref.shape[0]

    def project(member):
        base = jnp.dot(low_ref[member], up_ref[member], preferred_element_type=jnp.float32)
        base = base * adapter_scale
        for c in range(row_shards):
            base = base + jnp.dot(
                rows_ref[c], weight_ref[c, 0, member], preferred_element_type=jnp.float32
            )
        return base.astype(jnp.bfloat16)

    k = project(0)
    v = project(1)
    rows = q_ref.shape[0]
    visible = mask_ref[...] != 0
    contract_last = (((1,), (1,)), ((), ()))
    contract_first = (((0,), (0,)), ((), ()))
    raw_score = lax.dot_general(q, k, contract_last, preferred_element_type=jnp.float32) * query_scale
    bent_score = jnp.tanh(raw_score / logit_cap)
    expo_terms = jnp.where(visible, jnp.exp(logit_cap * bent_score), 0.0)
    denominator = jnp.sum(expo_terms, axis=-1, keepdims=True)
    prob_wide = (expo_terms * (1.0 / denominator)).astype(jnp.bfloat16).astype(jnp.float32)
    attn_prob = prob_wide.astype(jnp.bfloat16)
    head_out = jnp.dot(attn_prob, v, preferred_element_type=jnp.float32).astype(out_ref.dtype)
    out_ref[:, :half] = head_out[:rows]
    out_ref[:, half:] = head_out[rows:]
    prob_grad = lax.dot_general(do, v, contract_last, preferred_element_type=jnp.float32)
    row_delta = jnp.sum(prob_wide * prob_grad, axis=-1, keepdims=True)
    score_wide = prob_wide * (prob_grad - row_delta) * (1.0 - bent_score * bent_score) * query_scale
    score_grad = score_wide.astype(jnp.bfloat16)
    head_qgrad = jnp.dot(score_grad, k, preferred_element_type=jnp.float32).astype(dq_ref.dtype)
    dq_ref[:, :half] = head_qgrad[:rows]
    dq_ref[:, half:] = head_qgrad[rows:]
    key_grad = lax.dot_general(
        score_grad, q, contract_first, preferred_element_type=jnp.float32
    ).astype(jnp.bfloat16)
    value_grad = lax.dot_general(
        attn_prob, do, contract_first, preferred_element_type=jnp.float32
    ).astype(jnp.bfloat16)

    @pl.when(head == 0)
    def _():
        projected_acc[...] = jnp.zeros_like(projected_acc)

    for member, grad in enumerate((key_grad, value_grad)):
        projected_acc[member] += lax.dot_general(
            grad, up_ref[member], contract_last, preferred_element_type=jnp.float32
        )
        up_terms_ref[member] = lax.dot_general(
            low_ref[member], grad, contract_first, preferred_element_type=jnp.float32
        )

    @pl.when(head == pl.num_programs(0) - 1)
    def _():
        projected_ref[...] = projected_acc[...].astype(projected_ref.dtype)


def attention_heads(mask, queries, grads, rows_split, gathered, low_rows, up_full):
    rows, width = queries.shape
    row_shards, col_shards, members, depth, cols = gathered.shape
    keys = rows_split.shape[1]
    rank = up_full.shape[1]
    kv_width = col_shards * cols
    heads = kv_width // HEAD_DIM
    per_shard = cols // HEAD_DIM
    group_cols = width // heads
    row_block = pl.BlockSpec((rows, group_cols), lambda g: (0, g))
    whole = lambda shape: pl.BlockSpec(shape, lambda g: (0,) * len(shape))
    return pl.pallas_call(
        attention_kernel,
        grid=(heads,),
        in_specs=[
            whole(mask.shape),
            row_block,
            row_block,
            whole(rows_split.shape),
            pl.BlockSpec(
                (row_shards, 1, members, depth, HEAD_DIM),
                lambda g: (0, g // per_shard, 0, 0, g % per_shard),
            ),
            whole(low_rows.shape),
            pl.BlockSpec((members, rank, HEAD_DIM), lambda g: (0, 0, g)),
        ],
        out_specs=[
            row_block,
            row_block,
            whole((members, keys, rank)),
            pl.BlockSpec((members, rank, HEAD_DIM), lambda g: (0, 0, g)),
        ],
        out_shape=[
            jax.ShapeDtypeStruct((rows, width), jnp.bfloat16),
            jax.ShapeDtypeStruct((rows, width), jnp.bfloat16),
            jax.ShapeDtypeStruct((members, keys, rank), jnp.bfloat16),
            jax.ShapeDtypeStruct((members, rank, kv_width), jnp.float32),
        ],
        scratch_shapes=[pltpu.VMEM((members, keys, rank), jnp.float32)],
    )(mask, queries, grads, rows_split, gathered, low_rows, up_full)


def attend(query_rows, rows_split, gathered, grad_rows, is_first, low_rows, up_full):
    length = query_rows.shape[0]
    group_size = HEADS // KV_HEADS
    query_pos = lax.broadcasted_iota(jnp.int32, (group_size * length, 2 * length), 0) % length
    key_pos = lax.broadcasted_iota(jnp.int32, (group_size * length, 2 * length), 1)
    visible = (
        (key_pos > query_pos)
        & (key_pos <= query_pos + length)
        & (jnp.logical_not(is_first) | (key_pos >= length))
    )
    return attention_heads(
        visible.astype(jnp.int32), query_rows, grad_rows, rows_split, gathered, low_rows, up_full
    )


def project_rows(rows_previous, rows_own, kv_weight, down_full, up_full):
    def low_of(rows):
        return jnp.einsum(
            "rd,mkd->mrk", rows, down_full, preferred_element_type=jnp.float32
        ).astype(jnp.bfloat16)

    low_previous, low_rank = low_of(rows_previous), low_of(rows_own)
    row_shards, col_shards = lax.axis_size("ctx"), lax.axis_size(("dp", "sub"))
    rows_both = jnp.concatenate([rows_previous, rows_own], axis=0)
    rows_split = rows_both.reshape(rows_both.shape[0], row_shards, -1).swapaxes(0, 1)
    gathered = lax.all_gather(kv_weight, ("ctx", "dp", "sub"), axis=0, tiled=False)
    gathered = gathered.reshape((row_shards, col_shards) + kv_weight.shape)
    low_rows = jnp.concatenate([low_previous, low_rank], axis=1)
    return rows_both, rows_split, gathered, low_rows


def gather_adapters(adapter_down, adapter_up):
    axes = ("ctx", "dp", "sub")
    down_cols = adapter_down.shape[2]
    joined = jnp.concatenate([adapter_down, adapter_up], axis=2)
    gathered = lax.all_gather(joined, axes, axis=0, tiled=False)
    shards = gathered.shape[0]

    def unshard(piece):
        return piece.transpose(1, 2, 0, 3).reshape(2, piece.shape[2], shards * piece.shape[3])

    return unshard(gathered[..., :down_cols]), unshard(gathered[..., down_cols:])


def exchange_scatter(blocks, axis):
    size = lax.axis_size(axis)
    me = lax.axis_index(axis)
    total = lax.dynamic_index_in_dim(blocks, me, axis=0, keepdims=False)
    for shift in range(1, size):
        send = lax.dynamic_index_in_dim(blocks, (me + shift) % size, axis=0, keepdims=False)
        total = total + lax.ppermute(send, axis, [(i, (i + shift) % size) for i in range(size)])
    return total


def halving_scatter(blocks, axis):
    size = lax.axis_size(axis)
    if size <= 4:
        return exchange_scatter(blocks, axis)
    if size & (size - 1):
        return lax.psum_scatter(blocks, axis, scatter_dimension=0, tiled=True)[0]
    me = lax.axis_index(axis)
    stride = size // 2
    while stride >= 1:
        halves = blocks.reshape((2, blocks.shape[0] // 2) + blocks.shape[1:])
        bit = (me // stride) % 2
        keep = lax.dynamic_index_in_dim(halves, bit, axis=0, keepdims=False)
        send = lax.dynamic_index_in_dim(halves, 1 - bit, axis=0, keepdims=False)
        pairs = [(i, i ^ stride) for i in range(size)]
        blocks = keep + lax.ppermute(send, axis, pairs)
        stride //= 2
    return blocks[0]


def scatter_adapter_grads(joined_down, joined_up):
    members_rank = joined_down.shape[-1]
    down_cols = joined_down.shape[2]
    joined = jnp.concatenate([joined_down, joined_up], axis=2)
    mine = halving_scatter(joined, ("dp", "sub"))
    mine = halving_scatter(mine, "ctx")

    def unshard(piece):
        return piece.reshape(piece.shape[0], 2, -1).transpose(1, 2, 0)

    return unshard(mine[:down_cols]), unshard(mine[down_cols:])


def on_device(hidden, queries, kv_weight, adapter_down, adapter_up, out_grad):
    rows_own = hidden[0]
    query_rows = queries[0]
    grad_rows = out_grad[0]
    length = rows_own.shape[0]
    row_shards, col_shards = lax.axis_size("ctx"), lax.axis_size(("dp", "sub"))
    rows_previous = shifted(rows_own, "ctx", 1)
    down_full, up_full = gather_adapters(adapter_down, adapter_up)
    is_first = lax.axis_index("ctx") == 0
    rows_both, rows_split, gathered, low_rows = project_rows(
        rows_previous, rows_own, kv_weight, down_full, up_full
    )
    attended, query_grad, projected, up_terms = attend(
        query_rows, rows_split, gathered, grad_rows, is_first, low_rows, up_full
    )
    up_terms = up_terms.reshape(up_terms.shape[:2] + (row_shards, col_shards, -1)).transpose(3, 2, 4, 0, 1)
    down_terms = jnp.einsum(
        "mrk,rcij->icjmk",
        projected,
        rows_both.reshape(rows_both.shape[0], row_shards, col_shards, -1),
        preferred_element_type=jnp.float32,
    )
    factor = adapter_scale / (lax.axis_size("dp") * lax.axis_size("sub"))
    flat = lambda terms: (terms * factor).reshape(terms.shape[:3] + (-1,))
    down_part, up_part = scatter_adapter_grads(flat(down_terms), flat(up_terms))
    return (attended[None], query_grad[None], down_part, up_part)


def solution(mesh):
    placed = (
        P(("groups", "dp", "sub"), "ctx", None),
        P(("groups", "dp", "sub"), "ctx", None),
        P(None, "ctx", ("dp", "sub")),
        P(None, None, ("ctx", "dp", "sub")),
        P(None, None, ("ctx", "dp", "sub")),
        P(("groups", "dp", "sub"), "ctx", None),
    )
    return jax.shard_map(
        on_device,
        mesh=mesh,
        in_specs=placed,
        out_specs=(
            P(("groups", "dp", "sub"), "ctx", None),
            P(("groups", "dp", "sub"), "ctx", None),
            P("groups", None, ("ctx", "dp", "sub")),
            P("groups", None, ("ctx", "dp", "sub")),
        ),
        check_vma=False,
    )
```

```python
import jax
import jax.numpy as jnp
from jax import lax
from jax.experimental import pallas as pl
from jax.experimental.pallas import tpu as pltpu
from jax.sharding import PartitionSpec as P

HEADS = 16
KV_HEADS = 8
HEAD_DIM = 128


query_scale = 1.0 / 12.0
logit_cap = 50.0
adapter_scale = 0.5


def shifted(value, axis, by):
    length = lax.axis_size(axis)
    pairs = [(i, i + by) for i in range(length) if 0 <= i + by < length]
    return lax.ppermute(value, axis, pairs)


def attention_kernel(
    mask_ref, q_ref, do_ref, rows_ref, weight_ref, low_ref, up_ref,
    out_ref, dq_ref, projected_ref, up_terms_ref, projected_acc,
):
    step = pl.program_id(0)
    half = HEAD_DIM
    row_shards = weight_ref.shape[0]
    heads_here = weight_ref.shape[4] // HEAD_DIM
    rows = q_ref.shape[0]
    visible = mask_ref[...] != 0
    contract_last = (((1,), (1,)), ((), ()))
    contract_first = (((0,), (0,)), ((), ()))

    def project(member):
        base = jnp.dot(low_ref[member], up_ref[member], preferred_element_type=jnp.float32)
        base = base * adapter_scale
        for c in range(row_shards):
            base = base + jnp.dot(
                rows_ref[c], weight_ref[c, 0, member], preferred_element_type=jnp.float32
            )
        return base.astype(jnp.bfloat16)

    keys_here = project(0)
    values_here = project(1)

    @pl.when(step == 0)
    def _():
        projected_acc[...] = jnp.zeros_like(projected_acc)

    for h in range(heads_here):
        cols = slice(h * HEAD_DIM, (h + 1) * HEAD_DIM)
        qa = slice(2 * h * half, (2 * h + 1) * half)
        qb = slice((2 * h + 1) * half, (2 * h + 2) * half)
        q = jnp.concatenate([q_ref[:, qa], q_ref[:, qb]], axis=0)
        do = jnp.concatenate([do_ref[:, qa], do_ref[:, qb]], axis=0)
        k = keys_here[:, cols]
        v = values_here[:, cols]
        raw_score = lax.dot_general(q, k, contract_last, preferred_element_type=jnp.float32) * query_scale
        bent_score = jnp.tanh(raw_score / logit_cap)
        expo_terms = jnp.where(visible, jnp.exp(logit_cap * bent_score), 0.0)
        denominator = jnp.sum(expo_terms, axis=-1, keepdims=True)
        prob_wide = (expo_terms * (1.0 / denominator)).astype(jnp.bfloat16).astype(jnp.float32)
        attn_prob = prob_wide.astype(jnp.bfloat16)
        head_out = jnp.dot(attn_prob, v, preferred_element_type=jnp.float32).astype(out_ref.dtype)
        out_ref[:, qa] = head_out[:rows]
        out_ref[:, qb] = head_out[rows:]
        prob_grad = lax.dot_general(do, v, contract_last, preferred_element_type=jnp.float32)
        row_delta = jnp.sum(prob_wide * prob_grad, axis=-1, keepdims=True)
        score_wide = prob_wide * (prob_grad - row_delta) * (1.0 - bent_score * bent_score) * query_scale
        score_grad = score_wide.astype(jnp.bfloat16)
        head_qgrad = jnp.dot(score_grad, k, preferred_element_type=jnp.float32).astype(dq_ref.dtype)
        dq_ref[:, qa] = head_qgrad[:rows]
        dq_ref[:, qb] = head_qgrad[rows:]
        key_grad = lax.dot_general(
            score_grad, q, contract_first, preferred_element_type=jnp.float32
        ).astype(jnp.bfloat16)
        value_grad = lax.dot_general(
            attn_prob, do, contract_first, preferred_element_type=jnp.float32
        ).astype(jnp.bfloat16)
        for member, grad in enumerate((key_grad, value_grad)):
            projected_acc[member] += lax.dot_general(
                grad, up_ref[member, :, cols], contract_last, preferred_element_type=jnp.float32
            )
            up_terms_ref[member, :, cols] = lax.dot_general(
                low_ref[member], grad, contract_first, preferred_element_type=jnp.float32
            )

    @pl.when(step == pl.num_programs(0) - 1)
    def _():
        projected_ref[...] = projected_acc[...].astype(projected_ref.dtype)


def attention_heads(mask, queries, grads, rows_split, gathered, low_rows, up_full):
    rows, width = queries.shape
    row_shards, col_shards, members, depth, cols = gathered.shape
    keys = rows_split.shape[1]
    rank = up_full.shape[1]
    kv_width = col_shards * cols
    heads = kv_width // HEAD_DIM
    step_cols = width // col_shards
    row_block = pl.BlockSpec((rows, step_cols), lambda i: (0, i))
    whole = lambda shape: pl.BlockSpec(shape, lambda i: (0,) * len(shape))
    return pl.pallas_call(
        attention_kernel,
        grid=(col_shards,),
        in_specs=[
            whole(mask.shape),
            row_block,
            row_block,
            whole(rows_split.shape),
            pl.BlockSpec((row_shards, 1, members, depth, cols), lambda i: (0, i, 0, 0, 0)),
            whole(low_rows.shape),
            pl.BlockSpec((members, rank, cols), lambda i: (0, 0, i)),
        ],
        out_specs=[
            row_block,
            row_block,
            whole((members, keys, rank)),
            pl.BlockSpec((members, rank, cols), lambda i: (0, 0, i)),
        ],
        out_shape=[
            jax.ShapeDtypeStruct((rows, width), jnp.bfloat16),
            jax.ShapeDtypeStruct((rows, width), jnp.bfloat16),
            jax.ShapeDtypeStruct((members, keys, rank), jnp.bfloat16),
            jax.ShapeDtypeStruct((members, rank, kv_width), jnp.float32),
        ],
        scratch_shapes=[pltpu.VMEM((members, keys, rank), jnp.float32)],
    )(mask, queries, grads, rows_split, gathered, low_rows, up_full)


def attend(query_rows, rows_split, gathered, grad_rows, is_first, low_rows, up_full):
    length = query_rows.shape[0]
    group_size = HEADS // KV_HEADS
    query_pos = lax.broadcasted_iota(jnp.int32, (group_size * length, 2 * length), 0) % length
    key_pos = lax.broadcasted_iota(jnp.int32, (group_size * length, 2 * length), 1)
    visible = (
        (key_pos > query_pos)
        & (key_pos <= query_pos + length)
        & (jnp.logical_not(is_first) | (key_pos >= length))
    )
    return attention_heads(
        visible.astype(jnp.int32), query_rows, grad_rows, rows_split, gathered, low_rows, up_full
    )


def project_rows(rows_previous, rows_own, kv_weight, down_full, up_full):
    def low_of(rows):
        return jnp.einsum(
            "rd,mkd->mrk", rows, down_full, preferred_element_type=jnp.float32
        ).astype(jnp.bfloat16)

    low_previous, low_rank = low_of(rows_previous), low_of(rows_own)
    row_shards, col_shards = lax.axis_size("ctx"), lax.axis_size(("dp", "sub"))
    rows_both = jnp.concatenate([rows_previous, rows_own], axis=0)
    rows_split = rows_both.reshape(rows_both.shape[0], row_shards, -1).swapaxes(0, 1)
    gathered = lax.all_gather(kv_weight, ("ctx", "dp", "sub"), axis=0, tiled=False)
    gathered = gathered.reshape((row_shards, col_shards) + kv_weight.shape)
    low_rows = jnp.concatenate([low_previous, low_rank], axis=1)
    return rows_both, rows_split, gathered, low_rows


def gather_adapters(adapter_down, adapter_up):
    axes = ("ctx", "dp", "sub")
    down_cols = adapter_down.shape[2]
    joined = jnp.concatenate([adapter_down, adapter_up], axis=2)
    gathered = lax.all_gather(joined, axes, axis=0, tiled=False)
    shards = gathered.shape[0]

    def unshard(piece):
        return piece.transpose(1, 2, 0, 3).reshape(2, piece.shape[2], shards * piece.shape[3])

    return unshard(gathered[..., :down_cols]), unshard(gathered[..., down_cols:])


def exchange_scatter(blocks, axis):
    size = lax.axis_size(axis)
    me = lax.axis_index(axis)
    total = lax.dynamic_index_in_dim(blocks, me, axis=0, keepdims=False)
    for shift in range(1, size):
        send = lax.dynamic_index_in_dim(blocks, (me + shift) % size, axis=0, keepdims=False)
        total = total + lax.ppermute(send, axis, [(i, (i + shift) % size) for i in range(size)])
    return total


def halving_scatter(blocks, axis):
    size = lax.axis_size(axis)
    if size <= 4:
        return exchange_scatter(blocks, axis)
    if size & (size - 1):
        return lax.psum_scatter(blocks, axis, scatter_dimension=0, tiled=True)[0]
    me = lax.axis_index(axis)
    stride = size // 2
    while stride >= 1:
        halves = blocks.reshape((2, blocks.shape[0] // 2) + blocks.shape[1:])
        bit = (me // stride) % 2
        keep = lax.dynamic_index_in_dim(halves, bit, axis=0, keepdims=False)
        send = lax.dynamic_index_in_dim(halves, 1 - bit, axis=0, keepdims=False)
        pairs = [(i, i ^ stride) for i in range(size)]
        blocks = keep + lax.ppermute(send, axis, pairs)
        stride //= 2
    return blocks[0]


def scatter_adapter_grads(joined_down, joined_up):
    members_rank = joined_down.shape[-1]
    down_cols = joined_down.shape[2]
    joined = jnp.concatenate([joined_down, joined_up], axis=2)
    mine = halving_scatter(joined, ("dp", "sub"))
    mine = halving_scatter(mine, "ctx")

    def unshard(piece):
        return piece.reshape(piece.shape[0], 2, -1).transpose(1, 2, 0)

    return unshard(mine[:down_cols]), unshard(mine[down_cols:])


def on_device(hidden, queries, kv_weight, adapter_down, adapter_up, out_grad):
    rows_own = hidden[0]
    query_rows = queries[0]
    grad_rows = out_grad[0]
    length = rows_own.shape[0]
    row_shards, col_shards = lax.axis_size("ctx"), lax.axis_size(("dp", "sub"))
    rows_previous = shifted(rows_own, "ctx", 1)
    down_full, up_full = gather_adapters(adapter_down, adapter_up)
    is_first = lax.axis_index("ctx") == 0
    rows_both, rows_split, gathered, low_rows = project_rows(
        rows_previous, rows_own, kv_weight, down_full, up_full
    )
    attended, query_grad, projected, up_terms = attend(
        query_rows, rows_split, gathered, grad_rows, is_first, low_rows, up_full
    )
    up_terms = up_terms.reshape(up_terms.shape[:2] + (row_shards, col_shards, -1)).transpose(3, 2, 4, 0, 1)
    down_terms = jnp.einsum(
        "mrk,rcij->icjmk",
        projected,
        rows_both.reshape(rows_both.shape[0], row_shards, col_shards, -1),
        preferred_element_type=jnp.float32,
    )
    factor = adapter_scale / (lax.axis_size("dp") * lax.axis_size("sub"))
    flat = lambda terms: (terms * factor).reshape(terms.shape[:3] + (-1,))
    down_part, up_part = scatter_adapter_grads(flat(down_terms), flat(up_terms))
    return (attended[None], query_grad[None], down_part, up_part)


def solution(mesh):
    placed = (
        P(("groups", "dp", "sub"), "ctx", None),
        P(("groups", "dp", "sub"), "ctx", None),
        P(None, "ctx", ("dp", "sub")),
        P(None, None, ("ctx", "dp", "sub")),
        P(None, None, ("ctx", "dp", "sub")),
        P(("groups", "dp", "sub"), "ctx", None),
    )
    return jax.shard_map(
        on_device,
        mesh=mesh,
        in_specs=placed,
        out_specs=(
            P(("groups", "dp", "sub"), "ctx", None),
            P(("groups", "dp", "sub"), "ctx", None),
            P("groups", None, ("ctx", "dp", "sub")),
            P("groups", None, ("ctx", "dp", "sub")),
        ),
        check_vma=False,
    )
```

```python
import jax
import jax.numpy as jnp
from jax import lax
from jax.experimental import pallas as pl
from jax.experimental.pallas import tpu as pltpu
from jax.sharding import PartitionSpec as P

HEADS = 16
KV_HEADS = 8
HEAD_DIM = 128


query_scale = 1.0 / 12.0
logit_cap = 50.0
adapter_scale = 0.5


def shifted(value, axis, by):
    length = lax.axis_size(axis)
    pairs = [(i, i + by) for i in range(length) if 0 <= i + by < length]
    return lax.ppermute(value, axis, pairs)


def attention_kernel(
    mask_ref, q_ref, do_ref, rows_ref, weight_ref, low_ref, up_ref,
    out_ref, dq_ref, projected_ref, up_terms_ref, projected_acc,
):
    step = pl.program_id(0)
    half = HEAD_DIM
    row_shards = weight_ref.shape[0]
    heads_here = weight_ref.shape[4] // HEAD_DIM
    rows = q_ref.shape[0]
    visible = mask_ref[...] != 0
    contract_last = (((1,), (1,)), ((), ()))
    contract_first = (((0,), (0,)), ((), ()))

    def project(member):
        base = jnp.dot(low_ref[member], up_ref[member], preferred_element_type=jnp.float32)
        base = base * adapter_scale
        for c in range(row_shards):
            base = base + jnp.dot(
                rows_ref[c], weight_ref[c, 0, member], preferred_element_type=jnp.float32
            )
        return base.astype(jnp.bfloat16)

    keys_here = project(0)
    values_here = project(1)

    @pl.when(step == 0)
    def _():
        projected_acc[...] = jnp.zeros_like(projected_acc)

    for h in range(heads_here):
        cols = slice(h * HEAD_DIM, (h + 1) * HEAD_DIM)
        qa = slice(2 * h * half, (2 * h + 1) * half)
        qb = slice((2 * h + 1) * half, (2 * h + 2) * half)
        q = jnp.concatenate([q_ref[:, qa], q_ref[:, qb]], axis=0)
        do = jnp.concatenate([do_ref[:, qa], do_ref[:, qb]], axis=0)
        k = keys_here[:, cols]
        v = values_here[:, cols]
        raw_score = lax.dot_general(q, k, contract_last, preferred_element_type=jnp.float32) * query_scale
        bent_score = jnp.tanh(raw_score / logit_cap)
        expo_terms = jnp.where(visible, jnp.exp(logit_cap * bent_score), 0.0)
        denominator = jnp.sum(expo_terms, axis=-1, keepdims=True)
        prob_wide = (expo_terms * (1.0 / denominator)).astype(jnp.bfloat16).astype(jnp.float32)
        attn_prob = prob_wide.astype(jnp.bfloat16)
        head_out = jnp.dot(attn_prob, v, preferred_element_type=jnp.float32).astype(out_ref.dtype)
        out_ref[:, qa] = head_out[:rows]
        out_ref[:, qb] = head_out[rows:]
        prob_grad = lax.dot_general(do, v, contract_last, preferred_element_type=jnp.float32)
        row_delta = jnp.sum(prob_wide * prob_grad, axis=-1, keepdims=True)
        score_wide = prob_wide * (prob_grad - row_delta) * (1.0 - bent_score * bent_score) * query_scale
        score_grad = score_wide.astype(jnp.bfloat16)
        head_qgrad = jnp.dot(score_grad, k, preferred_element_type=jnp.float32).astype(dq_ref.dtype)
        dq_ref[:, qa] = head_qgrad[:rows]
        dq_ref[:, qb] = head_qgrad[rows:]
        key_grad = lax.dot_general(
            score_grad, q, contract_first, preferred_element_type=jnp.float32
        ).astype(jnp.bfloat16)
        value_grad = lax.dot_general(
            attn_prob, do, contract_first, preferred_element_type=jnp.float32
        ).astype(jnp.bfloat16)
        for member, grad in enumerate((key_grad, value_grad)):
            projected_acc[member] += lax.dot_general(
                grad, up_ref[member, :, cols], contract_last, preferred_element_type=jnp.float32
            )
            up_terms_ref[member, :, cols] = lax.dot_general(
                low_ref[member], grad, contract_first, preferred_element_type=jnp.float32
            )

    @pl.when(step == pl.num_programs(0) - 1)
    def _():
        projected_ref[...] = projected_acc[...].astype(projected_ref.dtype)


def attention_heads(mask, queries, grads, rows_split, gathered, low_rows, up_full):
    rows, width = queries.shape
    row_shards, col_shards, members, depth, cols = gathered.shape
    keys = rows_split.shape[1]
    rank = up_full.shape[1]
    kv_width = col_shards * cols
    heads = kv_width // HEAD_DIM
    step_cols = width // col_shards
    row_block = pl.BlockSpec((rows, step_cols), lambda i: (0, i))
    whole = lambda shape: pl.BlockSpec(shape, lambda i: (0,) * len(shape))
    return pl.pallas_call(
        attention_kernel,
        grid=(col_shards,),
        in_specs=[
            whole(mask.shape),
            row_block,
            row_block,
            whole(rows_split.shape),
            pl.BlockSpec((row_shards, 1, members, depth, cols), lambda i: (0, i, 0, 0, 0)),
            whole(low_rows.shape),
            pl.BlockSpec((members, rank, cols), lambda i: (0, 0, i)),
        ],
        out_specs=[
            row_block,
            row_block,
            whole((members, keys, rank)),
            pl.BlockSpec((members, rank, cols), lambda i: (0, 0, i)),
        ],
        out_shape=[
            jax.ShapeDtypeStruct((rows, width), jnp.bfloat16),
            jax.ShapeDtypeStruct((rows, width), jnp.bfloat16),
            jax.ShapeDtypeStruct((members, keys, rank), jnp.bfloat16),
            jax.ShapeDtypeStruct((members, rank, kv_width), jnp.float32),
        ],
        scratch_shapes=[pltpu.VMEM((members, keys, rank), jnp.float32)],
    )(mask, queries, grads, rows_split, gathered, low_rows, up_full)


def attend(query_rows, rows_split, gathered, grad_rows, is_first, low_rows, up_full):
    length = query_rows.shape[0]
    group_size = HEADS // KV_HEADS
    query_pos = lax.broadcasted_iota(jnp.int32, (group_size * length, 2 * length), 0) % length
    key_pos = lax.broadcasted_iota(jnp.int32, (group_size * length, 2 * length), 1)
    visible = (
        (key_pos > query_pos)
        & (key_pos <= query_pos + length)
        & (jnp.logical_not(is_first) | (key_pos >= length))
    )
    return attention_heads(
        visible.astype(jnp.int32), query_rows, grad_rows, rows_split, gathered, low_rows, up_full
    )


def project_rows(rows_previous, rows_own, kv_weight, down_full, up_full):
    def low_of(rows):
        return jnp.einsum(
            "rd,mkd->mrk", rows, down_full, preferred_element_type=jnp.float32
        ).astype(jnp.bfloat16)

    low_previous, low_rank = low_of(rows_previous), low_of(rows_own)
    row_shards, col_shards = lax.axis_size("ctx"), lax.axis_size(("dp", "sub"))
    rows_both = jnp.concatenate([rows_previous, rows_own], axis=0)
    rows_split = rows_both.reshape(rows_both.shape[0], row_shards, -1).swapaxes(0, 1)
    gathered = lax.all_gather(kv_weight, ("ctx", "dp", "sub"), axis=0, tiled=False)
    gathered = gathered.reshape((row_shards, col_shards) + kv_weight.shape)
    low_rows = jnp.concatenate([low_previous, low_rank], axis=1)
    return rows_both, rows_split, gathered, low_rows


def gather_adapters(adapter_down, adapter_up):
    axes = ("ctx", "dp", "sub")
    down_cols = adapter_down.shape[2]
    joined = jnp.concatenate([adapter_down, adapter_up], axis=2)
    gathered = lax.all_gather(joined, axes, axis=0, tiled=False)
    shards = gathered.shape[0]

    def unshard(piece):
        return piece.transpose(1, 2, 0, 3).reshape(2, piece.shape[2], shards * piece.shape[3])

    return unshard(gathered[..., :down_cols]), unshard(gathered[..., down_cols:])


def exchange_scatter(blocks, axis):
    size = lax.axis_size(axis)
    me = lax.axis_index(axis)
    total = lax.dynamic_index_in_dim(blocks, me, axis=0, keepdims=False)
    for shift in range(1, size):
        send = lax.dynamic_index_in_dim(blocks, (me + shift) % size, axis=0, keepdims=False)
        total = total + lax.ppermute(send, axis, [(i, (i + shift) % size) for i in range(size)])
    return total


def halving_scatter(blocks, axis):
    size = lax.axis_size(axis)
    if size <= 4:
        return exchange_scatter(blocks, axis)
    if size & (size - 1):
        return lax.psum_scatter(blocks, axis, scatter_dimension=0, tiled=True)[0]
    me = lax.axis_index(axis)
    stride = size // 2
    while stride >= 1:
        halves = blocks.reshape((2, blocks.shape[0] // 2) + blocks.shape[1:])
        bit = (me // stride) % 2
        keep = lax.dynamic_index_in_dim(halves, bit, axis=0, keepdims=False)
        send = lax.dynamic_index_in_dim(halves, 1 - bit, axis=0, keepdims=False)
        pairs = [(i, i ^ stride) for i in range(size)]
        blocks = keep + lax.ppermute(send, axis, pairs)
        stride //= 2
    return blocks[0]


def scatter_adapter_grads(joined_down, joined_up):
    members_rank = joined_down.shape[-1]
    down_cols = joined_down.shape[2]
    joined = jnp.concatenate([joined_down, joined_up], axis=2)
    if lax.axis_size(("ctx", "dp", "sub")) <= 16:
        owners = joined.swapaxes(0, 1).reshape((-1,) + joined.shape[2:])
        mine = exchange_scatter(owners, ("ctx", "dp", "sub"))
    else:
        mine = halving_scatter(joined, ("dp", "sub"))
        mine = halving_scatter(mine, "ctx")

    def unshard(piece):
        return piece.reshape(piece.shape[0], 2, -1).transpose(1, 2, 0)

    return unshard(mine[:down_cols]), unshard(mine[down_cols:])


def on_device(hidden, queries, kv_weight, adapter_down, adapter_up, out_grad):
    rows_own = hidden[0]
    query_rows = queries[0]
    grad_rows = out_grad[0]
    length = rows_own.shape[0]
    row_shards, col_shards = lax.axis_size("ctx"), lax.axis_size(("dp", "sub"))
    rows_previous = shifted(rows_own, "ctx", 1)
    down_full, up_full = gather_adapters(adapter_down, adapter_up)
    is_first = lax.axis_index("ctx") == 0
    rows_both, rows_split, gathered, low_rows = project_rows(
        rows_previous, rows_own, kv_weight, down_full, up_full
    )
    attended, query_grad, projected, up_terms = attend(
        query_rows, rows_split, gathered, grad_rows, is_first, low_rows, up_full
    )
    up_terms = up_terms.reshape(up_terms.shape[:2] + (row_shards, col_shards, -1)).transpose(3, 2, 4, 0, 1)
    down_terms = jnp.einsum(
        "mrk,rcij->icjmk",
        projected,
        rows_both.reshape(rows_both.shape[0], row_shards, col_shards, -1),
        preferred_element_type=jnp.float32,
    )
    factor = adapter_scale / (lax.axis_size("dp") * lax.axis_size("sub"))
    flat = lambda terms: (terms * factor).reshape(terms.shape[:3] + (-1,))
    down_part, up_part = scatter_adapter_grads(flat(down_terms), flat(up_terms))
    return (attended[None], query_grad[None], down_part, up_part)


def solution(mesh):
    placed = (
        P(("groups", "dp", "sub"), "ctx", None),
        P(("groups", "dp", "sub"), "ctx", None),
        P(None, "ctx", ("dp", "sub")),
        P(None, None, ("ctx", "dp", "sub")),
        P(None, None, ("ctx", "dp", "sub")),
        P(("groups", "dp", "sub"), "ctx", None),
    )
    return jax.shard_map(
        on_device,
        mesh=mesh,
        in_specs=placed,
        out_specs=(
            P(("groups", "dp", "sub"), "ctx", None),
            P(("groups", "dp", "sub"), "ctx", None),
            P("groups", None, ("ctx", "dp", "sub")),
            P("groups", None, ("ctx", "dp", "sub")),
        ),
        check_vma=False,
    )
```

```python
import jax
import jax.numpy as jnp
from jax import lax
from jax.experimental import pallas as pl
from jax.experimental.pallas import tpu as pltpu
from jax.sharding import PartitionSpec as P

HEADS = 16
KV_HEADS = 8
HEAD_DIM = 128


query_scale = 1.0 / 12.0
logit_cap = 50.0
adapter_scale = 0.5


def shifted(value, axis, by):
    length = lax.axis_size(axis)
    pairs = [(i, i + by) for i in range(length) if 0 <= i + by < length]
    return lax.ppermute(value, axis, pairs)


def attention_kernel(
    mask_ref, q_ref, do_ref, rows_ref, weight_ref, low_ref, up_ref,
    out_ref, dq_ref, projected_ref, up_terms_ref, projected_acc,
):
    step = pl.program_id(0)
    half = HEAD_DIM
    row_shards = weight_ref.shape[0]
    heads_here = weight_ref.shape[4] // HEAD_DIM
    rows = q_ref.shape[0]
    visible = mask_ref[...] != 0
    contract_last = (((1,), (1,)), ((), ()))
    contract_first = (((0,), (0,)), ((), ()))

    def project(member):
        base = jnp.dot(low_ref[member], up_ref[member], preferred_element_type=jnp.float32)
        base = base * adapter_scale
        for c in range(row_shards):
            base = base + jnp.dot(
                rows_ref[c], weight_ref[c, 0, member], preferred_element_type=jnp.float32
            )
        return base.astype(jnp.bfloat16)

    keys_here = project(0)
    values_here = project(1)

    @pl.when(step == 0)
    def _():
        projected_acc[...] = jnp.zeros_like(projected_acc)

    for h in range(heads_here):
        cols = slice(h * HEAD_DIM, (h + 1) * HEAD_DIM)
        qa = slice(2 * h * half, (2 * h + 1) * half)
        qb = slice((2 * h + 1) * half, (2 * h + 2) * half)
        q = jnp.concatenate([q_ref[:, qa], q_ref[:, qb]], axis=0)
        do = jnp.concatenate([do_ref[:, qa], do_ref[:, qb]], axis=0)
        k = keys_here[:, cols]
        v = values_here[:, cols]
        raw_score = lax.dot_general(q, k, contract_last, preferred_element_type=jnp.float32) * query_scale
        bent_score = jnp.tanh(raw_score / logit_cap)
        expo_terms = jnp.where(visible, jnp.exp(logit_cap * bent_score), 0.0)
        denominator = jnp.sum(expo_terms, axis=-1, keepdims=True)
        prob_wide = (expo_terms * (1.0 / denominator)).astype(jnp.bfloat16).astype(jnp.float32)
        attn_prob = prob_wide.astype(jnp.bfloat16)
        head_out = jnp.dot(attn_prob, v, preferred_element_type=jnp.float32).astype(out_ref.dtype)
        out_ref[:, qa] = head_out[:rows]
        out_ref[:, qb] = head_out[rows:]
        prob_grad = lax.dot_general(do, v, contract_last, preferred_element_type=jnp.float32)
        row_delta = jnp.sum(prob_wide * prob_grad, axis=-1, keepdims=True)
        score_wide = prob_wide * (prob_grad - row_delta) * (1.0 - bent_score * bent_score) * query_scale
        score_grad = score_wide.astype(jnp.bfloat16)
        head_qgrad = jnp.dot(score_grad, k, preferred_element_type=jnp.float32).astype(dq_ref.dtype)
        dq_ref[:, qa] = head_qgrad[:rows]
        dq_ref[:, qb] = head_qgrad[rows:]
        key_grad = lax.dot_general(
            score_grad, q, contract_first, preferred_element_type=jnp.float32
        ).astype(jnp.bfloat16)
        value_grad = lax.dot_general(
            attn_prob, do, contract_first, preferred_element_type=jnp.float32
        ).astype(jnp.bfloat16)
        for member, grad in enumerate((key_grad, value_grad)):
            projected_acc[member] += lax.dot_general(
                grad, up_ref[member, :, cols], contract_last, preferred_element_type=jnp.float32
            )
            up_terms_ref[member, :, cols] = lax.dot_general(
                low_ref[member], grad, contract_first, preferred_element_type=jnp.float32
            )

    @pl.when(step == pl.num_programs(0) - 1)
    def _():
        projected_ref[...] = projected_acc[...].astype(projected_ref.dtype)


def attention_heads(mask, queries, grads, rows_split, gathered, low_rows, up_full):
    rows, width = queries.shape
    row_shards, col_shards, members, depth, cols = gathered.shape
    keys = rows_split.shape[1]
    rank = up_full.shape[1]
    kv_width = col_shards * cols
    heads = kv_width // HEAD_DIM
    step_cols = width // col_shards
    row_block = pl.BlockSpec((rows, step_cols), lambda i: (0, i))
    whole = lambda shape: pl.BlockSpec(shape, lambda i: (0,) * len(shape))
    return pl.pallas_call(
        attention_kernel,
        grid=(col_shards,),
        in_specs=[
            whole(mask.shape),
            row_block,
            row_block,
            whole(rows_split.shape),
            pl.BlockSpec((row_shards, 1, members, depth, cols), lambda i: (0, i, 0, 0, 0)),
            whole(low_rows.shape),
            pl.BlockSpec((members, rank, cols), lambda i: (0, 0, i)),
        ],
        out_specs=[
            row_block,
            row_block,
            whole((members, keys, rank)),
            pl.BlockSpec((members, rank, cols), lambda i: (0, 0, i)),
        ],
        out_shape=[
            jax.ShapeDtypeStruct((rows, width), jnp.bfloat16),
            jax.ShapeDtypeStruct((rows, width), jnp.bfloat16),
            jax.ShapeDtypeStruct((members, keys, rank), jnp.bfloat16),
            jax.ShapeDtypeStruct((members, rank, kv_width), jnp.float32),
        ],
        scratch_shapes=[pltpu.VMEM((members, keys, rank), jnp.float32)],
    )(mask, queries, grads, rows_split, gathered, low_rows, up_full)


def attend(query_rows, rows_split, gathered, grad_rows, is_first, low_rows, up_full):
    length = query_rows.shape[0]
    group_size = HEADS // KV_HEADS
    query_pos = lax.broadcasted_iota(jnp.int32, (group_size * length, 2 * length), 0) % length
    key_pos = lax.broadcasted_iota(jnp.int32, (group_size * length, 2 * length), 1)
    visible = (
        (key_pos > query_pos)
        & (key_pos <= query_pos + length)
        & (jnp.logical_not(is_first) | (key_pos >= length))
    )
    return attention_heads(
        visible.astype(jnp.int32), query_rows, grad_rows, rows_split, gathered, low_rows, up_full
    )


def project_rows(rows_previous, rows_own, kv_weight, down_full, up_full):
    def low_of(rows):
        return jnp.einsum(
            "rd,mkd->mrk", rows, down_full, preferred_element_type=jnp.float32
        ).astype(jnp.bfloat16)

    low_previous, low_rank = low_of(rows_previous), low_of(rows_own)
    row_shards, col_shards = lax.axis_size("ctx"), lax.axis_size(("dp", "sub"))
    rows_both = jnp.concatenate([rows_previous, rows_own], axis=0)
    rows_split = rows_both.reshape(rows_both.shape[0], row_shards, -1).swapaxes(0, 1)
    gathered = lax.all_gather(kv_weight, ("ctx", "dp", "sub"), axis=0, tiled=False)
    gathered = gathered.reshape((row_shards, col_shards) + kv_weight.shape)
    low_rows = jnp.concatenate([low_previous, low_rank], axis=1)
    return rows_both, rows_split, gathered, low_rows


def gather_adapters(adapter_down, adapter_up):
    axes = ("ctx", "dp", "sub")
    down_cols = adapter_down.shape[2]
    joined = jnp.concatenate([adapter_down, adapter_up], axis=2)
    gathered = lax.all_gather(joined, axes, axis=0, tiled=False)
    shards = gathered.shape[0]

    def unshard(piece):
        return piece.transpose(1, 2, 0, 3).reshape(2, piece.shape[2], shards * piece.shape[3])

    return unshard(gathered[..., :down_cols]), unshard(gathered[..., down_cols:])


def exchange_scatter(blocks, axis):
    size = lax.axis_size(axis)
    me = lax.axis_index(axis)
    total = lax.dynamic_index_in_dim(blocks, me, axis=0, keepdims=False)
    for shift in range(1, size):
        send = lax.dynamic_index_in_dim(blocks, (me + shift) % size, axis=0, keepdims=False)
        total = total + lax.ppermute(send, axis, [(i, (i + shift) % size) for i in range(size)])
    return total


def halving_scatter(blocks, axis):
    size = lax.axis_size(axis)
    if size <= 4:
        return exchange_scatter(blocks, axis)
    if size & (size - 1):
        return lax.psum_scatter(blocks, axis, scatter_dimension=0, tiled=True)[0]
    me = lax.axis_index(axis)
    stride = size // 2
    while stride >= 1:
        halves = blocks.reshape((2, blocks.shape[0] // 2) + blocks.shape[1:])
        bit = (me // stride) % 2
        keep = lax.dynamic_index_in_dim(halves, bit, axis=0, keepdims=False)
        send = lax.dynamic_index_in_dim(halves, 1 - bit, axis=0, keepdims=False)
        pairs = [(i, i ^ stride) for i in range(size)]
        blocks = keep + lax.ppermute(send, axis, pairs)
        stride //= 2
    return blocks[0]


def scatter_adapter_grads(joined_down, joined_up):
    members_rank = joined_down.shape[-1]
    down_cols = joined_down.shape[2]
    joined = jnp.concatenate([joined_down, joined_up], axis=2)
    mine = halving_scatter(joined, ("dp", "sub"))
    mine = halving_scatter(mine, "ctx")

    def unshard(piece):
        return piece.reshape(piece.shape[0], 2, -1).transpose(1, 2, 0)

    return unshard(mine[:down_cols]), unshard(mine[down_cols:])


def on_device(hidden, queries, kv_weight, adapter_down, adapter_up, out_grad):
    rows_own = hidden[0]
    query_rows = queries[0]
    grad_rows = out_grad[0]
    length = rows_own.shape[0]
    row_shards, col_shards = lax.axis_size("ctx"), lax.axis_size(("dp", "sub"))
    down_full, up_full = gather_adapters(adapter_down, adapter_up)
    rows_own, down_full = lax.optimization_barrier((rows_own, down_full))
    rows_previous = shifted(rows_own, "ctx", 1)
    is_first = lax.axis_index("ctx") == 0
    rows_both, rows_split, gathered, low_rows = project_rows(
        rows_previous, rows_own, kv_weight, down_full, up_full
    )
    attended, query_grad, projected, up_terms = attend(
        query_rows, rows_split, gathered, grad_rows, is_first, low_rows, up_full
    )
    up_terms = up_terms.reshape(up_terms.shape[:2] + (row_shards, col_shards, -1)).transpose(3, 2, 4, 0, 1)
    down_terms = jnp.einsum(
        "mrk,rcij->icjmk",
        projected,
        rows_both.reshape(rows_both.shape[0], row_shards, col_shards, -1),
        preferred_element_type=jnp.float32,
    )
    factor = adapter_scale / (lax.axis_size("dp") * lax.axis_size("sub"))
    flat = lambda terms: (terms * factor).reshape(terms.shape[:3] + (-1,))
    down_part, up_part = scatter_adapter_grads(flat(down_terms), flat(up_terms))
    return (attended[None], query_grad[None], down_part, up_part)


def solution(mesh):
    placed = (
        P(("groups", "dp", "sub"), "ctx", None),
        P(("groups", "dp", "sub"), "ctx", None),
        P(None, "ctx", ("dp", "sub")),
        P(None, None, ("ctx", "dp", "sub")),
        P(None, None, ("ctx", "dp", "sub")),
        P(("groups", "dp", "sub"), "ctx", None),
    )
    return jax.shard_map(
        on_device,
        mesh=mesh,
        in_specs=placed,
        out_specs=(
            P(("groups", "dp", "sub"), "ctx", None),
            P(("groups", "dp", "sub"), "ctx", None),
            P("groups", None, ("ctx", "dp", "sub")),
            P("groups", None, ("ctx", "dp", "sub")),
        ),
        check_vma=False,
    )
```

```python
import functools

import jax
import jax.numpy as jnp
from jax import lax
from jax.experimental import pallas as pl
from jax.experimental.pallas import tpu as pltpu
from jax.sharding import PartitionSpec as P

HEADS = 16
KV_HEADS = 8
HEAD_DIM = 128


query_scale = 1.0 / 12.0
logit_cap = 50.0
adapter_scale = 0.5


def shifted(value, axis, by):
    length = lax.axis_size(axis)
    pairs = [(i, i + by) for i in range(length) if 0 <= i + by < length]
    return lax.ppermute(value, axis, pairs)


def attention_kernel(
    factor, mask_ref, q_ref, do_ref, rows_ref, weight_ref, low_ref, up_ref,
    out_ref, dq_ref, down_terms_ref, up_terms_ref, projected_acc,
):
    step = pl.program_id(0)
    half = HEAD_DIM
    row_shards = weight_ref.shape[0]
    heads_here = weight_ref.shape[4] // HEAD_DIM
    rows = q_ref.shape[0]
    visible = mask_ref[...] != 0
    contract_last = (((1,), (1,)), ((), ()))
    contract_first = (((0,), (0,)), ((), ()))

    def project(member):
        base = jnp.dot(low_ref[member], up_ref[member], preferred_element_type=jnp.float32)
        base = base * adapter_scale
        for c in range(row_shards):
            base = base + jnp.dot(
                rows_ref[c], weight_ref[c, 0, member], preferred_element_type=jnp.float32
            )
        return base.astype(jnp.bfloat16)

    keys_here = project(0)
    values_here = project(1)

    @pl.when(step == 0)
    def _():
        projected_acc[...] = jnp.zeros_like(projected_acc)

    for h in range(heads_here):
        cols = slice(h * HEAD_DIM, (h + 1) * HEAD_DIM)
        qa = slice(2 * h * half, (2 * h + 1) * half)
        qb = slice((2 * h + 1) * half, (2 * h + 2) * half)
        q = jnp.concatenate([q_ref[:, qa], q_ref[:, qb]], axis=0)
        do = jnp.concatenate([do_ref[:, qa], do_ref[:, qb]], axis=0)
        k = keys_here[:, cols]
        v = values_here[:, cols]
        raw_score = lax.dot_general(q, k, contract_last, preferred_element_type=jnp.float32) * query_scale
        bent_score = jnp.tanh(raw_score / logit_cap)
        expo_terms = jnp.where(visible, jnp.exp(logit_cap * bent_score), 0.0)
        denominator = jnp.sum(expo_terms, axis=-1, keepdims=True)
        prob_wide = (expo_terms * (1.0 / denominator)).astype(jnp.bfloat16).astype(jnp.float32)
        attn_prob = prob_wide.astype(jnp.bfloat16)
        head_out = jnp.dot(attn_prob, v, preferred_element_type=jnp.float32).astype(out_ref.dtype)
        out_ref[:, qa] = head_out[:rows]
        out_ref[:, qb] = head_out[rows:]
        prob_grad = lax.dot_general(do, v, contract_last, preferred_element_type=jnp.float32)
        row_delta = jnp.sum(prob_wide * prob_grad, axis=-1, keepdims=True)
        score_wide = prob_wide * (prob_grad - row_delta) * (1.0 - bent_score * bent_score) * query_scale
        score_grad = score_wide.astype(jnp.bfloat16)
        head_qgrad = jnp.dot(score_grad, k, preferred_element_type=jnp.float32).astype(dq_ref.dtype)
        dq_ref[:, qa] = head_qgrad[:rows]
        dq_ref[:, qb] = head_qgrad[rows:]
        key_grad = lax.dot_general(
            score_grad, q, contract_first, preferred_element_type=jnp.float32
        ).astype(jnp.bfloat16)
        value_grad = lax.dot_general(
            attn_prob, do, contract_first, preferred_element_type=jnp.float32
        ).astype(jnp.bfloat16)
        for member, grad in enumerate((key_grad, value_grad)):
            projected_acc[member] += lax.dot_general(
                grad, up_ref[member, :, cols], contract_last, preferred_element_type=jnp.float32
            )
            up_terms_ref[member, :, cols] = lax.dot_general(
                low_ref[member], grad, contract_first, preferred_element_type=jnp.float32
            ) * factor

    @pl.when(step == pl.num_programs(0) - 1)
    def _():
        for member in range(projected_acc.shape[0]):
            projected = projected_acc[member].astype(jnp.bfloat16)
            for c in range(row_shards):
                down_terms_ref[member, c] = lax.dot_general(
                    projected, rows_ref[c], contract_first, preferred_element_type=jnp.float32
                ) * factor


def attention_heads(mask, queries, grads, rows_split, gathered, low_rows, up_full, factor):
    rows, width = queries.shape
    row_shards, col_shards, members, depth, cols = gathered.shape
    keys = rows_split.shape[1]
    rank = up_full.shape[1]
    kv_width = col_shards * cols
    heads = kv_width // HEAD_DIM
    step_cols = width // col_shards
    row_block = pl.BlockSpec((rows, step_cols), lambda i: (0, i))
    whole = lambda shape: pl.BlockSpec(shape, lambda i: (0,) * len(shape))
    return pl.pallas_call(
        functools.partial(attention_kernel, factor),
        grid=(col_shards,),
        in_specs=[
            whole(mask.shape),
            row_block,
            row_block,
            whole(rows_split.shape),
            pl.BlockSpec((row_shards, 1, members, depth, cols), lambda i: (0, i, 0, 0, 0)),
            whole(low_rows.shape),
            pl.BlockSpec((members, rank, cols), lambda i: (0, 0, i)),
        ],
        out_specs=[
            row_block,
            row_block,
            whole((members, row_shards, rank, depth)),
            pl.BlockSpec((members, rank, cols), lambda i: (0, 0, i)),
        ],
        out_shape=[
            jax.ShapeDtypeStruct((rows, width), jnp.bfloat16),
            jax.ShapeDtypeStruct((rows, width), jnp.bfloat16),
            jax.ShapeDtypeStruct((members, row_shards, rank, depth), jnp.float32),
            jax.ShapeDtypeStruct((members, rank, kv_width), jnp.float32),
        ],
        scratch_shapes=[pltpu.VMEM((members, keys, rank), jnp.float32)],
    )(mask, queries, grads, rows_split, gathered, low_rows, up_full)


def attend(query_rows, rows_split, gathered, grad_rows, is_first, low_rows, up_full, factor):
    length = query_rows.shape[0]
    group_size = HEADS // KV_HEADS
    query_pos = lax.broadcasted_iota(jnp.int32, (group_size * length, 2 * length), 0) % length
    key_pos = lax.broadcasted_iota(jnp.int32, (group_size * length, 2 * length), 1)
    visible = (
        (key_pos > query_pos)
        & (key_pos <= query_pos + length)
        & (jnp.logical_not(is_first) | (key_pos >= length))
    )
    return attention_heads(
        visible.astype(jnp.int32), query_rows, grad_rows, rows_split, gathered, low_rows, up_full,
        factor,
    )


def project_rows(rows_previous, rows_own, kv_weight, down_full, up_full):
    def low_of(rows):
        return jnp.einsum(
            "rd,mkd->mrk", rows, down_full, preferred_element_type=jnp.float32
        ).astype(jnp.bfloat16)

    low_previous, low_rank = low_of(rows_previous), low_of(rows_own)
    row_shards, col_shards = lax.axis_size("ctx"), lax.axis_size(("dp", "sub"))
    rows_both = jnp.concatenate([rows_previous, rows_own], axis=0)
    rows_split = rows_both.reshape(rows_both.shape[0], row_shards, -1).swapaxes(0, 1)
    gathered = lax.all_gather(kv_weight, ("ctx", "dp", "sub"), axis=0, tiled=False)
    gathered = gathered.reshape((row_shards, col_shards) + kv_weight.shape)
    low_rows = jnp.concatenate([low_previous, low_rank], axis=1)
    return rows_both, rows_split, gathered, low_rows


def gather_adapters(adapter_down, adapter_up):
    axes = ("ctx", "dp", "sub")
    down_cols = adapter_down.shape[2]
    joined = jnp.concatenate([adapter_down, adapter_up], axis=2)
    gathered = lax.all_gather(joined, axes, axis=0, tiled=False)
    shards = gathered.shape[0]

    def unshard(piece):
        return piece.transpose(1, 2, 0, 3).reshape(2, piece.shape[2], shards * piece.shape[3])

    return unshard(gathered[..., :down_cols]), unshard(gathered[..., down_cols:])


def exchange_scatter(blocks, axis):
    size = lax.axis_size(axis)
    me = lax.axis_index(axis)
    total = lax.dynamic_index_in_dim(blocks, me, axis=0, keepdims=False)
    for shift in range(1, size):
        send = lax.dynamic_index_in_dim(blocks, (me + shift) % size, axis=0, keepdims=False)
        total = total + lax.ppermute(send, axis, [(i, (i + shift) % size) for i in range(size)])
    return total


def halving_scatter(blocks, axis):
    size = lax.axis_size(axis)
    if size <= 4:
        return exchange_scatter(blocks, axis)
    if size & (size - 1):
        return lax.psum_scatter(blocks, axis, scatter_dimension=0, tiled=True)[0]
    me = lax.axis_index(axis)
    stride = size // 2
    while stride >= 1:
        halves = blocks.reshape((2, blocks.shape[0] // 2) + blocks.shape[1:])
        bit = (me // stride) % 2
        keep = lax.dynamic_index_in_dim(halves, bit, axis=0, keepdims=False)
        send = lax.dynamic_index_in_dim(halves, 1 - bit, axis=0, keepdims=False)
        pairs = [(i, i ^ stride) for i in range(size)]
        blocks = keep + lax.ppermute(send, axis, pairs)
        stride //= 2
    return blocks[0]


def scatter_adapter_grads(joined_down, joined_up):
    members_rank = joined_down.shape[-1]
    down_cols = joined_down.shape[2]
    joined = jnp.concatenate([joined_down, joined_up], axis=2)
    mine = halving_scatter(joined, ("dp", "sub"))
    mine = halving_scatter(mine, "ctx")

    def unshard(piece):
        return piece.reshape(piece.shape[0], 2, -1).transpose(1, 2, 0)

    return unshard(mine[:down_cols]), unshard(mine[down_cols:])


def on_device(hidden, queries, kv_weight, adapter_down, adapter_up, out_grad):
    rows_own = hidden[0]
    query_rows = queries[0]
    grad_rows = out_grad[0]
    length = rows_own.shape[0]
    row_shards, col_shards = lax.axis_size("ctx"), lax.axis_size(("dp", "sub"))
    down_full, up_full = gather_adapters(adapter_down, adapter_up)
    rows_own, down_full = lax.optimization_barrier((rows_own, down_full))
    rows_previous = shifted(rows_own, "ctx", 1)
    is_first = lax.axis_index("ctx") == 0
    rows_both, rows_split, gathered, low_rows = project_rows(
        rows_previous, rows_own, kv_weight, down_full, up_full
    )
    factor = adapter_scale / (lax.axis_size("dp") * lax.axis_size("sub"))
    attended, query_grad, down_terms, up_terms = attend(
        query_rows, rows_split, gathered, grad_rows, is_first, low_rows, up_full, factor
    )
    members, rank = up_terms.shape[0], up_terms.shape[1]
    up_terms = up_terms.reshape((members, rank, row_shards, col_shards, -1)).transpose(3, 2, 4, 0, 1)
    down_terms = down_terms.reshape((members, row_shards, rank, col_shards, -1)).transpose(3, 1, 4, 0, 2)
    flat = lambda terms: terms.reshape(terms.shape[:3] + (-1,))
    down_part, up_part = scatter_adapter_grads(flat(down_terms), flat(up_terms))
    return (attended[None], query_grad[None], down_part, up_part)


def solution(mesh):
    placed = (
        P(("groups", "dp", "sub"), "ctx", None),
        P(("groups", "dp", "sub"), "ctx", None),
        P(None, "ctx", ("dp", "sub")),
        P(None, None, ("ctx", "dp", "sub")),
        P(None, None, ("ctx", "dp", "sub")),
        P(("groups", "dp", "sub"), "ctx", None),
    )
    return jax.shard_map(
        on_device,
        mesh=mesh,
        in_specs=placed,
        out_specs=(
            P(("groups", "dp", "sub"), "ctx", None),
            P(("groups", "dp", "sub"), "ctx", None),
            P("groups", None, ("ctx", "dp", "sub")),
            P("groups", None, ("ctx", "dp", "sub")),
        ),
        check_vma=False,
    )
```

```python
import functools

import jax
import jax.numpy as jnp
from jax import lax
from jax.experimental import pallas as pl
from jax.experimental.pallas import tpu as pltpu
from jax.sharding import PartitionSpec as P

HEADS = 16
KV_HEADS = 8
HEAD_DIM = 128


query_scale = 1.0 / 12.0
logit_cap = 50.0
adapter_scale = 0.5


def shifted(value, axis, by):
    length = lax.axis_size(axis)
    pairs = [(i, i + by) for i in range(length) if 0 <= i + by < length]
    return lax.ppermute(value, axis, pairs)


def attention_kernel(
    factor, mask_ref, q_ref, do_ref, rows_ref, weight_ref, low_ref, up_ref,
    out_ref, dq_ref, down_terms_ref, up_terms_ref, projected_acc,
):
    step = pl.program_id(0)
    half = HEAD_DIM
    row_shards = weight_ref.shape[0]
    heads_here = weight_ref.shape[4] // HEAD_DIM
    rows = q_ref.shape[0]
    visible = mask_ref[...] != 0
    contract_last = (((1,), (1,)), ((), ()))
    contract_first = (((0,), (0,)), ((), ()))

    def project(member):
        base = jnp.dot(low_ref[member], up_ref[member], preferred_element_type=jnp.float32)
        base = base * adapter_scale
        for c in range(row_shards):
            base = base + jnp.dot(
                rows_ref[c], weight_ref[c, 0, member], preferred_element_type=jnp.float32
            )
        return base.astype(jnp.bfloat16)

    keys_here = project(0)
    values_here = project(1)

    @pl.when(step == 0)
    def _():
        projected_acc[...] = jnp.zeros_like(projected_acc)

    for h in range(heads_here):
        cols = slice(h * HEAD_DIM, (h + 1) * HEAD_DIM)
        qa = slice(2 * h * half, (2 * h + 1) * half)
        qb = slice((2 * h + 1) * half, (2 * h + 2) * half)
        q = jnp.concatenate([q_ref[:, qa], q_ref[:, qb]], axis=0)
        do = jnp.concatenate([do_ref[:, qa], do_ref[:, qb]], axis=0)
        k = keys_here[:, cols]
        v = values_here[:, cols]
        bent_score = jnp.tanh(
            lax.dot_general(q, k, contract_last, preferred_element_type=jnp.float32)
            * (query_scale / logit_cap)
        )
        expo_terms = jnp.where(visible, jnp.exp(logit_cap * bent_score), 0.0)
        denominator = jnp.sum(expo_terms, axis=-1, keepdims=True)
        prob_wide = (expo_terms * (1.0 / denominator)).astype(jnp.bfloat16).astype(jnp.float32)
        attn_prob = prob_wide.astype(jnp.bfloat16)
        head_out = jnp.dot(attn_prob, v, preferred_element_type=jnp.float32).astype(out_ref.dtype)
        out_ref[:, qa] = head_out[:rows]
        out_ref[:, qb] = head_out[rows:]
        prob_grad = lax.dot_general(do, v, contract_last, preferred_element_type=jnp.float32)
        row_delta = jnp.sum(prob_wide * prob_grad, axis=-1, keepdims=True)
        score_wide = prob_wide * (prob_grad - row_delta) * (1.0 - bent_score * bent_score) * query_scale
        score_grad = score_wide.astype(jnp.bfloat16)
        head_qgrad = jnp.dot(score_grad, k, preferred_element_type=jnp.float32).astype(dq_ref.dtype)
        dq_ref[:, qa] = head_qgrad[:rows]
        dq_ref[:, qb] = head_qgrad[rows:]
        key_grad = lax.dot_general(
            score_grad, q, contract_first, preferred_element_type=jnp.float32
        ).astype(jnp.bfloat16)
        value_grad = lax.dot_general(
            attn_prob, do, contract_first, preferred_element_type=jnp.float32
        ).astype(jnp.bfloat16)
        for member, grad in enumerate((key_grad, value_grad)):
            projected_acc[member] += lax.dot_general(
                grad, up_ref[member, :, cols], contract_last, preferred_element_type=jnp.float32
            )
            up_terms_ref[member, :, cols] = lax.dot_general(
                low_ref[member], grad, contract_first, preferred_element_type=jnp.float32
            ) * factor

    @pl.when(step == pl.num_programs(0) - 1)
    def _():
        for member in range(projected_acc.shape[0]):
            projected = projected_acc[member].astype(jnp.bfloat16)
            for c in range(row_shards):
                down_terms_ref[member, c] = lax.dot_general(
                    projected, rows_ref[c], contract_first, preferred_element_type=jnp.float32
                ) * factor


def attention_heads(mask, queries, grads, rows_split, gathered, low_rows, up_full, factor):
    rows, width = queries.shape
    row_shards, col_shards, members, depth, cols = gathered.shape
    keys = rows_split.shape[1]
    rank = up_full.shape[1]
    kv_width = col_shards * cols
    heads = kv_width // HEAD_DIM
    step_cols = width // col_shards
    row_block = pl.BlockSpec((rows, step_cols), lambda i: (0, i))
    whole = lambda shape: pl.BlockSpec(shape, lambda i: (0,) * len(shape))
    return pl.pallas_call(
        functools.partial(attention_kernel, factor),
        grid=(col_shards,),
        in_specs=[
            whole(mask.shape),
            row_block,
            row_block,
            whole(rows_split.shape),
            pl.BlockSpec((row_shards, 1, members, depth, cols), lambda i: (0, i, 0, 0, 0)),
            whole(low_rows.shape),
            pl.BlockSpec((members, rank, cols), lambda i: (0, 0, i)),
        ],
        out_specs=[
            row_block,
            row_block,
            whole((members, row_shards, rank, depth)),
            pl.BlockSpec((members, rank, cols), lambda i: (0, 0, i)),
        ],
        out_shape=[
            jax.ShapeDtypeStruct((rows, width), jnp.bfloat16),
            jax.ShapeDtypeStruct((rows, width), jnp.bfloat16),
            jax.ShapeDtypeStruct((members, row_shards, rank, depth), jnp.float32),
            jax.ShapeDtypeStruct((members, rank, kv_width), jnp.float32),
        ],
        scratch_shapes=[pltpu.VMEM((members, keys, rank), jnp.float32)],
    )(mask, queries, grads, rows_split, gathered, low_rows, up_full)


def attend(query_rows, rows_split, gathered, grad_rows, is_first, low_rows, up_full, factor):
    length = query_rows.shape[0]
    group_size = HEADS // KV_HEADS
    query_pos = lax.broadcasted_iota(jnp.int32, (group_size * length, 2 * length), 0) % length
    key_pos = lax.broadcasted_iota(jnp.int32, (group_size * length, 2 * length), 1)
    visible = (
        (key_pos > query_pos)
        & (key_pos <= query_pos + length)
        & (jnp.logical_not(is_first) | (key_pos >= length))
    )
    return attention_heads(
        visible.astype(jnp.int32), query_rows, grad_rows, rows_split, gathered, low_rows, up_full,
        factor,
    )


def project_rows(rows_previous, rows_own, kv_weight, down_full, up_full):
    def low_of(rows):
        return jnp.einsum(
            "rd,mkd->mrk", rows, down_full, preferred_element_type=jnp.float32
        ).astype(jnp.bfloat16)

    low_previous, low_rank = low_of(rows_previous), low_of(rows_own)
    row_shards, col_shards = lax.axis_size("ctx"), lax.axis_size(("dp", "sub"))
    rows_both = jnp.concatenate([rows_previous, rows_own], axis=0)
    rows_split = rows_both.reshape(rows_both.shape[0], row_shards, -1).swapaxes(0, 1)
    gathered = lax.all_gather(kv_weight, ("ctx", "dp", "sub"), axis=0, tiled=False)
    gathered = gathered.reshape((row_shards, col_shards) + kv_weight.shape)
    low_rows = jnp.concatenate([low_previous, low_rank], axis=1)
    return rows_both, rows_split, gathered, low_rows


def gather_adapters(adapter_down, adapter_up):
    axes = ("ctx", "dp", "sub")
    down_cols = adapter_down.shape[2]
    joined = jnp.concatenate([adapter_down, adapter_up], axis=2)
    gathered = lax.all_gather(joined, axes, axis=0, tiled=False)
    shards = gathered.shape[0]

    def unshard(piece):
        return piece.transpose(1, 2, 0, 3).reshape(2, piece.shape[2], shards * piece.shape[3])

    return unshard(gathered[..., :down_cols]), unshard(gathered[..., down_cols:])


def exchange_scatter(blocks, axis):
    size = lax.axis_size(axis)
    me = lax.axis_index(axis)
    total = lax.dynamic_index_in_dim(blocks, me, axis=0, keepdims=False)
    for shift in range(1, size):
        send = lax.dynamic_index_in_dim(blocks, (me + shift) % size, axis=0, keepdims=False)
        total = total + lax.ppermute(send, axis, [(i, (i + shift) % size) for i in range(size)])
    return total


def halving_scatter(blocks, axis):
    size = lax.axis_size(axis)
    if size <= 4:
        return exchange_scatter(blocks, axis)
    if size & (size - 1):
        return lax.psum_scatter(blocks, axis, scatter_dimension=0, tiled=True)[0]
    me = lax.axis_index(axis)
    stride = size // 2
    while stride >= 1:
        halves = blocks.reshape((2, blocks.shape[0] // 2) + blocks.shape[1:])
        bit = (me // stride) % 2
        keep = lax.dynamic_index_in_dim(halves, bit, axis=0, keepdims=False)
        send = lax.dynamic_index_in_dim(halves, 1 - bit, axis=0, keepdims=False)
        pairs = [(i, i ^ stride) for i in range(size)]
        blocks = keep + lax.ppermute(send, axis, pairs)
        stride //= 2
    return blocks[0]


def scatter_adapter_grads(joined_down, joined_up):
    members_rank = joined_down.shape[-1]
    down_cols = joined_down.shape[2]
    joined = jnp.concatenate([joined_down, joined_up], axis=2)
    mine = halving_scatter(joined, ("dp", "sub"))
    mine = halving_scatter(mine, "ctx")

    def unshard(piece):
        return piece.reshape(piece.shape[0], 2, -1).transpose(1, 2, 0)

    return unshard(mine[:down_cols]), unshard(mine[down_cols:])


def on_device(hidden, queries, kv_weight, adapter_down, adapter_up, out_grad):
    rows_own = hidden[0]
    query_rows = queries[0]
    grad_rows = out_grad[0]
    length = rows_own.shape[0]
    row_shards, col_shards = lax.axis_size("ctx"), lax.axis_size(("dp", "sub"))
    down_full, up_full = gather_adapters(adapter_down, adapter_up)
    rows_own, down_full = lax.optimization_barrier((rows_own, down_full))
    rows_previous = shifted(rows_own, "ctx", 1)
    is_first = lax.axis_index("ctx") == 0
    rows_both, rows_split, gathered, low_rows = project_rows(
        rows_previous, rows_own, kv_weight, down_full, up_full
    )
    factor = adapter_scale / (lax.axis_size("dp") * lax.axis_size("sub"))
    attended, query_grad, down_terms, up_terms = attend(
        query_rows, rows_split, gathered, grad_rows, is_first, low_rows, up_full, factor
    )
    members, rank = up_terms.shape[0], up_terms.shape[1]
    up_terms = up_terms.reshape((members, rank, row_shards, col_shards, -1)).transpose(3, 2, 4, 0, 1)
    down_terms = down_terms.reshape((members, row_shards, rank, col_shards, -1)).transpose(3, 1, 4, 0, 2)
    flat = lambda terms: terms.reshape(terms.shape[:3] + (-1,))
    down_part, up_part = scatter_adapter_grads(flat(down_terms), flat(up_terms))
    return (attended[None], query_grad[None], down_part, up_part)


def solution(mesh):
    placed = (
        P(("groups", "dp", "sub"), "ctx", None),
        P(("groups", "dp", "sub"), "ctx", None),
        P(None, "ctx", ("dp", "sub")),
        P(None, None, ("ctx", "dp", "sub")),
        P(None, None, ("ctx", "dp", "sub")),
        P(("groups", "dp", "sub"), "ctx", None),
    )
    return jax.shard_map(
        on_device,
        mesh=mesh,
        in_specs=placed,
        out_specs=(
            P(("groups", "dp", "sub"), "ctx", None),
            P(("groups", "dp", "sub"), "ctx", None),
            P("groups", None, ("ctx", "dp", "sub")),
            P("groups", None, ("ctx", "dp", "sub")),
        ),
        check_vma=False,
    )
```

```python
import functools

import jax
import jax.numpy as jnp
from jax import lax
from jax.experimental import pallas as pl
from jax.experimental.pallas import tpu as pltpu
from jax.sharding import PartitionSpec as P

HEADS = 16
KV_HEADS = 8
HEAD_DIM = 128


query_scale = 1.0 / 12.0
logit_cap = 50.0
adapter_scale = 0.5


def shifted(value, axis, by):
    length = lax.axis_size(axis)
    pairs = [(i, i + by) for i in range(length) if 0 <= i + by < length]
    return lax.ppermute(value, axis, pairs)


def attention_kernel(
    factor, mask_ref, q_ref, do_ref, rows_ref, weight_ref, low_ref, up_ref,
    out_ref, dq_ref, down_terms_ref, up_terms_ref, projected_acc,
):
    step = pl.program_id(0)
    half = HEAD_DIM
    row_shards = weight_ref.shape[0]
    heads_here = weight_ref.shape[4] // HEAD_DIM
    rows = q_ref.shape[0]
    keys = rows_ref.shape[1]
    query_pos = lax.broadcasted_iota(jnp.int32, (2 * rows, keys), 0)
    query_pos = jnp.where(query_pos >= rows, query_pos - rows, query_pos)
    key_pos = lax.broadcasted_iota(jnp.int32, (2 * rows, keys), 1)
    visible = (
        (key_pos > query_pos)
        & (key_pos <= query_pos + rows)
        & ((mask_ref[0] == 0) | (key_pos >= rows))
    )
    contract_last = (((1,), (1,)), ((), ()))
    contract_first = (((0,), (0,)), ((), ()))

    def project(member):
        base = jnp.dot(low_ref[member], up_ref[member], preferred_element_type=jnp.float32)
        base = base * adapter_scale
        for c in range(row_shards):
            base = base + jnp.dot(
                rows_ref[c], weight_ref[c, 0, member], preferred_element_type=jnp.float32
            )
        return base.astype(jnp.bfloat16)

    keys_here = project(0)
    values_here = project(1)

    @pl.when(step == 0)
    def _():
        projected_acc[...] = jnp.zeros_like(projected_acc)

    for h in range(heads_here):
        cols = slice(h * HEAD_DIM, (h + 1) * HEAD_DIM)
        qa = slice(2 * h * half, (2 * h + 1) * half)
        qb = slice((2 * h + 1) * half, (2 * h + 2) * half)
        q = jnp.concatenate([q_ref[:, qa], q_ref[:, qb]], axis=0)
        do = jnp.concatenate([do_ref[:, qa], do_ref[:, qb]], axis=0)
        k = keys_here[:, cols]
        v = values_here[:, cols]
        raw_score = lax.dot_general(q, k, contract_last, preferred_element_type=jnp.float32) * query_scale
        bent_score = jnp.tanh(raw_score / logit_cap)
        expo_terms = jnp.where(visible, jnp.exp(logit_cap * bent_score), 0.0)
        denominator = jnp.sum(expo_terms, axis=-1, keepdims=True)
        prob_wide = (expo_terms * (1.0 / denominator)).astype(jnp.bfloat16).astype(jnp.float32)
        attn_prob = prob_wide.astype(jnp.bfloat16)
        head_out = jnp.dot(attn_prob, v, preferred_element_type=jnp.float32).astype(out_ref.dtype)
        out_ref[:, qa] = head_out[:rows]
        out_ref[:, qb] = head_out[rows:]
        prob_grad = lax.dot_general(do, v, contract_last, preferred_element_type=jnp.float32)
        row_delta = jnp.sum(prob_wide * prob_grad, axis=-1, keepdims=True)
        score_wide = prob_wide * (prob_grad - row_delta) * (1.0 - bent_score * bent_score) * query_scale
        score_grad = score_wide.astype(jnp.bfloat16)
        head_qgrad = jnp.dot(score_grad, k, preferred_element_type=jnp.float32).astype(dq_ref.dtype)
        dq_ref[:, qa] = head_qgrad[:rows]
        dq_ref[:, qb] = head_qgrad[rows:]
        key_grad = lax.dot_general(
            score_grad, q, contract_first, preferred_element_type=jnp.float32
        ).astype(jnp.bfloat16)
        value_grad = lax.dot_general(
            attn_prob, do, contract_first, preferred_element_type=jnp.float32
        ).astype(jnp.bfloat16)
        for member, grad in enumerate((key_grad, value_grad)):
            projected_acc[member] += lax.dot_general(
                grad, up_ref[member, :, cols], contract_last, preferred_element_type=jnp.float32
            )
            up_terms_ref[member, :, cols] = lax.dot_general(
                low_ref[member], grad, contract_first, preferred_element_type=jnp.float32
            ) * factor

    @pl.when(step == pl.num_programs(0) - 1)
    def _():
        for member in range(projected_acc.shape[0]):
            projected = projected_acc[member].astype(jnp.bfloat16)
            for c in range(row_shards):
                down_terms_ref[member, c] = lax.dot_general(
                    projected, rows_ref[c], contract_first, preferred_element_type=jnp.float32
                ) * factor


def attention_heads(mask, queries, grads, rows_split, gathered, low_rows, up_full, factor):
    rows, width = queries.shape
    row_shards, col_shards, members, depth, cols = gathered.shape
    keys = rows_split.shape[1]
    rank = up_full.shape[1]
    kv_width = col_shards * cols
    heads = kv_width // HEAD_DIM
    step_cols = width // col_shards
    row_block = pl.BlockSpec((rows, step_cols), lambda i: (0, i))
    whole = lambda shape: pl.BlockSpec(shape, lambda i: (0,) * len(shape))
    return pl.pallas_call(
        functools.partial(attention_kernel, factor),
        grid=(col_shards,),
        in_specs=[
            pl.BlockSpec(memory_space=pltpu.SMEM),
            row_block,
            row_block,
            whole(rows_split.shape),
            pl.BlockSpec((row_shards, 1, members, depth, cols), lambda i: (0, i, 0, 0, 0)),
            whole(low_rows.shape),
            pl.BlockSpec((members, rank, cols), lambda i: (0, 0, i)),
        ],
        out_specs=[
            row_block,
            row_block,
            whole((members, row_shards, rank, depth)),
            pl.BlockSpec((members, rank, cols), lambda i: (0, 0, i)),
        ],
        out_shape=[
            jax.ShapeDtypeStruct((rows, width), jnp.bfloat16),
            jax.ShapeDtypeStruct((rows, width), jnp.bfloat16),
            jax.ShapeDtypeStruct((members, row_shards, rank, depth), jnp.float32),
            jax.ShapeDtypeStruct((members, rank, kv_width), jnp.float32),
        ],
        scratch_shapes=[pltpu.VMEM((members, keys, rank), jnp.float32)],
    )(mask, queries, grads, rows_split, gathered, low_rows, up_full)


def attend(query_rows, rows_split, gathered, grad_rows, is_first, low_rows, up_full, factor):
    length = query_rows.shape[0]
    group_size = HEADS // KV_HEADS
    first_flag = is_first.astype(jnp.int32).reshape(1)
    return attention_heads(
        first_flag, query_rows, grad_rows, rows_split, gathered, low_rows, up_full,
        factor,
    )


def project_rows(rows_previous, rows_own, kv_weight, down_full, up_full):
    def low_of(rows):
        return jnp.einsum(
            "rd,mkd->mrk", rows, down_full, preferred_element_type=jnp.float32
        ).astype(jnp.bfloat16)

    low_previous, low_rank = low_of(rows_previous), low_of(rows_own)
    row_shards, col_shards = lax.axis_size("ctx"), lax.axis_size(("dp", "sub"))
    rows_both = jnp.concatenate([rows_previous, rows_own], axis=0)
    rows_split = rows_both.reshape(rows_both.shape[0], row_shards, -1).swapaxes(0, 1)
    gathered = lax.all_gather(kv_weight, ("ctx", "dp", "sub"), axis=0, tiled=False)
    gathered = gathered.reshape((row_shards, col_shards) + kv_weight.shape)
    low_rows = jnp.concatenate([low_previous, low_rank], axis=1)
    return rows_both, rows_split, gathered, low_rows


def gather_adapters(adapter_down, adapter_up):
    axes = ("ctx", "dp", "sub")
    down_cols = adapter_down.shape[2]
    joined = jnp.concatenate([adapter_down, adapter_up], axis=2)
    gathered = lax.all_gather(joined, axes, axis=0, tiled=False)
    shards = gathered.shape[0]

    def unshard(piece):
        return piece.transpose(1, 2, 0, 3).reshape(2, piece.shape[2], shards * piece.shape[3])

    return unshard(gathered[..., :down_cols]), unshard(gathered[..., down_cols:])


def exchange_scatter(blocks, axis):
    size = lax.axis_size(axis)
    me = lax.axis_index(axis)
    total = lax.dynamic_index_in_dim(blocks, me, axis=0, keepdims=False)
    for shift in range(1, size):
        send = lax.dynamic_index_in_dim(blocks, (me + shift) % size, axis=0, keepdims=False)
        total = total + lax.ppermute(send, axis, [(i, (i + shift) % size) for i in range(size)])
    return total


def halving_scatter(blocks, axis):
    size = lax.axis_size(axis)
    if size <= 4:
        return exchange_scatter(blocks, axis)
    if size & (size - 1):
        return lax.psum_scatter(blocks, axis, scatter_dimension=0, tiled=True)[0]
    me = lax.axis_index(axis)
    stride = size // 2
    while stride >= 1:
        halves = blocks.reshape((2, blocks.shape[0] // 2) + blocks.shape[1:])
        bit = (me // stride) % 2
        keep = lax.dynamic_index_in_dim(halves, bit, axis=0, keepdims=False)
        send = lax.dynamic_index_in_dim(halves, 1 - bit, axis=0, keepdims=False)
        pairs = [(i, i ^ stride) for i in range(size)]
        blocks = keep + lax.ppermute(send, axis, pairs)
        stride //= 2
    return blocks[0]


def scatter_adapter_grads(joined_down, joined_up):
    members_rank = joined_down.shape[-1]
    down_cols = joined_down.shape[2]
    joined = jnp.concatenate([joined_down, joined_up], axis=2)
    mine = halving_scatter(joined, ("dp", "sub"))
    mine = halving_scatter(mine, "ctx")

    def unshard(piece):
        return piece.reshape(piece.shape[0], 2, -1).transpose(1, 2, 0)

    return unshard(mine[:down_cols]), unshard(mine[down_cols:])


def on_device(hidden, queries, kv_weight, adapter_down, adapter_up, out_grad):
    rows_own = hidden[0]
    query_rows = queries[0]
    grad_rows = out_grad[0]
    length = rows_own.shape[0]
    row_shards, col_shards = lax.axis_size("ctx"), lax.axis_size(("dp", "sub"))
    down_full, up_full = gather_adapters(adapter_down, adapter_up)
    rows_own, down_full = lax.optimization_barrier((rows_own, down_full))
    rows_previous = shifted(rows_own, "ctx", 1)
    is_first = lax.axis_index("ctx") == 0
    rows_both, rows_split, gathered, low_rows = project_rows(
        rows_previous, rows_own, kv_weight, down_full, up_full
    )
    factor = adapter_scale / (lax.axis_size("dp") * lax.axis_size("sub"))
    attended, query_grad, down_terms, up_terms = attend(
        query_rows, rows_split, gathered, grad_rows, is_first, low_rows, up_full, factor
    )
    members, rank = up_terms.shape[0], up_terms.shape[1]
    up_terms = up_terms.reshape((members, rank, row_shards, col_shards, -1)).transpose(3, 2, 4, 0, 1)
    down_terms = down_terms.reshape((members, row_shards, rank, col_shards, -1)).transpose(3, 1, 4, 0, 2)
    flat = lambda terms: terms.reshape(terms.shape[:3] + (-1,))
    down_part, up_part = scatter_adapter_grads(flat(down_terms), flat(up_terms))
    return (attended[None], query_grad[None], down_part, up_part)


def solution(mesh):
    placed = (
        P(("groups", "dp", "sub"), "ctx", None),
        P(("groups", "dp", "sub"), "ctx", None),
        P(None, "ctx", ("dp", "sub")),
        P(None, None, ("ctx", "dp", "sub")),
        P(None, None, ("ctx", "dp", "sub")),
        P(("groups", "dp", "sub"), "ctx", None),
    )
    return jax.shard_map(
        on_device,
        mesh=mesh,
        in_specs=placed,
        out_specs=(
            P(("groups", "dp", "sub"), "ctx", None),
            P(("groups", "dp", "sub"), "ctx", None),
            P("groups", None, ("ctx", "dp", "sub")),
            P("groups", None, ("ctx", "dp", "sub")),
        ),
        check_vma=False,
    )
```

```python
import functools

import jax
import jax.numpy as jnp
from jax import lax
from jax.experimental import pallas as pl
from jax.experimental.pallas import tpu as pltpu
from jax.sharding import PartitionSpec as P

HEADS = 16
KV_HEADS = 8
HEAD_DIM = 128


query_scale = 1.0 / 12.0
logit_cap = 50.0
adapter_scale = 0.5


def shifted(value, axis, by):
    length = lax.axis_size(axis)
    pairs = [(i, i + by) for i in range(length) if 0 <= i + by < length]
    return lax.ppermute(value, axis, pairs)


def attention_kernel(
    factor, mask_ref, q_ref, do_ref, rows_ref, weight_ref, low_ref, up_ref,
    out_ref, dq_ref, down_terms_ref, up_terms_ref, projected_acc,
):
    step = pl.program_id(0)
    half = HEAD_DIM
    row_shards = weight_ref.shape[0]
    heads_here = weight_ref.shape[4] // HEAD_DIM
    rows = q_ref.shape[0]
    keys = rows_ref.shape[1]
    query_pos = lax.broadcasted_iota(jnp.int32, (2 * rows, keys), 0)
    query_pos = jnp.where(query_pos >= rows, query_pos - rows, query_pos)
    key_pos = lax.broadcasted_iota(jnp.int32, (2 * rows, keys), 1)
    visible = (
        (key_pos > query_pos)
        & (key_pos <= query_pos + rows)
        & ((mask_ref[0] == 0) | (key_pos >= rows))
    )
    contract_last = (((1,), (1,)), ((), ()))
    contract_first = (((0,), (0,)), ((), ()))

    def project(member):
        base = jnp.dot(low_ref[member], up_ref[member], preferred_element_type=jnp.float32)
        base = base * adapter_scale
        for c in range(row_shards):
            base = base + jnp.dot(
                rows_ref[c], weight_ref[c, 0, member], preferred_element_type=jnp.float32
            )
        return base.astype(jnp.bfloat16)

    keys_here = project(0)
    values_here = project(1)

    @pl.when(step == 0)
    def _():
        projected_acc[...] = jnp.zeros_like(projected_acc)

    for h in range(heads_here):
        cols = slice(h * HEAD_DIM, (h + 1) * HEAD_DIM)
        qa = slice(2 * h * half, (2 * h + 1) * half)
        qb = slice((2 * h + 1) * half, (2 * h + 2) * half)
        q = jnp.concatenate([q_ref[:, qa], q_ref[:, qb]], axis=0)
        do = jnp.concatenate([do_ref[:, qa], do_ref[:, qb]], axis=0)
        k = keys_here[:, cols]
        v = values_here[:, cols]
        raw_score = lax.dot_general(q, k, contract_last, preferred_element_type=jnp.float32) * query_scale
        bent_score = jnp.tanh(raw_score / logit_cap)
        expo_terms = jnp.where(visible, jnp.exp(logit_cap * bent_score), 0.0)
        denominator = jnp.sum(expo_terms, axis=-1, keepdims=True)
        prob_wide = (expo_terms * (1.0 / denominator)).astype(jnp.bfloat16).astype(jnp.float32)
        attn_prob = prob_wide.astype(jnp.bfloat16)
        head_out = jnp.dot(attn_prob, v, preferred_element_type=jnp.float32).astype(out_ref.dtype)
        out_ref[:, qa] = head_out[:rows]
        out_ref[:, qb] = head_out[rows:]
        prob_grad = lax.dot_general(do, v, contract_last, preferred_element_type=jnp.float32)
        row_delta = jnp.sum(prob_wide * prob_grad, axis=-1, keepdims=True)
        score_wide = prob_wide * (prob_grad - row_delta) * (1.0 - bent_score * bent_score) * query_scale
        score_grad = score_wide.astype(jnp.bfloat16)
        head_qgrad = jnp.dot(score_grad, k, preferred_element_type=jnp.float32).astype(dq_ref.dtype)
        dq_ref[:, qa] = head_qgrad[:rows]
        dq_ref[:, qb] = head_qgrad[rows:]
        key_grad = lax.dot_general(
            score_grad, q, contract_first, preferred_element_type=jnp.float32
        ).astype(jnp.bfloat16)
        value_grad = lax.dot_general(
            attn_prob, do, contract_first, preferred_element_type=jnp.float32
        ).astype(jnp.bfloat16)
        for member, grad in enumerate((key_grad, value_grad)):
            projected_acc[member] += lax.dot_general(
                grad, up_ref[member, :, cols], contract_last, preferred_element_type=jnp.float32
            )
            up_terms_ref[member, :, cols] = lax.dot_general(
                low_ref[member], grad, contract_first, preferred_element_type=jnp.float32
            ) * factor

    @pl.when(step == pl.num_programs(0) - 1)
    def _():
        for member in range(projected_acc.shape[0]):
            projected = projected_acc[member].astype(jnp.bfloat16)
            for c in range(row_shards):
                down_terms_ref[member, c] = lax.dot_general(
                    projected, rows_ref[c], contract_first, preferred_element_type=jnp.float32
                ) * factor


def attention_heads(mask, queries, grads, rows_split, gathered, low_rows, up_full, factor):
    rows, width = queries.shape
    row_shards, col_shards, members, depth, cols = gathered.shape
    keys = rows_split.shape[1]
    rank = up_full.shape[1]
    kv_width = col_shards * cols
    heads = kv_width // HEAD_DIM
    step_cols = width // col_shards
    row_block = pl.BlockSpec((rows, step_cols), lambda i: (0, i))
    whole = lambda shape: pl.BlockSpec(shape, lambda i: (0,) * len(shape))
    return pl.pallas_call(
        functools.partial(attention_kernel, factor),
        grid=(col_shards,),
        in_specs=[
            pl.BlockSpec(memory_space=pltpu.SMEM),
            row_block,
            row_block,
            whole(rows_split.shape),
            pl.BlockSpec((row_shards, 1, members, depth, cols), lambda i: (0, i, 0, 0, 0)),
            whole(low_rows.shape),
            pl.BlockSpec((members, rank, cols), lambda i: (0, 0, i)),
        ],
        out_specs=[
            row_block,
            row_block,
            whole((members, row_shards, rank, depth)),
            pl.BlockSpec((members, rank, cols), lambda i: (0, 0, i)),
        ],
        out_shape=[
            jax.ShapeDtypeStruct((rows, width), jnp.bfloat16),
            jax.ShapeDtypeStruct((rows, width), jnp.bfloat16),
            jax.ShapeDtypeStruct((members, row_shards, rank, depth), jnp.float32),
            jax.ShapeDtypeStruct((members, rank, kv_width), jnp.float32),
        ],
        scratch_shapes=[pltpu.VMEM((members, keys, rank), jnp.float32)],
    )(mask, queries, grads, rows_split, gathered, low_rows, up_full)


def attend(query_rows, rows_split, gathered, grad_rows, is_first, low_rows, up_full, factor):
    length = query_rows.shape[0]
    group_size = HEADS // KV_HEADS
    first_flag = is_first.astype(jnp.int32).reshape(1)
    return attention_heads(
        first_flag, query_rows, grad_rows, rows_split, gathered, low_rows, up_full,
        factor,
    )


def project_rows(rows_previous, rows_own, kv_weight, down_full, up_full):
    def low_of(rows):
        return jnp.einsum(
            "rd,mkd->mrk", rows, down_full, preferred_element_type=jnp.float32
        ).astype(jnp.bfloat16)

    low_previous, low_rank = low_of(rows_previous), low_of(rows_own)
    row_shards, col_shards = lax.axis_size("ctx"), lax.axis_size(("dp", "sub"))
    rows_both = jnp.concatenate([rows_previous, rows_own], axis=0)
    rows_split = rows_both.reshape(rows_both.shape[0], row_shards, -1).swapaxes(0, 1)
    gathered = lax.all_gather(kv_weight, ("ctx", "dp", "sub"), axis=0, tiled=False)
    gathered = gathered.reshape((row_shards, col_shards) + kv_weight.shape)
    low_rows = jnp.concatenate([low_previous, low_rank], axis=1)
    return rows_both, rows_split, gathered, low_rows


def gather_adapters(adapter_down, adapter_up):
    axes = ("ctx", "dp", "sub")
    down_cols = adapter_down.shape[2]
    joined = jnp.concatenate([adapter_down, adapter_up], axis=2)
    gathered = lax.all_gather(joined, axes, axis=0, tiled=False)
    shards = gathered.shape[0]

    def unshard(piece):
        return piece.transpose(1, 2, 0, 3).reshape(2, piece.shape[2], shards * piece.shape[3])

    return unshard(gathered[..., :down_cols]), unshard(gathered[..., down_cols:])


def exchange_scatter(blocks, axis):
    size = lax.axis_size(axis)
    me = lax.axis_index(axis)
    rolled = lax.dynamic_slice_in_dim(jnp.concatenate([blocks, blocks], axis=0), me, size, axis=0)
    total = rolled[0]
    for shift in range(1, size):
        total = total + lax.ppermute(
            rolled[shift], axis, [(i, (i + shift) % size) for i in range(size)]
        )
    return total


def halving_scatter(blocks, axis):
    size = lax.axis_size(axis)
    if size <= 4:
        return exchange_scatter(blocks, axis)
    if size & (size - 1):
        return lax.psum_scatter(blocks, axis, scatter_dimension=0, tiled=True)[0]
    me = lax.axis_index(axis)
    stride = size // 2
    while stride >= 1:
        halves = blocks.reshape((2, blocks.shape[0] // 2) + blocks.shape[1:])
        bit = (me // stride) % 2
        keep = lax.dynamic_index_in_dim(halves, bit, axis=0, keepdims=False)
        send = lax.dynamic_index_in_dim(halves, 1 - bit, axis=0, keepdims=False)
        pairs = [(i, i ^ stride) for i in range(size)]
        blocks = keep + lax.ppermute(send, axis, pairs)
        stride //= 2
    return blocks[0]


def scatter_adapter_grads(joined_down, joined_up):
    members_rank = joined_down.shape[-1]
    down_cols = joined_down.shape[2]
    joined = jnp.concatenate([joined_down, joined_up], axis=2)
    mine = halving_scatter(joined, ("dp", "sub"))
    mine = halving_scatter(mine, "ctx")

    def unshard(piece):
        return piece.reshape(piece.shape[0], 2, -1).transpose(1, 2, 0)

    return unshard(mine[:down_cols]), unshard(mine[down_cols:])


def on_device(hidden, queries, kv_weight, adapter_down, adapter_up, out_grad):
    rows_own = hidden[0]
    query_rows = queries[0]
    grad_rows = out_grad[0]
    length = rows_own.shape[0]
    row_shards, col_shards = lax.axis_size("ctx"), lax.axis_size(("dp", "sub"))
    down_full, up_full = gather_adapters(adapter_down, adapter_up)
    rows_own, down_full = lax.optimization_barrier((rows_own, down_full))
    rows_previous = shifted(rows_own, "ctx", 1)
    is_first = lax.axis_index("ctx") == 0
    rows_both, rows_split, gathered, low_rows = project_rows(
        rows_previous, rows_own, kv_weight, down_full, up_full
    )
    factor = adapter_scale / (lax.axis_size("dp") * lax.axis_size("sub"))
    attended, query_grad, down_terms, up_terms = attend(
        query_rows, rows_split, gathered, grad_rows, is_first, low_rows, up_full, factor
    )
    members, rank = up_terms.shape[0], up_terms.shape[1]
    up_terms = up_terms.reshape((members, rank, row_shards, col_shards, -1)).transpose(3, 2, 4, 0, 1)
    down_terms = down_terms.reshape((members, row_shards, rank, col_shards, -1)).transpose(3, 1, 4, 0, 2)
    flat = lambda terms: terms.reshape(terms.shape[:3] + (-1,))
    down_part, up_part = scatter_adapter_grads(flat(down_terms), flat(up_terms))
    return (attended[None], query_grad[None], down_part, up_part)


def solution(mesh):
    placed = (
        P(("groups", "dp", "sub"), "ctx", None),
        P(("groups", "dp", "sub"), "ctx", None),
        P(None, "ctx", ("dp", "sub")),
        P(None, None, ("ctx", "dp", "sub")),
        P(None, None, ("ctx", "dp", "sub")),
        P(("groups", "dp", "sub"), "ctx", None),
    )
    return jax.shard_map(
        on_device,
        mesh=mesh,
        in_specs=placed,
        out_specs=(
            P(("groups", "dp", "sub"), "ctx", None),
            P(("groups", "dp", "sub"), "ctx", None),
            P("groups", None, ("ctx", "dp", "sub")),
            P("groups", None, ("ctx", "dp", "sub")),
        ),
        check_vma=False,
    )
```
